32 devices in a mesh: tok: 8 (over z, x), hv: 4 (over y, core).
Axes of the slice: x: 2, y: 2, z: 4, core: 2. Of those that a mesh axis runs over, the one named last changes fastest.
Arguments:
- tokens: bfloat16 [2048, 2048], P(('tok', 'hv')), may hold values from -6 to 6
- prompt_lengths: int32 [5], replicated, may hold values from 1 to 1365, 2048 in all
- query_weight: bfloat16 [2048, 1024], P(None, 'hv'), may hold values from -0.125 to 0.125
- key_weight: bfloat16 [2048, 1024], P(None, 'hv'), may hold values from -0.125 to 0.125
- value_weight: bfloat16 [2048, 2048], P(None, 'hv'), may hold values from -0.125 to 0.125
- query_conv: bfloat16 [4, 1024], P(None, 'hv'), may hold values from -3 to 3
- key_conv: bfloat16 [4, 1024], P(None, 'hv'), may hold values from -3 to 3
- value_conv: bfloat16 [4, 2048], P(None, 'hv'), may hold values from -3 to 3
- decay_down: bfloat16 [2048, 16], replicated, may hold values from -0.125 to 0.125
- decay_up: bfloat16 [16, 1024], P(None, 'hv'), may hold values from -3 to 3
- decay_bias: float32 [1024], P('hv')
- gate_weight: bfloat16 [2048, 2048], P(None, 'hv'), may hold values from -0.125 to 0.125
- norm_gain: float32 [512], replicated, may hold values from 0.1 to 1.9
- out_weight: bfloat16 [2048, 2048], P('hv'), may hold values from -0.125 to 0.125
Outputs:
- mixed: bfloat16 [2048, 2048], P(('tok', 'hv'))
- segment_states: float32 [8, 4, 256, 512], P('tok', 'hv')
- conv_edges: bfloat16 [8, 3, 4, 1024], P('tok', None, 'hv')
The draws below stay inside these ranges and needn't reach their ends.
Inputs may be any that keep to these rules, and one draw needn't show every extreme that they name: `prompt_lengths`: the rows of 5 prompts that fill all 2048 packed rows; exactly one prompt has 1365 rows.
All inputs are finite; a program needn't handle non-finite values.
Results may differ from the reference program's by a relative error of at most 0.022.
Values may be sent and summed in bfloat16 or wider, within the bound.
No kernel may reach another device: no remote copies, remote signals or barrier semaphores. Data moves between devices by JAX's collectives and lax.ppermute only.
A program may use at most 128 MiB of HBM per device.

```python
import math
import jax
import jax.numpy as jnp
import numpy as np
from jax import lax

D = 2048
H = 4
DK = 256
DV = 512
RANK = 16
CONV = 4
SPAN = 64
TOK_DEV = 256
TOKENS = 2048
PROMPTS = 5
LONG = 1365
HK = 1024
HV = 2048
N_TOK = 8


def draw_decay_bias(key, part):
    choose_key, slow_key, fast_key = jax.random.split(key, 3)
    share = 0.5
    slow_mask = jax.random.uniform(choose_key, (HK,)) < share
    slow_bias = math.log(LONG / 2.0) + jax.random.uniform(slow_key, (HK,), minval=0.0, maxval=1.5)
    fast_bias = jax.random.uniform(fast_key, (HK,), minval=-0.5, maxval=1.0)
    return jnp.where(slow_mask, slow_bias, fast_bias).astype(jnp.float32)


def levels(rng, dims, cuts, least, largest):
    level, own = 1.0, jax.random.fold_in(rng, 6)
    for dim, blocks in cuts:
        heights = jnp.exp(jax.random.uniform(jax.random.fold_in(own, dim), (blocks,), jnp.float32, least / len(cuts), largest / len(cuts)))
        level = level * jnp.repeat(heights, dims[dim] // blocks).reshape([-1 if axis == dim else 1 for axis in range(len(dims))])
    return level


def split_up(count, total, most, lean):
    weights = [(1 << 20) // math.isqrt(standing ** lean) + 1 for standing in range(2, count + 1)]
    spare, counts = total - most - (count - 1), [1] * (count - 1)
    while spare > 0:
        movable = [i for i in range(count - 1) if counts[i] < most]
        pool, left = sum([weights[i] for i in movable]), spare
        for i in movable:
            more = min(most - counts[i], max(1, left * weights[i] // pool), spare)
            counts[i] = counts[i] + more
            spare = spare - more
    return np.array([most] + counts)


def uneven_parts(rng, number_of, total, limit, skew):
    if number_of == 2:
        one = jax.random.randint(rng, (), max(1, total - limit), min(limit, total - 1) + 1)
        return jnp.stack([one, total - one])
    tallies = jnp.asarray(split_up(number_of, total, limit, skew), jnp.int32)
    couples = (number_of - 1) // 2
    donor, sink = tallies[1:1 + 2 * couples:2], tallies[2:2 + 2 * couples:2]
    margin = jnp.minimum(donor - 1, limit - sink)
    moved = jax.random.randint(jax.random.fold_in(rng, 1), (couples,), 0, 1 << 20) % (margin + 1)
    tallies = tallies.at[1:1 + 2 * couples:2].set(donor - moved).at[2:2 + 2 * couples:2].set(sink + moved)
    return tallies[jax.random.permutation(jax.random.fold_in(rng, 2), number_of)]


def gaussian(rng, shape, spread, most, shards=(), kind=jnp.bfloat16):
    loudness = levels(rng, shape, shards, -0.22, 0.18) if shards else 1.0
    result = jax.random.normal(rng, shape, jnp.float32) * spread * loudness
    return jnp.minimum(jnp.maximum(result, -most), most).astype(kind)


def setup_inputs(seed: int = 0) -> dict:
    arg_keys = jax.random.split(jax.random.key(seed), 15)
    return {
        "tokens": gaussian(arg_keys[0], (TOKENS, D), 1.0, 6.0, ((0, 32),)),
        "prompt_lengths": uneven_parts(arg_keys[1], PROMPTS, TOKENS, LONG, 2).astype(jnp.int32),
        "query_weight": gaussian(arg_keys[2], (D, HK), D ** -0.5, 0.125, ((1, 4),)),
        "key_weight": gaussian(arg_keys[3], (D, HK), D ** -0.5, 0.125, ((1, 4),)),
        "value_weight": gaussian(arg_keys[4], (D, HV), D ** -0.5, 0.125, ((1, 4),)),
        "query_conv": gaussian(arg_keys[5], (CONV, HK), CONV ** -0.5, 3.0, ((1, 4),)),
        "key_conv": gaussian(arg_keys[6], (CONV, HK), CONV ** -0.5, 3.0, ((1, 4),)),
        "value_conv": gaussian(arg_keys[7], (CONV, HV), CONV ** -0.5, 3.0, ((1, 4),)),
        "decay_down": gaussian(arg_keys[8], (D, RANK), D ** -0.5, 0.125),
        "decay_up": gaussian(arg_keys[9], (RANK, HK), (RANK // 4) ** -0.5, 3.0, ((1, 4),)),
        "decay_bias": draw_decay_bias(jax.random.fold_in(arg_keys[14], 71), 0),
        "gate_weight": gaussian(arg_keys[11], (D, HV), D ** -0.5, 0.125, ((1, 4),)),
        "norm_gain": jnp.clip(1.0 + 0.18 * jax.random.normal(arg_keys[12], (DV,), jnp.float32), 0.1, 1.9),
        "out_weight": gaussian(arg_keys[13], (HV, D), HV ** -0.5, 0.125, ((0, 4),)),
    }


HIGHEST_PRECISION = lax.Precision.HIGHEST

def prompt_marks(positions, offsets):
    before = offsets[None, :] <= positions[:, None]
    prompt_first = lax.optimization_barrier(jnp.max(jnp.where(before, offsets[None, :], 0), axis=1)).astype(jnp.int32)
    return (prompt_first, (prompt_first == positions).astype(jnp.float32))

def short_conv(raw_rows, before_rows, weight, positions, prompt_first):
    tap_count = weight.shape[0]
    extended = jnp.concatenate([before_rows, raw_rows], axis=0)
    summed = jnp.zeros(raw_rows.shape, jnp.float32)
    for tap_index in range(tap_count):
        lag_rows = tap_count - 1 - tap_index
        inside_prompt = (positions - lag_rows >= prompt_first).astype(jnp.float32)
        window = lax.slice_in_dim(extended, tap_index, tap_index + raw_rows.shape[0], axis=0)
        summed = summed + weight[tap_index].astype(jnp.float32)[None, :] * window.astype(jnp.float32) * inside_prompt[:, None]
    return jax.nn.silu(summed).astype(jnp.bfloat16)

def span_parts(head_keys, head_values, decays, starts):
    cumulative = jnp.cumsum(decays, axis=0)
    groups = jnp.cumsum(starts)
    intact = (groups == 0.0).astype(jnp.float32)
    final_log = cumulative[-1]
    in_tail = (groups == groups[-1]).astype(jnp.float32)
    weighted = (head_keys.astype(jnp.float32) * jnp.exp(final_log[None, :] - cumulative) * in_tail[:, None]).astype(jnp.bfloat16)
    update = lax.dot_general(weighted, head_values, (((0,), (0,)), ((), ())), preferred_element_type=jnp.float32)
    step_decay = jnp.exp(final_log) * intact[-1]
    return (cumulative, groups, intact, update, step_decay)

def span_step(carried, pieces):
    memory, product = carried
    queries, head_keys, head_values, decays, starts = pieces
    cumulative, groups, intact, update, step_decay = span_parts(head_keys, head_values, decays, starts)
    index_rows = jnp.arange(queries.shape[0])
    allowed = (groups[:, None] == groups[None, :]) & (index_rows[:, None] >= index_rows[None, :])
    lifted = queries.astype(jnp.float32) * jnp.exp(cumulative)
    lowered = (head_keys.astype(jnp.float32) * jnp.exp(-cumulative)).astype(jnp.bfloat16)
    raw_scores = lax.dot_general(lifted.astype(jnp.bfloat16), lowered, (((1,), (1,)), ((), ())), preferred_element_type=jnp.float32)
    scores = jnp.where(allowed, raw_scores, 0.0).astype(jnp.bfloat16)
    inside = jnp.dot(scores, head_values, preferred_element_type=jnp.float32)
    outside = jnp.dot(lifted * intact[:, None], memory, precision=HIGHEST_PRECISION)
    reaches = product[None, :] * jnp.exp(cumulative) * intact[:, None]
    return ((step_decay[:, None] * memory + update, product * step_decay), (inside + outside, reaches))

def sweep(queries, head_keys, head_values, decays, starts, memory):
    block_count = queries.shape[0] // SPAN

    def blocked(array_in):
        return array_in.reshape((block_count, SPAN) + array_in.shape[1:])
    initial = (memory, jnp.ones((decays.shape[1],), jnp.float32))
    (closing, product), (outputs, reaches) = lax.scan(span_step, initial, (blocked(queries), blocked(head_keys), blocked(head_values), blocked(decays), blocked(starts)))
    row_count = queries.shape[0]
    return (outputs.reshape((row_count, head_values.shape[1])), reaches.reshape((row_count, decays.shape[1])), closing, product)

def run_head(queries, head_keys, head_values, decays, starts):

    def cut(array_in):
        return array_in.reshape((N_TOK, TOK_DEV) + array_in.shape[1:])

    def block_step(memory, pieces):
        outputs, _, closing, _ = sweep(pieces[0], pieces[1], pieces[2], pieces[3], pieces[4], memory)
        return (closing, (outputs, closing))
    initial = jnp.zeros((DK, DV), jnp.float32)
    _, (outputs, closings) = lax.scan(block_step, initial, (cut(queries), cut(head_keys), cut(head_values), cut(decays), cut(starts)))
    return (outputs.reshape((TOKENS, DV)), closings)

def reference(tokens, prompt_lengths, query_weight, key_weight, value_weight, query_conv, key_conv, value_conv, decay_down, decay_up, decay_bias, gate_weight, norm_gain, out_weight):
    positions = jnp.arange(TOKENS, dtype=jnp.int32)
    offsets = (jnp.cumsum(prompt_lengths) - prompt_lengths).astype(jnp.int32)
    prompt_first, starts = prompt_marks(positions, offsets)

    def project(weight):
        return jnp.dot(tokens, weight, preferred_element_type=jnp.float32).astype(jnp.bfloat16)
    raw_query = project(query_weight)
    raw_key = project(key_weight)
    raw_value = project(value_weight)
    gate_values = project(gate_weight)
    low_rank = project(decay_down)
    decays = jax.nn.log_sigmoid(jnp.dot(low_rank, decay_up, preferred_element_type=jnp.float32) + decay_bias) / 16.0
    rim_rows = CONV - 1

    def convolve(raw_rows, weight):
        before_rows = jnp.zeros((rim_rows, raw_rows.shape[1]), jnp.bfloat16)
        return short_conv(raw_rows, before_rows, weight, positions, prompt_first)
    conv_query = convolve(raw_query, query_conv)
    conv_key = convolve(raw_key, key_conv)
    conv_value = convolve(raw_value, value_conv)
    summed = jnp.zeros((TOKENS, D), jnp.float32)
    closings = []
    for head_index in range(H):
        k_lo = head_index * DK
        v_lo = head_index * DV
        heads_out, closing = run_head(conv_query[:, k_lo:k_lo + DK], conv_key[:, k_lo:k_lo + DK], conv_value[:, v_lo:v_lo + DV], decays[:, k_lo:k_lo + DK], starts)
        gate_float = gate_values[:, v_lo:v_lo + DV].astype(jnp.float32)
        rescale = lax.rsqrt(lax.optimization_barrier(jnp.mean(heads_out * heads_out, axis=1, keepdims=True)) + 1e-05)
        gated_out = (heads_out * rescale * norm_gain[None, :] * gate_float * jax.nn.sigmoid(gate_float)).astype(jnp.bfloat16)
        partial_value = jnp.dot(gated_out, out_weight[v_lo:v_lo + DV, :], preferred_element_type=jnp.float32).astype(jnp.bfloat16)
        partial_value = lax.optimization_barrier(partial_value)
        summed = summed + partial_value.astype(jnp.float32)
        closings.append(closing)
    mixed = summed.astype(jnp.bfloat16)
    segment_states = jnp.stack(closings, axis=1)
    joined = jnp.concatenate([raw_query.reshape(TOKENS, H, DK), raw_key.reshape(TOKENS, H, DK), raw_value.reshape(TOKENS, H, DV)], axis=2)
    joined = joined.reshape(N_TOK, TOK_DEV, H, 2 * DK + DV)[:, TOK_DEV - rim_rows:]
    spots = positions.reshape(N_TOK, TOK_DEV)[:, TOK_DEV - rim_rows:]
    anchor = prompt_first.reshape(N_TOK, TOK_DEV)[:, TOK_DEV - 1]
    in_prompt = spots >= anchor[:, None]
    conv_edges = jnp.where(in_prompt[:, :, None, None], joined, jnp.zeros_like(joined))
    return (mixed, segment_states, conv_edges)
```

```python
import jax
import jax.numpy as jnp
from jax import lax
from jax.sharding import PartitionSpec as P

SPAN = 64


HIGHEST_PRECISION = lax.Precision.HIGHEST


def shifted(value, axis, steps):
    count = lax.axis_size(axis)
    initial, last = (max(0, -steps), min(count, count - steps))
    return lax.ppermute(value, axis, [(source, source + steps) for source in range(initial, last)])


def prompt_marks(positions, offsets):
    before = offsets[None, :] <= positions[:, None]
    prompt_first = jnp.max(jnp.where(before, offsets[None, :], 0), axis=1)
    return (prompt_first, (prompt_first == positions).astype(jnp.float32))


def short_conv(raw_rows, before_rows, weight, positions, prompt_first):
    tap_count = weight.shape[0]
    extended = jnp.concatenate([before_rows, raw_rows], axis=0)
    summed = jnp.zeros(raw_rows.shape, jnp.float32)
    for tap_index in range(tap_count):
        lag_rows = tap_count - 1 - tap_index
        inside_prompt = (positions - lag_rows >= prompt_first).astype(jnp.float32)
        window = lax.slice_in_dim(extended, tap_index, tap_index + raw_rows.shape[0], axis=0)
        summed = (
            summed
            + weight[tap_index].astype(jnp.float32)[None, :]
            * window.astype(jnp.float32)
            * inside_prompt[:, None]
        )
    return jax.nn.silu(summed).astype(jnp.bfloat16)


def blocked(array_in):
    return array_in.reshape((array_in.shape[0] // SPAN, SPAN) + array_in.shape[1:])


def segment_parts(queries, head_keys, head_values, decays, starts):
    cumulative = jnp.cumsum(decays, axis=1)
    groups = jnp.cumsum(starts, axis=1)
    intact = (groups == 0.0).astype(jnp.float32)
    final_log = cumulative[:, -1]
    in_tail = (groups == groups[:, -1:]).astype(jnp.float32)
    weighted = (
        head_keys.astype(jnp.float32)
        * jnp.exp(final_log[:, None, :] - cumulative)
        * in_tail[:, :, None]
    ).astype(jnp.bfloat16)
    update = jnp.einsum("bsk,bsv->bkv", weighted, head_values, preferred_element_type=jnp.float32)
    step_decay = jnp.exp(final_log) * intact[:, -1:]
    index_rows = jnp.arange(queries.shape[1])
    allowed = (groups[:, :, None] == groups[:, None, :]) & (
        index_rows[None, :, None] >= index_rows[None, None, :]
    )
    lifted = queries.astype(jnp.float32) * jnp.exp(cumulative)
    lowered = (head_keys.astype(jnp.float32) * jnp.exp(-cumulative)).astype(jnp.bfloat16)
    raw_scores = jnp.einsum(
        "bak,bck->bac", lifted.astype(jnp.bfloat16), lowered, preferred_element_type=jnp.float32
    )
    scores = jnp.where(allowed, raw_scores, 0.0).astype(jnp.bfloat16)
    inside = jnp.einsum("bac,bcv->bav", scores, head_values, preferred_element_type=jnp.float32)
    lifted_intact = lifted * intact[:, :, None]
    block_count = queries.shape[0]
    memory = jnp.zeros(update.shape[1:], jnp.float32)
    product = jnp.ones(step_decay.shape[1:], jnp.float32)
    local_outs = [jnp.zeros(inside.shape[1:], jnp.float32)]
    products = [product]
    for block in range(block_count):
        if block > 0:
            local_outs.append(jnp.dot(lifted_intact[block], memory, precision=HIGHEST_PRECISION))
            products.append(product)
        memory = step_decay[block][:, None] * memory + update[block]
        product = product * step_decay[block]
    local_out = inside + jnp.stack(local_outs)
    carry_lift = lifted_intact * jnp.stack(products)[:, None, :]
    return (local_out, carry_lift, memory, product)


def prefix_states(decay, memory, axis):
    count = lax.axis_size(axis)
    place = lax.axis_index(axis)
    steps = 1
    while steps < count:
        earlier_decay, earlier_memory = shifted((decay, memory), axis, steps)
        valid = place >= steps
        memory = jnp.where(valid, decay[:, None] * earlier_memory + memory, memory)
        decay = jnp.where(valid, earlier_decay * decay, decay)
        steps *= 2
    entering = shifted(memory, axis, 1)
    return (memory, entering)


def shards(
    tokens,
    prompt_lengths,
    query_weight,
    key_weight,
    value_weight,
    query_conv,
    key_conv,
    value_conv,
    decay_down,
    decay_up,
    decay_bias,
    gate_weight,
    norm_gain,
    out_weight,
):
    gathered = lax.all_gather(tokens, "hv", axis=0, tiled=True)

    def project(weight):
        return jnp.dot(gathered, weight, preferred_element_type=jnp.float32).astype(jnp.bfloat16)

    raw_query = project(query_weight)
    raw_key = project(key_weight)
    raw_value = project(value_weight)
    gate_values = project(gate_weight)
    low_rank = project(decay_down)
    row_count = raw_query.shape[0]
    key_width = raw_query.shape[1]
    value_width = raw_value.shape[1]
    positions = lax.axis_index("tok") * row_count + jnp.arange(row_count, dtype=jnp.int32)
    offsets = jnp.cumsum(prompt_lengths) - prompt_lengths
    prompt_first, starts = prompt_marks(positions, offsets)
    rim_rows = query_conv.shape[0] - 1
    joined = jnp.concatenate([raw_query, raw_key, raw_value], axis=1)
    before_rows = shifted(joined[row_count - rim_rows :], "tok", 1)
    conv_query = short_conv(
        raw_query, before_rows[:, :key_width], query_conv, positions, prompt_first
    )
    conv_key = short_conv(
        raw_key, before_rows[:, key_width : 2 * key_width], key_conv, positions, prompt_first
    )
    conv_value = short_conv(
        raw_value, before_rows[:, 2 * key_width :], value_conv, positions, prompt_first
    )
    decays = (
        jax.nn.log_sigmoid(
            jnp.dot(low_rank, decay_up, preferred_element_type=jnp.float32) + decay_bias
        )
        / 16.0
    )
    local_out, carry_lift, local_memory, local_decay = segment_parts(
        blocked(conv_query), blocked(conv_key), blocked(conv_value), blocked(decays), blocked(starts)
    )
    closing, entering = prefix_states(local_decay, local_memory, "tok")
    heads_out = local_out.reshape((row_count, value_width)) + jnp.dot(
        carry_lift.reshape((row_count, key_width)), entering, precision=HIGHEST_PRECISION
    )
    gate_float = gate_values.astype(jnp.float32)
    rescale = lax.rsqrt(jnp.mean(heads_out * heads_out, axis=1, keepdims=True) + 1e-05)
    gated_out = (
        heads_out * rescale * norm_gain[None, :] * gate_float * jax.nn.sigmoid(gate_float)
    ).astype(jnp.bfloat16)
    mixed = lax.psum_scatter(
        jnp.dot(gated_out, out_weight, preferred_element_type=jnp.float32).astype(jnp.bfloat16),
        "hv",
        scatter_dimension=0,
        tiled=True,
    )
    segment_states = closing[None, None]
    in_prompt = positions[row_count - rim_rows :] >= prompt_first[row_count - 1]
    tail_rows = joined[row_count - rim_rows :]
    conv_edges = jnp.where(in_prompt[:, None], tail_rows, jnp.zeros_like(tail_rows))
    conv_edges = conv_edges.reshape((1, rim_rows, 1, joined.shape[1]))
    return (mixed, segment_states, conv_edges)


def solution(mesh):
    in_specs = (
        P(("tok", "hv"), None),
        P(),
        P(None, "hv"),
        P(None, "hv"),
        P(None, "hv"),
        P(None, "hv"),
        P(None, "hv"),
        P(None, "hv"),
        P(),
        P(None, "hv"),
        P("hv"),
        P(None, "hv"),
        P(),
        P("hv", None),
    )
    out_specs = (P(("tok", "hv"), None), P("tok", "hv", None, None), P("tok", None, "hv", None))
    return jax.shard_map(shards, mesh=mesh, in_specs=in_specs, out_specs=out_specs, check_vma=False)
```

```python
import jax
import jax.numpy as jnp
from jax import lax
from jax.sharding import PartitionSpec as P

SPAN = 64


HIGHEST_PRECISION = lax.Precision.HIGHEST


def shifted(value, axis, steps):
    count = lax.axis_size(axis)
    initial, last = (max(0, -steps), min(count, count - steps))
    return lax.ppermute(value, axis, [(source, source + steps) for source in range(initial, last)])


def prompt_marks(positions, offsets):
    before = offsets[None, :] <= positions[:, None]
    prompt_first = jnp.max(jnp.where(before, offsets[None, :], 0), axis=1)
    return (prompt_first, (prompt_first == positions).astype(jnp.float32))


def short_conv(raw_rows, before_rows, weight, positions, prompt_first):
    tap_count = weight.shape[0]
    extended = jnp.concatenate([before_rows, raw_rows], axis=0)
    summed = jnp.zeros(raw_rows.shape, jnp.float32)
    for tap_index in range(tap_count):
        lag_rows = tap_count - 1 - tap_index
        inside_prompt = (positions - lag_rows >= prompt_first).astype(jnp.float32)
        window = lax.slice_in_dim(extended, tap_index, tap_index + raw_rows.shape[0], axis=0)
        summed = (
            summed
            + weight[tap_index].astype(jnp.float32)[None, :]
            * window.astype(jnp.float32)
            * inside_prompt[:, None]
        )
    return jax.nn.silu(summed).astype(jnp.bfloat16)


def blocked(array_in):
    return array_in.reshape((array_in.shape[0] // SPAN, SPAN) + array_in.shape[1:])


def segment_parts(queries, head_keys, head_values, decays, starts):
    cumulative = jnp.cumsum(decays, axis=1)
    groups = jnp.cumsum(starts, axis=1)
    intact = (groups == 0.0).astype(jnp.float32)
    final_log = cumulative[:, -1]
    in_tail = (groups == groups[:, -1:]).astype(jnp.float32)
    weighted = (
        head_keys.astype(jnp.float32)
        * jnp.exp(final_log[:, None, :] - cumulative)
        * in_tail[:, :, None]
    ).astype(jnp.bfloat16)
    update = jnp.einsum("bsk,bsv->bkv", weighted, head_values, preferred_element_type=jnp.float32)
    step_decay = jnp.exp(final_log) * intact[:, -1:]
    index_rows = jnp.arange(queries.shape[1])
    allowed = (groups[:, :, None] == groups[:, None, :]) & (
        index_rows[None, :, None] >= index_rows[None, None, :]
    )
    lifted = queries.astype(jnp.float32) * jnp.exp(cumulative)
    lowered = (head_keys.astype(jnp.float32) * jnp.exp(-cumulative)).astype(jnp.bfloat16)
    raw_scores = jnp.einsum(
        "bak,bck->bac", lifted.astype(jnp.bfloat16), lowered, preferred_element_type=jnp.float32
    )
    scores = jnp.where(allowed, raw_scores, 0.0).astype(jnp.bfloat16)
    inside = jnp.einsum("bac,bcv->bav", scores, head_values, preferred_element_type=jnp.float32)
    lifted_intact = lifted * intact[:, :, None]
    block_count = queries.shape[0]
    memory = jnp.zeros(update.shape[1:], jnp.float32)
    product = jnp.ones(step_decay.shape[1:], jnp.float32)
    local_outs = [jnp.zeros(inside.shape[1:], jnp.float32)]
    products = [product]
    for block in range(block_count):
        if block > 0:
            local_outs.append(jnp.dot(lifted_intact[block], memory, precision=HIGHEST_PRECISION))
            products.append(product)
        memory = step_decay[block][:, None] * memory + update[block]
        product = product * step_decay[block]
    local_out = inside + jnp.stack(local_outs)
    carry_lift = lifted_intact * jnp.stack(products)[:, None, :]
    return (local_out, carry_lift, memory, product)


def prefix_states(decay, memory, axis):
    count = lax.axis_size(axis)
    place = lax.axis_index(axis)
    entering_decay = jnp.ones_like(decay)
    entering = jnp.zeros_like(memory)
    steps = 1
    while steps < count:
        earlier_decay, earlier_memory = shifted((decay, memory), axis, steps)
        valid = place >= steps
        memory = jnp.where(valid, decay[:, None] * earlier_memory + memory, memory)
        decay = jnp.where(valid, earlier_decay * decay, decay)
        if steps == 1:
            entering = earlier_memory
            entering_decay = earlier_decay
        else:
            entering = jnp.where(valid, entering_decay[:, None] * earlier_memory + entering, entering)
            entering_decay = jnp.where(valid, earlier_decay * entering_decay, entering_decay)
        steps *= 2
    return (memory, entering)


def rotations(axis):
    count = lax.axis_size(axis)
    return [[(source, (source + step) % count) for source in range(count)] for step in range(1, count)]


def gather_rows(rows, axis):
    count = lax.axis_size(axis)
    place = lax.axis_index(axis)
    received = [rows] + [lax.ppermute(rows, axis, pairs) for pairs in rotations(axis)]
    reverse = [received[(-index) % count] for index in range(count)]
    doubled = jnp.stack(reverse + reverse)
    ordered = lax.dynamic_slice_in_dim(doubled, (count - place) % count, count, axis=0)
    return ordered.reshape((count * rows.shape[0],) + rows.shape[1:])


def scatter_sum(terms, axis):
    count = lax.axis_size(axis)
    place = lax.axis_index(axis)
    chunks = terms.reshape((count, terms.shape[0] // count) + terms.shape[1:])
    total = lax.dynamic_index_in_dim(chunks, place, 0, False).astype(jnp.float32)
    for step, pairs in enumerate(rotations(axis), start=1):
        outgoing = lax.dynamic_index_in_dim(chunks, (place + step) % count, 0, False)
        total = total + lax.ppermute(outgoing, axis, pairs).astype(jnp.float32)
    return total.astype(jnp.bfloat16)


def shards(
    tokens,
    prompt_lengths,
    query_weight,
    key_weight,
    value_weight,
    query_conv,
    key_conv,
    value_conv,
    decay_down,
    decay_up,
    decay_bias,
    gate_weight,
    norm_gain,
    out_weight,
):
    gathered = gather_rows(tokens, "hv")

    def project(weight):
        return jnp.dot(gathered, weight, preferred_element_type=jnp.float32).astype(jnp.bfloat16)

    raw_query = project(query_weight)
    raw_key = project(key_weight)
    raw_value = project(value_weight)
    gate_values = project(gate_weight)
    low_rank = project(decay_down)
    row_count = raw_query.shape[0]
    key_width = raw_query.shape[1]
    value_width = raw_value.shape[1]
    positions = lax.axis_index("tok") * row_count + jnp.arange(row_count, dtype=jnp.int32)
    offsets = jnp.cumsum(prompt_lengths) - prompt_lengths
    prompt_first, starts = prompt_marks(positions, offsets)
    rim_rows = query_conv.shape[0] - 1
    joined = jnp.concatenate([raw_query, raw_key, raw_value], axis=1)
    before_rows = shifted(joined[row_count - rim_rows :], "tok", 1)
    conv_query = short_conv(
        raw_query, before_rows[:, :key_width], query_conv, positions, prompt_first
    )
    conv_key = short_conv(
        raw_key, before_rows[:, key_width : 2 * key_width], key_conv, positions, prompt_first
    )
    conv_value = short_conv(
        raw_value, before_rows[:, 2 * key_width :], value_conv, positions, prompt_first
    )
    decays = (
        jax.nn.log_sigmoid(
            jnp.dot(low_rank, decay_up, preferred_element_type=jnp.float32) + decay_bias
        )
        / 16.0
    )
    local_out, carry_lift, local_memory, local_decay = segment_parts(
        blocked(conv_query), blocked(conv_key), blocked(conv_value), blocked(decays), blocked(starts)
    )
    closing, entering = prefix_states(local_decay, local_memory, "tok")
    heads_out = local_out.reshape((row_count, value_width)) + jnp.dot(
        carry_lift.reshape((row_count, key_width)), entering, precision=HIGHEST_PRECISION
    )
    gate_float = gate_values.astype(jnp.float32)
    rescale = lax.rsqrt(jnp.mean(heads_out * heads_out, axis=1, keepdims=True) + 1e-05)
    gated_out = (
        heads_out * rescale * norm_gain[None, :] * gate_float * jax.nn.sigmoid(gate_float)
    ).astype(jnp.bfloat16)
    mixed = scatter_sum(
        jnp.dot(gated_out, out_weight, preferred_element_type=jnp.float32).astype(jnp.bfloat16),
        "hv",
    )
    segment_states = closing[None, None]
    in_prompt = positions[row_count - rim_rows :] >= prompt_first[row_count - 1]
    tail_rows = joined[row_count - rim_rows :]
    conv_edges = jnp.where(in_prompt[:, None], tail_rows, jnp.zeros_like(tail_rows))
    conv_edges = conv_edges.reshape((1, rim_rows, 1, joined.shape[1]))
    return (mixed, segment_states, conv_edges)


def solution(mesh):
    in_specs = (
        P(("tok", "hv"), None),
        P(),
        P(None, "hv"),
        P(None, "hv"),
        P(None, "hv"),
        P(None, "hv"),
        P(None, "hv"),
        P(None, "hv"),
        P(),
        P(None, "hv"),
        P("hv"),
        P(None, "hv"),
        P(),
        P("hv", None),
    )
    out_specs = (P(("tok", "hv"), None), P("tok", "hv", None, None), P("tok", None, "hv", None))
    return jax.shard_map(shards, mesh=mesh, in_specs=in_specs, out_specs=out_specs, check_vma=False)
```

```python
import functools

import jax
import jax.numpy as jnp
from jax import lax
from jax.sharding import PartitionSpec as P

SPAN = 64


HIGHEST_PRECISION = lax.Precision.HIGHEST


def shifted(value, axis, steps):
    count = lax.axis_size(axis)
    initial, last = (max(0, -steps), min(count, count - steps))
    return lax.ppermute(value, axis, [(source, source + steps) for source in range(initial, last)])


def prompt_marks(positions, offsets):
    before = offsets[None, :] <= positions[:, None]
    prompt_first = jnp.max(jnp.where(before, offsets[None, :], 0), axis=1)
    return (prompt_first, (prompt_first == positions).astype(jnp.float32))


def short_conv(raw_rows, before_rows, weight, positions, prompt_first):
    tap_count = weight.shape[0]
    extended = jnp.concatenate([before_rows, raw_rows], axis=0)
    summed = jnp.zeros(raw_rows.shape, jnp.float32)
    for tap_index in range(tap_count):
        lag_rows = tap_count - 1 - tap_index
        inside_prompt = (positions - lag_rows >= prompt_first).astype(jnp.float32)
        window = lax.slice_in_dim(extended, tap_index, tap_index + raw_rows.shape[0], axis=0)
        summed = (
            summed
            + weight[tap_index].astype(jnp.float32)[None, :]
            * window.astype(jnp.float32)
            * inside_prompt[:, None]
        )
    return jax.nn.silu(summed).astype(jnp.bfloat16)


def blocked(array_in):
    return array_in.reshape((array_in.shape[0] // SPAN, SPAN) + array_in.shape[1:])


def segment_parts(queries, head_keys, head_values, decays, starts):
    cumulative = jnp.cumsum(decays, axis=1)
    groups = jnp.cumsum(starts, axis=1)
    intact = (groups == 0.0).astype(jnp.float32)
    final_log = cumulative[:, -1]
    in_tail = (groups == groups[:, -1:]).astype(jnp.float32)
    weighted = (
        head_keys.astype(jnp.float32)
        * jnp.exp(final_log[:, None, :] - cumulative)
        * in_tail[:, :, None]
    ).astype(jnp.bfloat16)
    update = jnp.einsum("bsk,bsv->bkv", weighted, head_values, preferred_element_type=jnp.float32)
    step_decay = jnp.exp(final_log) * intact[:, -1:]
    index_rows = jnp.arange(queries.shape[1])
    allowed = (groups[:, :, None] == groups[:, None, :]) & (
        index_rows[None, :, None] >= index_rows[None, None, :]
    )
    lifted = queries.astype(jnp.float32) * jnp.exp(cumulative)
    lowered = (head_keys.astype(jnp.float32) * jnp.exp(-cumulative)).astype(jnp.bfloat16)
    raw_scores = jnp.einsum(
        "bak,bck->bac", lifted.astype(jnp.bfloat16), lowered, preferred_element_type=jnp.float32
    )
    scores = jnp.where(allowed, raw_scores, 0.0).astype(jnp.bfloat16)
    inside = jnp.einsum("bac,bcv->bav", scores, head_values, preferred_element_type=jnp.float32)
    lifted_intact = lifted * intact[:, :, None]
    block_count = queries.shape[0]
    memory = jnp.zeros(update.shape[1:], jnp.float32)
    product = jnp.ones(step_decay.shape[1:], jnp.float32)
    local_outs = [jnp.zeros(inside.shape[1:], jnp.float32)]
    products = [product]
    for block in range(block_count):
        if block > 0:
            local_outs.append(jnp.dot(lifted_intact[block], memory, precision=HIGHEST_PRECISION))
            products.append(product)
        memory = step_decay[block][:, None] * memory + update[block]
        product = product * step_decay[block]
    local_out = inside + jnp.stack(local_outs)
    carry_lift = lifted_intact * jnp.stack(products)[:, None, :]
    return (local_out, carry_lift, memory, product)


def prefix_states(decay, memory, axis):
    count = lax.axis_size(axis)
    place = lax.axis_index(axis)
    entering_decay = jnp.ones_like(decay)
    entering = jnp.zeros_like(memory)
    steps = 1
    while steps < count:
        earlier_decay, earlier_memory = shifted((decay, memory), axis, steps)
        valid = place >= steps
        memory = jnp.where(valid, decay[:, None] * earlier_memory + memory, memory)
        decay = jnp.where(valid, earlier_decay * decay, decay)
        if steps == 1:
            entering = earlier_memory
            entering_decay = earlier_decay
        else:
            entering = jnp.where(valid, entering_decay[:, None] * earlier_memory + entering, entering)
            entering_decay = jnp.where(valid, earlier_decay * entering_decay, entering_decay)
        steps *= 2
    return (memory, entering)


def rotations(axis):
    count = lax.axis_size(axis)
    return [[(source, (source + step) % count) for source in range(count)] for step in range(1, count)]


def gather_rows(rows, axis):
    count = lax.axis_size(axis)
    place = lax.axis_index(axis)
    received = [rows] + [lax.ppermute(rows, axis, pairs) for pairs in rotations(axis)]

    def ordered(shift):
        return jnp.concatenate([received[(shift - index) % count] for index in range(count)])

    return lax.switch(place, [functools.partial(ordered, shift) for shift in range(count)])


def scatter_sum(terms, axis):
    count = lax.axis_size(axis)
    place = lax.axis_index(axis)
    chunks = terms.reshape((count, terms.shape[0] // count) + terms.shape[1:])
    total = lax.dynamic_index_in_dim(chunks, place, 0, False).astype(jnp.float32)
    for step, pairs in enumerate(rotations(axis), start=1):
        outgoing = lax.dynamic_index_in_dim(chunks, (place + step) % count, 0, False)
        total = total + lax.ppermute(outgoing, axis, pairs).astype(jnp.float32)
    return total.astype(jnp.bfloat16)


def shards(
    tokens,
    prompt_lengths,
    query_weight,
    key_weight,
    value_weight,
    query_conv,
    key_conv,
    value_conv,
    decay_down,
    decay_up,
    decay_bias,
    gate_weight,
    norm_gain,
    out_weight,
):
    gathered = gather_rows(tokens, "hv")

    def project(weight):
        return jnp.dot(gathered, weight, preferred_element_type=jnp.float32).astype(jnp.bfloat16)

    raw_query = project(query_weight)
    raw_key = project(key_weight)
    raw_value = project(value_weight)
    gate_values = project(gate_weight)
    low_rank = project(decay_down)
    row_count = raw_query.shape[0]
    key_width = raw_query.shape[1]
    value_width = raw_value.shape[1]
    positions = lax.axis_index("tok") * row_count + jnp.arange(row_count, dtype=jnp.int32)
    offsets = jnp.cumsum(prompt_lengths) - prompt_lengths
    prompt_first, starts = prompt_marks(positions, offsets)
    rim_rows = query_conv.shape[0] - 1
    joined = jnp.concatenate([raw_query, raw_key, raw_value], axis=1)
    before_rows = shifted(joined[row_count - rim_rows :], "tok", 1)
    conv_query = short_conv(
        raw_query, before_rows[:, :key_width], query_conv, positions, prompt_first
    )
    conv_key = short_conv(
        raw_key, before_rows[:, key_width : 2 * key_width], key_conv, positions, prompt_first
    )
    conv_value = short_conv(
        raw_value, before_rows[:, 2 * key_width :], value_conv, positions, prompt_first
    )
    decays = (
        jax.nn.log_sigmoid(
            jnp.dot(low_rank, decay_up, preferred_element_type=jnp.float32) + decay_bias
        )
        / 16.0
    )
    local_out, carry_lift, local_memory, local_decay = segment_parts(
        blocked(conv_query), blocked(conv_key), blocked(conv_value), blocked(decays), blocked(starts)
    )
    closing, entering = prefix_states(local_decay, local_memory, "tok")
    heads_out = local_out.reshape((row_count, value_width)) + jnp.dot(
        carry_lift.reshape((row_count, key_width)), entering, precision=HIGHEST_PRECISION
    )
    gate_float = gate_values.astype(jnp.float32)
    rescale = lax.rsqrt(jnp.mean(heads_out * heads_out, axis=1, keepdims=True) + 1e-05)
    gated_out = (
        heads_out * rescale * norm_gain[None, :] * gate_float * jax.nn.sigmoid(gate_float)
    ).astype(jnp.bfloat16)
    mixed = scatter_sum(
        jnp.dot(gated_out, out_weight, preferred_element_type=jnp.float32).astype(jnp.bfloat16),
        "hv",
    )
    segment_states = closing[None, None]
    in_prompt = positions[row_count - rim_rows :] >= prompt_first[row_count - 1]
    tail_rows = joined[row_count - rim_rows :]
    conv_edges = jnp.where(in_prompt[:, None], tail_rows, jnp.zeros_like(tail_rows))
    conv_edges = conv_edges.reshape((1, rim_rows, 1, joined.shape[1]))
    return (mixed, segment_states, conv_edges)


def solution(mesh):
    in_specs = (
        P(("tok", "hv"), None),
        P(),
        P(None, "hv"),
        P(None, "hv"),
        P(None, "hv"),
        P(None, "hv"),
        P(None, "hv"),
        P(None, "hv"),
        P(),
        P(None, "hv"),
        P("hv"),
        P(None, "hv"),
        P(),
        P("hv", None),
    )
    out_specs = (P(("tok", "hv"), None), P("tok", "hv", None, None), P("tok", None, "hv", None))
    return jax.shard_map(shards, mesh=mesh, in_specs=in_specs, out_specs=out_specs, check_vma=False)
```

```python
import functools

import jax
import jax.numpy as jnp
from jax import lax
from jax.sharding import PartitionSpec as P

SPAN = 64


HIGHEST_PRECISION = lax.Precision.HIGHEST


def shifted(value, axis, steps):
    count = lax.axis_size(axis)
    initial, last = (max(0, -steps), min(count, count - steps))
    return lax.ppermute(value, axis, [(source, source + steps) for source in range(initial, last)])


def prompt_marks(positions, offsets):
    before = offsets[None, :] <= positions[:, None]
    prompt_first = jnp.max(jnp.where(before, offsets[None, :], 0), axis=1)
    return (prompt_first, (prompt_first == positions).astype(jnp.float32))


def short_conv(raw_rows, before_rows, weight, positions, prompt_first):
    tap_count = weight.shape[0]
    extended = jnp.concatenate([before_rows, raw_rows], axis=0)
    summed = jnp.zeros(raw_rows.shape, jnp.float32)
    for tap_index in range(tap_count):
        lag_rows = tap_count - 1 - tap_index
        inside_prompt = (positions - lag_rows >= prompt_first).astype(jnp.float32)
        window = lax.slice_in_dim(extended, tap_index, tap_index + raw_rows.shape[0], axis=0)
        summed = (
            summed
            + weight[tap_index].astype(jnp.float32)[None, :]
            * window.astype(jnp.float32)
            * inside_prompt[:, None]
        )
    return jax.nn.silu(summed).astype(jnp.bfloat16)


def blocked(array_in):
    return array_in.reshape((array_in.shape[0] // SPAN, SPAN) + array_in.shape[1:])


def segment_parts(queries, head_keys, head_values, decays, starts):
    cumulative = jnp.cumsum(decays, axis=1)
    groups = jnp.cumsum(starts, axis=1)
    intact = (groups == 0.0).astype(jnp.float32)
    final_log = cumulative[:, -1]
    in_tail = (groups == groups[:, -1:]).astype(jnp.float32)
    weighted = (
        head_keys.astype(jnp.float32)
        * jnp.exp(final_log[:, None, :] - cumulative)
        * in_tail[:, :, None]
    ).astype(jnp.bfloat16)
    update = jnp.einsum("bsk,bsv->bkv", weighted, head_values, preferred_element_type=jnp.float32)
    step_decay = jnp.exp(final_log) * intact[:, -1:]
    index_rows = jnp.arange(queries.shape[1])
    allowed = (groups[:, :, None] == groups[:, None, :]) & (
        index_rows[None, :, None] >= index_rows[None, None, :]
    )
    lifted = queries.astype(jnp.float32) * jnp.exp(cumulative)
    lowered = (head_keys.astype(jnp.float32) * jnp.exp(-cumulative)).astype(jnp.bfloat16)
    raw_scores = jnp.einsum(
        "bak,bck->bac", lifted.astype(jnp.bfloat16), lowered, preferred_element_type=jnp.float32
    )
    scores = jnp.where(allowed, raw_scores, 0.0).astype(jnp.bfloat16)
    inside = jnp.einsum("bac,bcv->bav", scores, head_values, preferred_element_type=jnp.float32)
    lifted_intact = lifted * intact[:, :, None]
    block_count = queries.shape[0]
    memory = jnp.zeros(update.shape[1:], jnp.float32)
    product = jnp.ones(step_decay.shape[1:], jnp.float32)
    local_outs = [jnp.zeros(inside.shape[1:], jnp.float32)]
    products = [product]
    for block in range(block_count):
        if block > 0:
            local_outs.append(jnp.dot(lifted_intact[block], memory, precision=HIGHEST_PRECISION))
            products.append(product)
        memory = step_decay[block][:, None] * memory + update[block]
        product = product * step_decay[block]
    local_out = inside + jnp.stack(local_outs)
    carry_lift = lifted_intact * jnp.stack(products)[:, None, :]
    return (local_out, carry_lift, memory, product)


def prefix_states(decay, memory, axis):
    count = lax.axis_size(axis)
    place = lax.axis_index(axis)
    entering_decay = jnp.ones_like(decay)
    entering = jnp.zeros_like(memory)
    steps = 1
    while steps < count:
        earlier_decay, earlier_memory = shifted((decay, memory.astype(jnp.bfloat16)), axis, steps)
        earlier_memory = earlier_memory.astype(jnp.float32)
        valid = place >= steps
        memory = jnp.where(valid, decay[:, None] * earlier_memory + memory, memory)
        decay = jnp.where(valid, earlier_decay * decay, decay)
        if steps == 1:
            entering = earlier_memory
            entering_decay = earlier_decay
        else:
            entering = jnp.where(valid, entering_decay[:, None] * earlier_memory + entering, entering)
            entering_decay = jnp.where(valid, earlier_decay * entering_decay, entering_decay)
        steps *= 2
    return (memory, entering)


def rotations(axis):
    count = lax.axis_size(axis)
    return [[(source, (source + step) % count) for source in range(count)] for step in range(1, count)]


def gather_rows(rows, axis):
    count = lax.axis_size(axis)
    place = lax.axis_index(axis)
    received = [rows] + [lax.ppermute(rows, axis, pairs) for pairs in rotations(axis)]

    def ordered(shift):
        return jnp.concatenate([received[(shift - index) % count] for index in range(count)])

    return lax.switch(place, [functools.partial(ordered, shift) for shift in range(count)])


def scatter_sum(terms, axis):
    count = lax.axis_size(axis)
    place = lax.axis_index(axis)
    chunks = terms.reshape((count, terms.shape[0] // count) + terms.shape[1:])
    total = lax.dynamic_index_in_dim(chunks, place, 0, False).astype(jnp.float32)
    for step, pairs in enumerate(rotations(axis), start=1):
        outgoing = lax.dynamic_index_in_dim(chunks, (place + step) % count, 0, False)
        total = total + lax.ppermute(outgoing, axis, pairs).astype(jnp.float32)
    return total.astype(jnp.bfloat16)


def shards(
    tokens,
    prompt_lengths,
    query_weight,
    key_weight,
    value_weight,
    query_conv,
    key_conv,
    value_conv,
    decay_down,
    decay_up,
    decay_bias,
    gate_weight,
    norm_gain,
    out_weight,
):
    gathered = gather_rows(tokens, "hv")

    def project(weight):
        return jnp.dot(gathered, weight, preferred_element_type=jnp.float32).astype(jnp.bfloat16)

    raw_query = project(query_weight)
    raw_key = project(key_weight)
    raw_value = project(value_weight)
    gate_values = project(gate_weight)
    low_rank = project(decay_down)
    row_count = raw_query.shape[0]
    key_width = raw_query.shape[1]
    value_width = raw_value.shape[1]
    positions = lax.axis_index("tok") * row_count + jnp.arange(row_count, dtype=jnp.int32)
    offsets = jnp.cumsum(prompt_lengths) - prompt_lengths
    prompt_first, starts = prompt_marks(positions, offsets)
    rim_rows = query_conv.shape[0] - 1
    joined = jnp.concatenate([raw_query, raw_key, raw_value], axis=1)
    before_rows = shifted(joined[row_count - rim_rows :], "tok", 1)
    conv_query = short_conv(
        raw_query, before_rows[:, :key_width], query_conv, positions, prompt_first
    )
    conv_key = short_conv(
        raw_key, before_rows[:, key_width : 2 * key_width], key_conv, positions, prompt_first
    )
    conv_value = short_conv(
        raw_value, before_rows[:, 2 * key_width :], value_conv, positions, prompt_first
    )
    decays = (
        jax.nn.log_sigmoid(
            jnp.dot(low_rank, decay_up, preferred_element_type=jnp.float32) + decay_bias
        )
        / 16.0
    )
    local_out, carry_lift, local_memory, local_decay = segment_parts(
        blocked(conv_query), blocked(conv_key), blocked(conv_value), blocked(decays), blocked(starts)
    )
    closing, entering = prefix_states(local_decay, local_memory, "tok")
    heads_out = local_out.reshape((row_count, value_width)) + jnp.dot(
        carry_lift.reshape((row_count, key_width)), entering, precision=HIGHEST_PRECISION
    )
    gate_float = gate_values.astype(jnp.float32)
    rescale = lax.rsqrt(jnp.mean(heads_out * heads_out, axis=1, keepdims=True) + 1e-05)
    gated_out = (
        heads_out * rescale * norm_gain[None, :] * gate_float * jax.nn.sigmoid(gate_float)
    ).astype(jnp.bfloat16)
    mixed = scatter_sum(
        jnp.dot(gated_out, out_weight, preferred_element_type=jnp.float32).astype(jnp.bfloat16),
        "hv",
    )
    segment_states = closing[None, None]
    in_prompt = positions[row_count - rim_rows :] >= prompt_first[row_count - 1]
    tail_rows = joined[row_count - rim_rows :]
    conv_edges = jnp.where(in_prompt[:, None], tail_rows, jnp.zeros_like(tail_rows))
    conv_edges = conv_edges.reshape((1, rim_rows, 1, joined.shape[1]))
    return (mixed, segment_states, conv_edges)


def solution(mesh):
    in_specs = (
        P(("tok", "hv"), None),
        P(),
        P(None, "hv"),
        P(None, "hv"),
        P(None, "hv"),
        P(None, "hv"),
        P(None, "hv"),
        P(None, "hv"),
        P(),
        P(None, "hv"),
        P("hv"),
        P(None, "hv"),
        P(),
        P("hv", None),
    )
    out_specs = (P(("tok", "hv"), None), P("tok", "hv", None, None), P("tok", None, "hv", None))
    return jax.shard_map(shards, mesh=mesh, in_specs=in_specs, out_specs=out_specs, check_vma=False)
```

```python
import functools

import jax
import jax.numpy as jnp
from jax import lax
from jax.sharding import PartitionSpec as P

SPAN = 64


HIGHEST_PRECISION = lax.Precision.HIGHEST


def shifted(value, axis, steps):
    count = lax.axis_size(axis)
    initial, last = (max(0, -steps), min(count, count - steps))
    return lax.ppermute(value, axis, [(source, source + steps) for source in range(initial, last)])


def prompt_marks(positions, offsets):
    before = offsets[None, :] <= positions[:, None]
    prompt_first = jnp.max(jnp.where(before, offsets[None, :], 0), axis=1)
    return (prompt_first, (prompt_first == positions).astype(jnp.float32))


def short_conv(raw_rows, before_rows, weight, positions, prompt_first):
    tap_count = weight.shape[0]
    extended = jnp.concatenate([before_rows, raw_rows], axis=0)
    summed = jnp.zeros(raw_rows.shape, jnp.float32)
    for tap_index in range(tap_count):
        lag_rows = tap_count - 1 - tap_index
        inside_prompt = (positions - lag_rows >= prompt_first).astype(jnp.float32)
        window = lax.slice_in_dim(extended, tap_index, tap_index + raw_rows.shape[0], axis=0)
        summed = (
            summed
            + weight[tap_index].astype(jnp.float32)[None, :]
            * window.astype(jnp.float32)
            * inside_prompt[:, None]
        )
    return jax.nn.silu(summed).astype(jnp.bfloat16)


def blocked(array_in):
    return array_in.reshape((array_in.shape[0] // SPAN, SPAN) + array_in.shape[1:])


def segment_parts(queries, head_keys, head_values, decays, starts):
    cumulative = jnp.cumsum(decays, axis=1)
    groups = jnp.cumsum(starts, axis=1)
    intact = (groups == 0.0).astype(jnp.float32)
    final_log = cumulative[:, -1]
    in_tail = (groups == groups[:, -1:]).astype(jnp.float32)
    weighted = (
        head_keys.astype(jnp.float32)
        * jnp.exp(final_log[:, None, :] - cumulative)
        * in_tail[:, :, None]
    ).astype(jnp.bfloat16)
    update = jnp.einsum("bsk,bsv->bkv", weighted, head_values, preferred_element_type=jnp.float32)
    step_decay = jnp.exp(final_log) * intact[:, -1:]
    index_rows = jnp.arange(queries.shape[1])
    allowed = (groups[:, :, None] == groups[:, None, :]) & (
        index_rows[None, :, None] >= index_rows[None, None, :]
    )
    lifted = queries.astype(jnp.float32) * jnp.exp(cumulative)
    lowered = (head_keys.astype(jnp.float32) * jnp.exp(-cumulative)).astype(jnp.bfloat16)
    raw_scores = jnp.einsum(
        "bak,bck->bac", lifted.astype(jnp.bfloat16), lowered, preferred_element_type=jnp.float32
    )
    scores = jnp.where(allowed, raw_scores, 0.0).astype(jnp.bfloat16)
    inside = jnp.einsum("bac,bcv->bav", scores, head_values, preferred_element_type=jnp.float32)
    lifted_intact = lifted * intact[:, :, None]
    block_count = queries.shape[0]
    memory = jnp.zeros(update.shape[1:], jnp.float32)
    product = jnp.ones(step_decay.shape[1:], jnp.float32)
    local_outs = [jnp.zeros(inside.shape[1:], jnp.float32)]
    products = [product]
    for block in range(block_count):
        if block > 0:
            local_outs.append(jnp.dot(lifted_intact[block], memory, precision=HIGHEST_PRECISION))
            products.append(product)
        memory = step_decay[block][:, None] * memory + update[block]
        product = product * step_decay[block]
    local_out = inside + jnp.stack(local_outs)
    carry_lift = lifted_intact * jnp.stack(products)[:, None, :]
    return (local_out, carry_lift, memory, product)


def packed_state(decay, memory):
    high = decay.astype(jnp.bfloat16)
    low = (decay - high.astype(jnp.float32)).astype(jnp.bfloat16)
    width = memory.shape[1]
    flat = jnp.concatenate([high, low])
    flat = jnp.pad(flat, (0, -flat.shape[0] % width))
    return jnp.concatenate([memory.astype(jnp.bfloat16), flat.reshape((-1, width))], axis=0)


def unpacked_state(packed, key_width):
    memory = packed[:key_width].astype(jnp.float32)
    flat = packed[key_width:].reshape((-1,)).astype(jnp.float32)
    return (flat[:key_width] + flat[key_width : 2 * key_width], memory)


def prefix_states(decay, memory, axis):
    count = lax.axis_size(axis)
    place = lax.axis_index(axis)
    key_width = memory.shape[0]
    entering_decay = jnp.ones_like(decay)
    entering = jnp.zeros_like(memory)
    steps = 1
    while steps < count:
        valid = place >= steps
        if steps * 2 < count:
            earlier_decay, earlier_memory = unpacked_state(
                shifted(packed_state(decay, memory), axis, steps), key_width
            )
        else:
            earlier_decay = None
            earlier_memory = shifted(memory.astype(jnp.bfloat16), axis, steps).astype(jnp.float32)
        memory = jnp.where(valid, decay[:, None] * earlier_memory + memory, memory)
        if steps == 1:
            entering = earlier_memory
            entering_decay = earlier_decay
        else:
            entering = jnp.where(valid, entering_decay[:, None] * earlier_memory + entering, entering)
        if earlier_decay is not None:
            decay = jnp.where(valid, earlier_decay * decay, decay)
            if steps > 1:
                entering_decay = jnp.where(valid, earlier_decay * entering_decay, entering_decay)
        steps *= 2
    return (memory, entering)


def rotations(axis):
    count = lax.axis_size(axis)
    return [[(source, (source + step) % count) for source in range(count)] for step in range(1, count)]


def gather_rows(rows, axis):
    count = lax.axis_size(axis)
    place = lax.axis_index(axis)
    if count & (count - 1):
        received = [rows] + [lax.ppermute(rows, axis, pairs) for pairs in rotations(axis)]
        order = [(-step) % count for step in range(count)]
    else:
        received = [rows]
        order = [0]
        mask = count // 2
        while mask >= 1:
            incoming = lax.ppermute(
                jnp.concatenate(received), axis, [(source, source ^ mask) for source in range(count)]
            )
            received = received + list(jnp.split(incoming, len(received)))
            order = order + [flip ^ mask for flip in order]
            mask //= 2

    def ordered(shift):
        if count & (count - 1):
            picks = [order.index((index - shift) % count) for index in range(count)]
        else:
            picks = [order.index(shift ^ index) for index in range(count)]
        return jnp.concatenate([received[pick] for pick in picks])

    return lax.switch(place, [functools.partial(ordered, shift) for shift in range(count)])


def scatter_sum(terms, axis):
    count = lax.axis_size(axis)
    place = lax.axis_index(axis)
    chunks = terms.reshape((count, terms.shape[0] // count) + terms.shape[1:])
    total = lax.dynamic_index_in_dim(chunks, place, 0, False).astype(jnp.float32)
    for step, pairs in enumerate(rotations(axis), start=1):
        outgoing = lax.dynamic_index_in_dim(chunks, (place + step) % count, 0, False)
        total = total + lax.ppermute(outgoing, axis, pairs).astype(jnp.float32)
    return total.astype(jnp.bfloat16)


def shards(
    tokens,
    prompt_lengths,
    query_weight,
    key_weight,
    value_weight,
    query_conv,
    key_conv,
    value_conv,
    decay_down,
    decay_up,
    decay_bias,
    gate_weight,
    norm_gain,
    out_weight,
):
    gathered = gather_rows(tokens, "hv")

    def project(weight):
        return jnp.dot(gathered, weight, preferred_element_type=jnp.float32).astype(jnp.bfloat16)

    raw_query = project(query_weight)
    raw_key = project(key_weight)
    raw_value = project(value_weight)
    gate_values = project(gate_weight)
    low_rank = project(decay_down)
    row_count = raw_query.shape[0]
    key_width = raw_query.shape[1]
    value_width = raw_value.shape[1]
    positions = lax.axis_index("tok") * row_count + jnp.arange(row_count, dtype=jnp.int32)
    offsets = jnp.cumsum(prompt_lengths) - prompt_lengths
    prompt_first, starts = prompt_marks(positions, offsets)
    rim_rows = query_conv.shape[0] - 1
    joined = jnp.concatenate([raw_query, raw_key, raw_value], axis=1)
    before_rows = shifted(joined[row_count - rim_rows :], "tok", 1)
    conv_query = short_conv(
        raw_query, before_rows[:, :key_width], query_conv, positions, prompt_first
    )
    conv_key = short_conv(
        raw_key, before_rows[:, key_width : 2 * key_width], key_conv, positions, prompt_first
    )
    conv_value = short_conv(
        raw_value, before_rows[:, 2 * key_width :], value_conv, positions, prompt_first
    )
    decays = (
        jax.nn.log_sigmoid(
            jnp.dot(low_rank, decay_up, preferred_element_type=jnp.float32) + decay_bias
        )
        / 16.0
    )
    local_out, carry_lift, local_memory, local_decay = segment_parts(
        blocked(conv_query), blocked(conv_key), blocked(conv_value), blocked(decays), blocked(starts)
    )
    closing, entering = prefix_states(local_decay, local_memory, "tok")
    heads_out = local_out.reshape((row_count, value_width)) + jnp.dot(
        carry_lift.reshape((row_count, key_width)), entering, precision=HIGHEST_PRECISION
    )
    gate_float = gate_values.astype(jnp.float32)
    rescale = lax.rsqrt(jnp.mean(heads_out * heads_out, axis=1, keepdims=True) + 1e-05)
    gated_out = (
        heads_out * rescale * norm_gain[None, :] * gate_float * jax.nn.sigmoid(gate_float)
    ).astype(jnp.bfloat16)
    mixed = scatter_sum(
        jnp.dot(gated_out, out_weight, preferred_element_type=jnp.float32).astype(jnp.bfloat16),
        "hv",
    )
    segment_states = closing[None, None]
    in_prompt = positions[row_count - rim_rows :] >= prompt_first[row_count - 1]
    tail_rows = joined[row_count - rim_rows :]
    conv_edges = jnp.where(in_prompt[:, None], tail_rows, jnp.zeros_like(tail_rows))
    conv_edges = conv_edges.reshape((1, rim_rows, 1, joined.shape[1]))
    return (mixed, segment_states, conv_edges)


def solution(mesh):
    in_specs = (
        P(("tok", "hv"), None),
        P(),
        P(None, "hv"),
        P(None, "hv"),
        P(None, "hv"),
        P(None, "hv"),
        P(None, "hv"),
        P(None, "hv"),
        P(),
        P(None, "hv"),
        P("hv"),
        P(None, "hv"),
        P(),
        P("hv", None),
    )
    out_specs = (P(("tok", "hv"), None), P("tok", "hv", None, None), P("tok", None, "hv", None))
    return jax.shard_map(shards, mesh=mesh, in_specs=in_specs, out_specs=out_specs, check_vma=False)
```

```python
import functools

import jax
import jax.numpy as jnp
from jax import lax
from jax.sharding import PartitionSpec as P

SPAN = 64


HIGH_PRECISION = lax.Precision.HIGH


def shifted(value, axis, steps):
    count = lax.axis_size(axis)
    initial, last = (max(0, -steps), min(count, count - steps))
    return lax.ppermute(value, axis, [(source, source + steps) for source in range(initial, last)])


def prompt_marks(positions, offsets):
    before = offsets[None, :] <= positions[:, None]
    prompt_first = jnp.max(jnp.where(before, offsets[None, :], 0), axis=1)
    return (prompt_first, (prompt_first == positions).astype(jnp.float32))


def short_conv(raw_rows, before_rows, weight, positions, prompt_first):
    tap_count = weight.shape[0]
    extended = jnp.concatenate([before_rows, raw_rows], axis=0)
    summed = jnp.zeros(raw_rows.shape, jnp.float32)
    for tap_index in range(tap_count):
        lag_rows = tap_count - 1 - tap_index
        inside_prompt = (positions - lag_rows >= prompt_first).astype(jnp.float32)
        window = lax.slice_in_dim(extended, tap_index, tap_index + raw_rows.shape[0], axis=0)
        summed = (
            summed
            + weight[tap_index].astype(jnp.float32)[None, :]
            * window.astype(jnp.float32)
            * inside_prompt[:, None]
        )
    return jax.nn.silu(summed).astype(jnp.bfloat16)


def blocked(array_in):
    return array_in.reshape((array_in.shape[0] // SPAN, SPAN) + array_in.shape[1:])


def segment_parts(queries, head_keys, head_values, decays, starts):
    cumulative = jnp.cumsum(decays, axis=1)
    groups = jnp.cumsum(starts, axis=1)
    intact = (groups == 0.0).astype(jnp.float32)
    final_log = cumulative[:, -1]
    in_tail = (groups == groups[:, -1:]).astype(jnp.float32)
    weighted = (
        head_keys.astype(jnp.float32)
        * jnp.exp(final_log[:, None, :] - cumulative)
        * in_tail[:, :, None]
    ).astype(jnp.bfloat16)
    update = jnp.einsum("bsk,bsv->bkv", weighted, head_values, preferred_element_type=jnp.float32)
    step_decay = jnp.exp(final_log) * intact[:, -1:]
    index_rows = jnp.arange(queries.shape[1])
    allowed = (groups[:, :, None] == groups[:, None, :]) & (
        index_rows[None, :, None] >= index_rows[None, None, :]
    )
    lifted = queries.astype(jnp.float32) * jnp.exp(cumulative)
    lowered = (head_keys.astype(jnp.float32) * jnp.exp(-cumulative)).astype(jnp.bfloat16)
    raw_scores = jnp.einsum(
        "bak,bck->bac", lifted.astype(jnp.bfloat16), lowered, preferred_element_type=jnp.float32
    )
    scores = jnp.where(allowed, raw_scores, 0.0).astype(jnp.bfloat16)
    inside = jnp.einsum("bac,bcv->bav", scores, head_values, preferred_element_type=jnp.float32)
    lifted_intact = lifted * intact[:, :, None]
    block_count = queries.shape[0]
    memory = jnp.zeros(update.shape[1:], jnp.float32)
    product = jnp.ones(step_decay.shape[1:], jnp.float32)
    local_outs = [jnp.zeros(inside.shape[1:], jnp.float32)]
    products = [product]
    for block in range(block_count):
        if block > 0:
            local_outs.append(jnp.dot(lifted_intact[block], memory, precision=HIGH_PRECISION))
            products.append(product)
        memory = step_decay[block][:, None] * memory + update[block]
        product = product * step_decay[block]
    local_out = inside + jnp.stack(local_outs)
    carry_lift = lifted_intact * jnp.stack(products)[:, None, :]
    return (local_out, carry_lift, memory, product)


def packed_state(decay, memory):
    high = decay.astype(jnp.bfloat16)
    low = (decay - high.astype(jnp.float32)).astype(jnp.bfloat16)
    width = memory.shape[1]
    flat = jnp.concatenate([high, low])
    flat = jnp.pad(flat, (0, -flat.shape[0] % width))
    return jnp.concatenate([memory.astype(jnp.bfloat16), flat.reshape((-1, width))], axis=0)


def unpacked_state(packed, key_width):
    memory = packed[:key_width].astype(jnp.float32)
    flat = packed[key_width:].reshape((-1,)).astype(jnp.float32)
    return (flat[:key_width] + flat[key_width : 2 * key_width], memory)


def prefix_states(decay, memory, axis):
    count = lax.axis_size(axis)
    place = lax.axis_index(axis)
    key_width = memory.shape[0]
    entering_decay = jnp.ones_like(decay)
    entering = jnp.zeros_like(memory)
    steps = 1
    while steps < count:
        valid = place >= steps
        if steps * 2 < count:
            earlier_decay, earlier_memory = unpacked_state(
                shifted(packed_state(decay, memory), axis, steps), key_width
            )
        else:
            earlier_decay = None
            earlier_memory = shifted(memory.astype(jnp.bfloat16), axis, steps).astype(jnp.float32)
        memory = jnp.where(valid, decay[:, None] * earlier_memory + memory, memory)
        if steps == 1:
            entering = earlier_memory
            entering_decay = earlier_decay
        else:
            entering = jnp.where(valid, entering_decay[:, None] * earlier_memory + entering, entering)
        if earlier_decay is not None:
            decay = jnp.where(valid, earlier_decay * decay, decay)
            if steps > 1:
                entering_decay = jnp.where(valid, earlier_decay * entering_decay, entering_decay)
        steps *= 2
    return (memory, entering)


def rotations(axis):
    count = lax.axis_size(axis)
    return [[(source, (source + step) % count) for source in range(count)] for step in range(1, count)]


def gather_rows(rows, axis):
    count = lax.axis_size(axis)
    place = lax.axis_index(axis)
    if count & (count - 1):
        received = [rows] + [lax.ppermute(rows, axis, pairs) for pairs in rotations(axis)]
        order = [(-step) % count for step in range(count)]
    else:
        received = [rows]
        order = [0]
        mask = count // 2
        while mask >= 1:
            incoming = lax.ppermute(
                jnp.concatenate(received), axis, [(source, source ^ mask) for source in range(count)]
            )
            received = received + list(jnp.split(incoming, len(received)))
            order = order + [flip ^ mask for flip in order]
            mask //= 2

    def ordered(shift):
        if count & (count - 1):
            picks = [order.index((index - shift) % count) for index in range(count)]
        else:
            picks = [order.index(shift ^ index) for index in range(count)]
        return jnp.concatenate([received[pick] for pick in picks])

    return lax.switch(place, [functools.partial(ordered, shift) for shift in range(count)])


def scatter_sum(gated, weight, axis):
    count = lax.axis_size(axis)
    place = lax.axis_index(axis)
    chunk = gated.shape[0] // count

    def term(index):
        rows = lax.slice_in_dim(gated, index * chunk, (index + 1) * chunk, axis=0)
        return jnp.dot(rows, weight, preferred_element_type=jnp.float32).astype(jnp.bfloat16)

    if count & (count - 1):
        chunks = jnp.stack([term(index) for index in range(count)])
        total = lax.dynamic_index_in_dim(chunks, place, 0, False).astype(jnp.float32)
        for step, pairs in enumerate(rotations(axis), start=1):
            outgoing = lax.dynamic_index_in_dim(chunks, (place + step) % count, 0, False)
            total = total + lax.ppermute(outgoing, axis, pairs).astype(jnp.float32)
        return total.astype(jnp.bfloat16)
    held = [term(index) for index in range(count)]
    mask = 1
    while mask < count:
        odd = (place // mask) % 2 == 1
        pairs = list(zip(held[0::2], held[1::2]))
        keep = [jnp.where(odd, high, low) for low, high in pairs]
        outgoing = jnp.stack([jnp.where(odd, low, high).astype(jnp.bfloat16) for low, high in pairs])
        incoming = lax.ppermute(outgoing, axis, [(source, source ^ mask) for source in range(count)])
        held = [
            kept.astype(jnp.float32) + incoming[index].astype(jnp.float32)
            for index, kept in enumerate(keep)
        ]
        mask *= 2
    return held[0].astype(jnp.bfloat16)


def shards(
    tokens,
    prompt_lengths,
    query_weight,
    key_weight,
    value_weight,
    query_conv,
    key_conv,
    value_conv,
    decay_down,
    decay_up,
    decay_bias,
    gate_weight,
    norm_gain,
    out_weight,
):
    gathered = gather_rows(tokens, "hv")

    def project(weight):
        return jnp.dot(gathered, weight, preferred_element_type=jnp.float32).astype(jnp.bfloat16)

    raw_query = project(query_weight)
    raw_key = project(key_weight)
    raw_value = project(value_weight)
    gate_values = project(gate_weight)
    low_rank = project(decay_down)
    row_count = raw_query.shape[0]
    key_width = raw_query.shape[1]
    value_width = raw_value.shape[1]
    positions = lax.axis_index("tok") * row_count + jnp.arange(row_count, dtype=jnp.int32)
    offsets = jnp.cumsum(prompt_lengths) - prompt_lengths
    prompt_first, starts = prompt_marks(positions, offsets)
    rim_rows = query_conv.shape[0] - 1
    joined = jnp.concatenate([raw_query, raw_key, raw_value], axis=1)
    before_rows = shifted(joined[row_count - rim_rows :], "tok", 1)
    conv_query = short_conv(
        raw_query, before_rows[:, :key_width], query_conv, positions, prompt_first
    )
    conv_key = short_conv(
        raw_key, before_rows[:, key_width : 2 * key_width], key_conv, positions, prompt_first
    )
    conv_value = short_conv(
        raw_value, before_rows[:, 2 * key_width :], value_conv, positions, prompt_first
    )
    decays = (
        jax.nn.log_sigmoid(
            jnp.dot(low_rank, decay_up, preferred_element_type=jnp.float32) + decay_bias
        )
        / 16.0
    )
    local_out, carry_lift, local_memory, local_decay = segment_parts(
        blocked(conv_query), blocked(conv_key), blocked(conv_value), blocked(decays), blocked(starts)
    )
    closing, entering = prefix_states(local_decay, local_memory, "tok")
    heads_out = local_out.reshape((row_count, value_width)) + jnp.dot(
        carry_lift.reshape((row_count, key_width)), entering, precision=HIGH_PRECISION
    )
    gate_float = gate_values.astype(jnp.float32)
    rescale = lax.rsqrt(jnp.mean(heads_out * heads_out, axis=1, keepdims=True) + 1e-05)
    gated_out = (
        heads_out * rescale * norm_gain[None, :] * gate_float * jax.nn.sigmoid(gate_float)
    ).astype(jnp.bfloat16)
    mixed = scatter_sum(gated_out, out_weight, "hv")
    segment_states = closing[None, None]
    in_prompt = positions[row_count - rim_rows :] >= prompt_first[row_count - 1]
    tail_rows = joined[row_count - rim_rows :]
    conv_edges = jnp.where(in_prompt[:, None], tail_rows, jnp.zeros_like(tail_rows))
    conv_edges = conv_edges.reshape((1, rim_rows, 1, joined.shape[1]))
    return (mixed, segment_states, conv_edges)


def solution(mesh):
    in_specs = (
        P(("tok", "hv"), None),
        P(),
        P(None, "hv"),
        P(None, "hv"),
        P(None, "hv"),
        P(None, "hv"),
        P(None, "hv"),
        P(None, "hv"),
        P(),
        P(None, "hv"),
        P("hv"),
        P(None, "hv"),
        P(),
        P("hv", None),
    )
    out_specs = (P(("tok", "hv"), None), P("tok", "hv", None, None), P("tok", None, "hv", None))
    return jax.shard_map(shards, mesh=mesh, in_specs=in_specs, out_specs=out_specs, check_vma=False)
```

```python
import functools

import jax
import jax.numpy as jnp
from jax import lax
from jax.sharding import PartitionSpec as P

SPAN = 64


HIGH_PRECISION = lax.Precision.HIGH


def shifted(value, axis, steps):
    count = lax.axis_size(axis)
    initial, last = (max(0, -steps), min(count, count - steps))
    return lax.ppermute(value, axis, [(source, source + steps) for source in range(initial, last)])


def prompt_marks(positions, offsets):
    before = offsets[None, :] <= positions[:, None]
    prompt_first = jnp.max(jnp.where(before, offsets[None, :], 0), axis=1)
    return (prompt_first, (prompt_first == positions).astype(jnp.float32))


def short_conv(raw_rows, before_rows, weight, positions, prompt_first):
    tap_count = weight.shape[0]
    extended = jnp.concatenate([before_rows, raw_rows], axis=0)
    summed = jnp.zeros(raw_rows.shape, jnp.float32)
    for tap_index in range(tap_count):
        lag_rows = tap_count - 1 - tap_index
        inside_prompt = (positions - lag_rows >= prompt_first).astype(jnp.float32)
        window = lax.slice_in_dim(extended, tap_index, tap_index + raw_rows.shape[0], axis=0)
        summed = (
            summed
            + weight[tap_index].astype(jnp.float32)[None, :]
            * window.astype(jnp.float32)
            * inside_prompt[:, None]
        )
    return jax.nn.silu(summed).astype(jnp.bfloat16)


def blocked(array_in):
    return array_in.reshape((array_in.shape[0] // SPAN, SPAN) + array_in.shape[1:])


def segment_parts(queries, head_keys, head_values, decays, starts):
    cumulative = jnp.cumsum(decays, axis=1)
    groups = jnp.cumsum(starts, axis=1)
    intact = (groups == 0.0).astype(jnp.float32)
    final_log = cumulative[:, -1]
    in_tail = (groups == groups[:, -1:]).astype(jnp.float32)
    weighted = (
        head_keys.astype(jnp.float32)
        * jnp.exp(final_log[:, None, :] - cumulative)
        * in_tail[:, :, None]
    ).astype(jnp.bfloat16)
    update = jnp.einsum("bsk,bsv->bkv", weighted, head_values, preferred_element_type=jnp.float32)
    step_decay = jnp.exp(final_log) * intact[:, -1:]
    index_rows = jnp.arange(queries.shape[1])
    allowed = (groups[:, :, None] == groups[:, None, :]) & (
        index_rows[None, :, None] >= index_rows[None, None, :]
    )
    lifted = queries.astype(jnp.float32) * jnp.exp(cumulative)
    lowered = (head_keys.astype(jnp.float32) * jnp.exp(-cumulative)).astype(jnp.bfloat16)
    raw_scores = jnp.einsum(
        "bak,bck->bac", lifted.astype(jnp.bfloat16), lowered, preferred_element_type=jnp.float32
    )
    scores = jnp.where(allowed, raw_scores, 0.0).astype(jnp.bfloat16)
    inside = jnp.einsum("bac,bcv->bav", scores, head_values, preferred_element_type=jnp.float32)
    lifted_intact = lifted * intact[:, :, None]
    block_count = queries.shape[0]
    memory = jnp.zeros(update.shape[1:], jnp.float32)
    product = jnp.ones(step_decay.shape[1:], jnp.float32)
    local_outs = [jnp.zeros(inside.shape[1:], jnp.float32)]
    products = [product]
    for block in range(block_count):
        if block > 0:
            local_outs.append(jnp.dot(lifted_intact[block], memory, precision=HIGH_PRECISION))
            products.append(product)
        memory = step_decay[block][:, None] * memory + update[block]
        product = product * step_decay[block]
    local_out = inside + jnp.stack(local_outs)
    carry_lift = lifted_intact * jnp.stack(products)[:, None, :]
    return (local_out, carry_lift, memory, product)


def packed_state(decay, memory):
    high = decay.astype(jnp.bfloat16)
    low = (decay - high.astype(jnp.float32)).astype(jnp.bfloat16)
    width = memory.shape[1]
    flat = jnp.concatenate([high, low])
    flat = jnp.pad(flat, (0, -flat.shape[0] % width))
    return jnp.concatenate([memory.astype(jnp.bfloat16), flat.reshape((-1, width))], axis=0)


def unpacked_state(packed, key_width):
    memory = packed[:key_width].astype(jnp.float32)
    flat = packed[key_width:].reshape((-1,)).astype(jnp.float32)
    return (flat[:key_width] + flat[key_width : 2 * key_width], memory)


def prefix_states(decay, memory, axis):
    count = lax.axis_size(axis)
    place = lax.axis_index(axis)
    key_width = memory.shape[0]
    entering_decay = jnp.ones_like(decay)
    entering = jnp.zeros_like(memory)
    steps = 1
    while steps < count:
        valid = place >= steps
        if steps * 2 < count:
            earlier_decay, earlier_memory = unpacked_state(
                shifted(packed_state(decay, memory), axis, steps), key_width
            )
        else:
            earlier_decay = None
            earlier_memory = shifted(memory.astype(jnp.bfloat16), axis, steps).astype(jnp.float32)
        memory = jnp.where(valid, decay[:, None] * earlier_memory + memory, memory)
        if steps == 1:
            entering = earlier_memory
            entering_decay = earlier_decay
        else:
            entering = jnp.where(valid, entering_decay[:, None] * earlier_memory + entering, entering)
        if earlier_decay is not None:
            decay = jnp.where(valid, earlier_decay * decay, decay)
            if steps > 1:
                entering_decay = jnp.where(valid, earlier_decay * entering_decay, entering_decay)
        steps *= 2
    return (memory, entering)


def rotations(axis):
    count = lax.axis_size(axis)
    return [[(source, (source + step) % count) for source in range(count)] for step in range(1, count)]


def gather_rows(rows, axis):
    count = lax.axis_size(axis)
    place = lax.axis_index(axis)
    if count & (count - 1):
        received = [rows] + [lax.ppermute(rows, axis, pairs) for pairs in rotations(axis)]
        order = [(-step) % count for step in range(count)]
    else:
        received = [rows]
        order = [0]
        mask = count // 2
        while mask >= 1:
            incoming = lax.ppermute(
                jnp.concatenate(received), axis, [(source, source ^ mask) for source in range(count)]
            )
            received = received + list(jnp.split(incoming, len(received)))
            order = order + [flip ^ mask for flip in order]
            mask //= 2

    def ordered(shift):
        if count & (count - 1):
            picks = [order.index((index - shift) % count) for index in range(count)]
        else:
            picks = [order.index(shift ^ index) for index in range(count)]
        return jnp.concatenate([received[pick] for pick in picks])

    return lax.switch(place, [functools.partial(ordered, shift) for shift in range(count)])


def scatter_sum(gated, weight, axis):
    count = lax.axis_size(axis)
    terms = jnp.dot(gated, weight, preferred_element_type=jnp.float32).astype(jnp.bfloat16)
    parts = lax.all_to_all(terms.reshape((count, -1) + terms.shape[1:]), axis, 0, 0, tiled=True)
    return jnp.sum(parts.astype(jnp.float32), axis=0).astype(jnp.bfloat16)


def shards(
    tokens,
    prompt_lengths,
    query_weight,
    key_weight,
    value_weight,
    query_conv,
    key_conv,
    value_conv,
    decay_down,
    decay_up,
    decay_bias,
    gate_weight,
    norm_gain,
    out_weight,
):
    gathered = lax.all_to_all(
        jnp.broadcast_to(tokens[None], (lax.axis_size("hv"),) + tokens.shape), "hv", 0, 0, tiled=True
    ).reshape((-1, tokens.shape[1]))

    def project(weight):
        return jnp.dot(gathered, weight, preferred_element_type=jnp.float32).astype(jnp.bfloat16)

    raw_query = project(query_weight)
    raw_key = project(key_weight)
    raw_value = project(value_weight)
    gate_values = project(gate_weight)
    low_rank = project(decay_down)
    row_count = raw_query.shape[0]
    key_width = raw_query.shape[1]
    value_width = raw_value.shape[1]
    positions = lax.axis_index("tok") * row_count + jnp.arange(row_count, dtype=jnp.int32)
    offsets = jnp.cumsum(prompt_lengths) - prompt_lengths
    prompt_first, starts = prompt_marks(positions, offsets)
    rim_rows = query_conv.shape[0] - 1
    joined = jnp.concatenate([raw_query, raw_key, raw_value], axis=1)
    before_rows = shifted(joined[row_count - rim_rows :], "tok", 1)
    conv_query = short_conv(
        raw_query, before_rows[:, :key_width], query_conv, positions, prompt_first
    )
    conv_key = short_conv(
        raw_key, before_rows[:, key_width : 2 * key_width], key_conv, positions, prompt_first
    )
    conv_value = short_conv(
        raw_value, before_rows[:, 2 * key_width :], value_conv, positions, prompt_first
    )
    decays = (
        jax.nn.log_sigmoid(
            jnp.dot(low_rank, decay_up, preferred_element_type=jnp.float32) + decay_bias
        )
        / 16.0
    )
    local_out, carry_lift, local_memory, local_decay = segment_parts(
        blocked(conv_query), blocked(conv_key), blocked(conv_value), blocked(decays), blocked(starts)
    )
    closing, entering = prefix_states(local_decay, local_memory, "tok")
    heads_out = local_out.reshape((row_count, value_width)) + jnp.dot(
        carry_lift.reshape((row_count, key_width)), entering, precision=HIGH_PRECISION
    )
    gate_float = gate_values.astype(jnp.float32)
    rescale = lax.rsqrt(jnp.mean(heads_out * heads_out, axis=1, keepdims=True) + 1e-05)
    gated_out = (
        heads_out * rescale * norm_gain[None, :] * gate_float * jax.nn.sigmoid(gate_float)
    ).astype(jnp.bfloat16)
    mixed = scatter_sum(gated_out, out_weight, "hv")
    segment_states = closing[None, None]
    in_prompt = positions[row_count - rim_rows :] >= prompt_first[row_count - 1]
    tail_rows = joined[row_count - rim_rows :]
    conv_edges = jnp.where(in_prompt[:, None], tail_rows, jnp.zeros_like(tail_rows))
    conv_edges = conv_edges.reshape((1, rim_rows, 1, joined.shape[1]))
    return (mixed, segment_states, conv_edges)


def solution(mesh):
    in_specs = (
        P(("tok", "hv"), None),
        P(),
        P(None, "hv"),
        P(None, "hv"),
        P(None, "hv"),
        P(None, "hv"),
        P(None, "hv"),
        P(None, "hv"),
        P(),
        P(None, "hv"),
        P("hv"),
        P(None, "hv"),
        P(),
        P("hv", None),
    )
    out_specs = (P(("tok", "hv"), None), P("tok", "hv", None, None), P("tok", None, "hv", None))
    return jax.shard_map(shards, mesh=mesh, in_specs=in_specs, out_specs=out_specs, check_vma=False)
```

```python
import functools

import jax
import jax.numpy as jnp
from jax import lax
from jax.sharding import PartitionSpec as P

SPAN = 64


HIGH_PRECISION = lax.Precision.HIGH


def shifted(value, axis, steps):
    count = lax.axis_size(axis)
    initial, last = (max(0, -steps), min(count, count - steps))
    return lax.ppermute(value, axis, [(source, source + steps) for source in range(initial, last)])


def prompt_marks(positions, offsets):
    before = offsets[None, :] <= positions[:, None]
    prompt_first = jnp.max(jnp.where(before, offsets[None, :], 0), axis=1)
    return (prompt_first, (prompt_first == positions).astype(jnp.float32))


def short_conv(raw_rows, before_rows, weight, positions, prompt_first):
    tap_count = weight.shape[0]
    row_count = raw_rows.shape[0]
    extended = jnp.concatenate([before_rows, raw_rows], axis=0)
    lags = tap_count - 1 - jnp.arange(tap_count)
    inside_prompt = (positions[None, :] - lags[:, None] >= prompt_first[None, :]).astype(jnp.float32)
    windows = jnp.stack(
        [lax.slice_in_dim(extended, tap, tap + row_count, axis=0) for tap in range(tap_count)]
    )
    summed = jnp.sum(
        weight.astype(jnp.float32)[:, None, :]
        * windows.astype(jnp.float32)
        * inside_prompt[:, :, None],
        axis=0,
    )
    return jax.nn.silu(summed).astype(jnp.bfloat16)


def blocked(array_in):
    return array_in.reshape((array_in.shape[0] // SPAN, SPAN) + array_in.shape[1:])


def segment_parts(queries, head_keys, head_values, decays, starts):
    cumulative = jnp.cumsum(decays, axis=1)
    groups = jnp.cumsum(starts, axis=1)
    intact = (groups == 0.0).astype(jnp.float32)
    final_log = cumulative[:, -1]
    in_tail = (groups == groups[:, -1:]).astype(jnp.float32)
    weighted = (
        head_keys.astype(jnp.float32)
        * jnp.exp(final_log[:, None, :] - cumulative)
        * in_tail[:, :, None]
    ).astype(jnp.bfloat16)
    update = jnp.einsum("bsk,bsv->bkv", weighted, head_values, preferred_element_type=jnp.float32)
    step_decay = jnp.exp(final_log) * intact[:, -1:]
    index_rows = jnp.arange(queries.shape[1])
    allowed = (groups[:, :, None] == groups[:, None, :]) & (
        index_rows[None, :, None] >= index_rows[None, None, :]
    )
    lifted = queries.astype(jnp.float32) * jnp.exp(cumulative)
    lowered = (head_keys.astype(jnp.float32) * jnp.exp(-cumulative)).astype(jnp.bfloat16)
    raw_scores = jnp.einsum(
        "bak,bck->bac", lifted.astype(jnp.bfloat16), lowered, preferred_element_type=jnp.float32
    )
    scores = jnp.where(allowed, raw_scores, 0.0).astype(jnp.bfloat16)
    inside = jnp.einsum("bac,bcv->bav", scores, head_values, preferred_element_type=jnp.float32)
    lifted_intact = lifted * intact[:, :, None]
    block_count = queries.shape[0]
    memory = jnp.zeros(update.shape[1:], jnp.float32)
    product = jnp.ones(step_decay.shape[1:], jnp.float32)
    local_outs = [jnp.zeros(inside.shape[1:], jnp.float32)]
    products = [product]
    for block in range(block_count):
        if block > 0:
            local_outs.append(jnp.dot(lifted_intact[block], memory, precision=HIGH_PRECISION))
            products.append(product)
        memory = step_decay[block][:, None] * memory + update[block]
        product = product * step_decay[block]
    local_out = inside + jnp.stack(local_outs)
    carry_lift = lifted_intact * jnp.stack(products)[:, None, :]
    return (local_out, carry_lift, memory, product)


def packed_state(decay, memory):
    high = decay.astype(jnp.bfloat16)
    low = (decay - high.astype(jnp.float32)).astype(jnp.bfloat16)
    width = memory.shape[1]
    flat = jnp.concatenate([high, low])
    flat = jnp.pad(flat, (0, -flat.shape[0] % width))
    return jnp.concatenate([memory.astype(jnp.bfloat16), flat.reshape((-1, width))], axis=0)


def unpacked_state(packed, key_width):
    memory = packed[:key_width].astype(jnp.float32)
    flat = packed[key_width:].reshape((-1,)).astype(jnp.float32)
    return (flat[:key_width] + flat[key_width : 2 * key_width], memory)


def prefix_states(decay, memory, axis):
    count = lax.axis_size(axis)
    place = lax.axis_index(axis)
    key_width = memory.shape[0]
    entering_decay = jnp.ones_like(decay)
    entering = jnp.zeros_like(memory)
    steps = 1
    while steps < count:
        valid = place >= steps
        if steps * 2 < count:
            earlier_decay, earlier_memory = unpacked_state(
                shifted(packed_state(decay, memory), axis, steps), key_width
            )
        else:
            earlier_decay = None
            earlier_memory = shifted(memory.astype(jnp.bfloat16), axis, steps).astype(jnp.float32)
        memory = jnp.where(valid, decay[:, None] * earlier_memory + memory, memory)
        if steps == 1:
            entering = earlier_memory
            entering_decay = earlier_decay
        else:
            entering = jnp.where(valid, entering_decay[:, None] * earlier_memory + entering, entering)
        if earlier_decay is not None:
            decay = jnp.where(valid, earlier_decay * decay, decay)
            if steps > 1:
                entering_decay = jnp.where(valid, earlier_decay * entering_decay, entering_decay)
        steps *= 2
    return (memory, entering)


def rotations(axis):
    count = lax.axis_size(axis)
    return [[(source, (source + step) % count) for source in range(count)] for step in range(1, count)]


def gather_rows(rows, axis):
    count = lax.axis_size(axis)
    place = lax.axis_index(axis)
    if count & (count - 1):
        received = [rows] + [lax.ppermute(rows, axis, pairs) for pairs in rotations(axis)]
        order = [(-step) % count for step in range(count)]
    else:
        received = [rows]
        order = [0]
        mask = count // 2
        while mask >= 1:
            incoming = lax.ppermute(
                jnp.concatenate(received), axis, [(source, source ^ mask) for source in range(count)]
            )
            received = received + list(jnp.split(incoming, len(received)))
            order = order + [flip ^ mask for flip in order]
            mask //= 2

    def ordered(shift):
        if count & (count - 1):
            picks = [order.index((index - shift) % count) for index in range(count)]
        else:
            picks = [order.index(shift ^ index) for index in range(count)]
        return jnp.concatenate([received[pick] for pick in picks])

    return lax.switch(place, [functools.partial(ordered, shift) for shift in range(count)])


def scatter_sum(gated, weight, axis):
    count = lax.axis_size(axis)
    place = lax.axis_index(axis)
    chunk = gated.shape[0] // count

    def term(index):
        rows = lax.slice_in_dim(gated, index * chunk, (index + 1) * chunk, axis=0)
        return jnp.dot(rows, weight, preferred_element_type=jnp.float32).astype(jnp.bfloat16)

    if count & (count - 1):
        chunks = jnp.stack([term(index) for index in range(count)])
        total = lax.dynamic_index_in_dim(chunks, place, 0, False).astype(jnp.float32)
        for step, pairs in enumerate(rotations(axis), start=1):
            outgoing = lax.dynamic_index_in_dim(chunks, (place + step) % count, 0, False)
            total = total + lax.ppermute(outgoing, axis, pairs).astype(jnp.float32)
        return total.astype(jnp.bfloat16)
    held = [term(index) for index in range(count)]
    mask = 1
    while mask < count:
        odd = (place // mask) % 2 == 1
        pairs = list(zip(held[0::2], held[1::2]))
        keep = [jnp.where(odd, high, low) for low, high in pairs]
        outgoing = jnp.stack([jnp.where(odd, low, high).astype(jnp.bfloat16) for low, high in pairs])
        incoming = lax.ppermute(outgoing, axis, [(source, source ^ mask) for source in range(count)])
        held = [
            kept.astype(jnp.float32) + incoming[index].astype(jnp.float32)
            for index, kept in enumerate(keep)
        ]
        mask *= 2
    return held[0].astype(jnp.bfloat16)


def shards(
    tokens,
    prompt_lengths,
    query_weight,
    key_weight,
    value_weight,
    query_conv,
    key_conv,
    value_conv,
    decay_down,
    decay_up,
    decay_bias,
    gate_weight,
    norm_gain,
    out_weight,
):
    gathered = gather_rows(tokens, "hv")

    def project(weight):
        return jnp.dot(gathered, weight, preferred_element_type=jnp.float32).astype(jnp.bfloat16)

    raw_query = project(query_weight)
    raw_key = project(key_weight)
    raw_value = project(value_weight)
    gate_values = project(gate_weight)
    low_rank = project(decay_down)
    row_count = raw_query.shape[0]
    key_width = raw_query.shape[1]
    value_width = raw_value.shape[1]
    positions = lax.axis_index("tok") * row_count + jnp.arange(row_count, dtype=jnp.int32)
    prompt_index = jnp.arange(prompt_lengths.shape[0])
    offsets = jnp.sum(
        jnp.where(prompt_index[None, :] < prompt_index[:, None], prompt_lengths[None, :], 0), axis=1
    )
    prompt_first, starts = prompt_marks(positions, offsets)
    rim_rows = query_conv.shape[0] - 1
    joined = jnp.concatenate([raw_query, raw_key, raw_value], axis=1)
    before_rows = shifted(joined[row_count - rim_rows :], "tok", 1)
    conv_query = short_conv(
        raw_query, before_rows[:, :key_width], query_conv, positions, prompt_first
    )
    conv_key = short_conv(
        raw_key, before_rows[:, key_width : 2 * key_width], key_conv, positions, prompt_first
    )
    conv_value = short_conv(
        raw_value, before_rows[:, 2 * key_width :], value_conv, positions, prompt_first
    )
    decays = (
        jax.nn.log_sigmoid(
            jnp.dot(low_rank, decay_up, preferred_element_type=jnp.float32) + decay_bias
        )
        / 16.0
    )
    local_out, carry_lift, local_memory, local_decay = segment_parts(
        blocked(conv_query), blocked(conv_key), blocked(conv_value), blocked(decays), blocked(starts)
    )
    closing, entering = prefix_states(local_decay, local_memory, "tok")
    heads_out = local_out.reshape((row_count, value_width)) + jnp.dot(
        carry_lift.reshape((row_count, key_width)), entering, precision=HIGH_PRECISION
    )
    gate_float = gate_values.astype(jnp.float32)
    rescale = lax.rsqrt(jnp.mean(heads_out * heads_out, axis=1, keepdims=True) + 1e-05)
    gated_out = (
        heads_out * rescale * norm_gain[None, :] * gate_float * jax.nn.sigmoid(gate_float)
    ).astype(jnp.bfloat16)
    mixed = scatter_sum(gated_out, out_weight, "hv")
    segment_states = closing[None, None]
    in_prompt = positions[row_count - rim_rows :] >= prompt_first[row_count - 1]
    tail_rows = joined[row_count - rim_rows :]
    conv_edges = jnp.where(in_prompt[:, None], tail_rows, jnp.zeros_like(tail_rows))
    conv_edges = conv_edges.reshape((1, rim_rows, 1, joined.shape[1]))
    return (mixed, segment_states, conv_edges)


def solution(mesh):
    in_specs = (
        P(("tok", "hv"), None),
        P(),
        P(None, "hv"),
        P(None, "hv"),
        P(None, "hv"),
        P(None, "hv"),
        P(None, "hv"),
        P(None, "hv"),
        P(),
        P(None, "hv"),
        P("hv"),
        P(None, "hv"),
        P(),
        P("hv", None),
    )
    out_specs = (P(("tok", "hv"), None), P("tok", "hv", None, None), P("tok", None, "hv", None))
    return jax.shard_map(shards, mesh=mesh, in_specs=in_specs, out_specs=out_specs, check_vma=False)
```

```python
import functools

import jax
import jax.numpy as jnp
from jax import lax
from jax.sharding import PartitionSpec as P

SPAN = 64


HIGH_PRECISION = lax.Precision.HIGH


def shifted(value, axis, steps):
    count = lax.axis_size(axis)
    initial, last = (max(0, -steps), min(count, count - steps))
    return lax.ppermute(value, axis, [(source, source + steps) for source in range(initial, last)])


def prompt_marks(positions, offsets):
    before = offsets[None, :] <= positions[:, None]
    prompt_first = jnp.max(jnp.where(before, offsets[None, :], 0), axis=1)
    return (prompt_first, (prompt_first == positions).astype(jnp.float32))


def short_conv(raw_rows, before_rows, weight, positions, prompt_first):
    tap_count = weight.shape[0]
    row_count = raw_rows.shape[0]
    extended = jnp.concatenate([before_rows, raw_rows], axis=0)
    lags = tap_count - 1 - jnp.arange(tap_count)
    inside_prompt = (positions[None, :] - lags[:, None] >= prompt_first[None, :]).astype(jnp.float32)
    windows = jnp.stack(
        [lax.slice_in_dim(extended, tap, tap + row_count, axis=0) for tap in range(tap_count)]
    )
    summed = jnp.sum(
        weight.astype(jnp.float32)[:, None, :]
        * windows.astype(jnp.float32)
        * inside_prompt[:, :, None],
        axis=0,
    )
    return jax.nn.silu(summed).astype(jnp.bfloat16)


def blocked(array_in):
    return array_in.reshape((array_in.shape[0] // SPAN, SPAN) + array_in.shape[1:])


def segment_parts(queries, head_keys, head_values, decays, starts):
    cumulative = jnp.cumsum(decays, axis=1)
    groups = jnp.cumsum(starts, axis=1)
    intact = (groups == 0.0).astype(jnp.float32)
    final_log = cumulative[:, -1]
    in_tail = (groups == groups[:, -1:]).astype(jnp.float32)
    weighted = (
        head_keys.astype(jnp.float32)
        * jnp.exp(final_log[:, None, :] - cumulative)
        * in_tail[:, :, None]
    ).astype(jnp.bfloat16)
    update = jnp.einsum("bsk,bsv->bkv", weighted, head_values, preferred_element_type=jnp.float32)
    step_decay = jnp.exp(final_log) * intact[:, -1:]
    index_rows = jnp.arange(queries.shape[1])
    allowed = (groups[:, :, None] == groups[:, None, :]) & (
        index_rows[None, :, None] >= index_rows[None, None, :]
    )
    lifted = queries.astype(jnp.float32) * jnp.exp(cumulative)
    lowered = (head_keys.astype(jnp.float32) * jnp.exp(-cumulative)).astype(jnp.bfloat16)
    raw_scores = jnp.einsum(
        "bak,bck->bac", lifted.astype(jnp.bfloat16), lowered, preferred_element_type=jnp.float32
    )
    scores = jnp.where(allowed, raw_scores, 0.0).astype(jnp.bfloat16)
    inside = jnp.einsum("bac,bcv->bav", scores, head_values, preferred_element_type=jnp.float32)
    lifted_intact = lifted * intact[:, :, None]
    block_count = queries.shape[0]
    memory = jnp.zeros(update.shape[1:], jnp.float32)
    product = jnp.ones(step_decay.shape[1:], jnp.float32)
    local_outs = [jnp.zeros(inside.shape[1:], jnp.float32)]
    products = [product]
    for block in range(block_count):
        if block > 0:
            local_outs.append(jnp.dot(lifted_intact[block], memory, precision=HIGH_PRECISION))
            products.append(product)
        memory = step_decay[block][:, None] * memory + update[block]
        product = product * step_decay[block]
    local_out = inside + jnp.stack(local_outs)
    carry_lift = lifted_intact * jnp.stack(products)[:, None, :]
    return (local_out, carry_lift, memory, product)


def packed_state(decay, memory):
    high = decay.astype(jnp.bfloat16)
    low = (decay - high.astype(jnp.float32)).astype(jnp.bfloat16)
    width = memory.shape[1]
    flat = jnp.concatenate([high, low])
    flat = jnp.pad(flat, (0, -flat.shape[0] % width))
    return jnp.concatenate([memory.astype(jnp.bfloat16), flat.reshape((-1, width))], axis=0)


def unpacked_state(packed, key_width):
    memory = packed[:key_width].astype(jnp.float32)
    flat = packed[key_width:].reshape((-1,)).astype(jnp.float32)
    return (flat[:key_width] + flat[key_width : 2 * key_width], memory)


def prefix_states(decay, memory, axis):
    count = lax.axis_size(axis)
    place = lax.axis_index(axis)
    key_width = memory.shape[0]
    entering_decay = jnp.ones_like(decay)
    entering = jnp.zeros_like(memory)
    steps = 1
    while steps < count:
        valid = place >= steps
        if steps * 2 < count:
            earlier_decay, earlier_memory = unpacked_state(
                shifted(packed_state(decay, memory), axis, steps), key_width
            )
        else:
            earlier_decay = None
            earlier_memory = shifted(memory.astype(jnp.bfloat16), axis, steps).astype(jnp.float32)
        memory = jnp.where(valid, decay[:, None] * earlier_memory + memory, memory)
        if steps == 1:
            entering = earlier_memory
            entering_decay = earlier_decay
        else:
            entering = jnp.where(valid, entering_decay[:, None] * earlier_memory + entering, entering)
        if earlier_decay is not None:
            decay = jnp.where(valid, earlier_decay * decay, decay)
            if steps > 1:
                entering_decay = jnp.where(valid, earlier_decay * entering_decay, entering_decay)
        steps *= 2
    return (memory, entering)


def rotations(axis):
    count = lax.axis_size(axis)
    return [[(source, (source + step) % count) for source in range(count)] for step in range(1, count)]


def gather_rows(rows, axis):
    count = lax.axis_size(axis)
    place = lax.axis_index(axis)
    if count & (count - 1):
        received = [rows] + [lax.ppermute(rows, axis, pairs) for pairs in rotations(axis)]
        order = [(-step) % count for step in range(count)]
    else:
        received = [rows]
        order = [0]
        mask = count // 2
        while mask >= 1:
            incoming = lax.ppermute(
                jnp.concatenate(received), axis, [(source, source ^ mask) for source in range(count)]
            )
            received = received + list(jnp.split(incoming, len(received)))
            order = order + [flip ^ mask for flip in order]
            mask //= 2

    def ordered(shift):
        if count & (count - 1):
            picks = [order.index((index - shift) % count) for index in range(count)]
        else:
            picks = [order.index(shift ^ index) for index in range(count)]
        return jnp.concatenate([received[pick] for pick in picks])

    return lax.switch(place, [functools.partial(ordered, shift) for shift in range(count)])


def scatter_sum(gated, weight, axis):
    count = lax.axis_size(axis)
    place = lax.axis_index(axis)
    chunk = gated.shape[0] // count

    def term(index):
        rows = lax.slice_in_dim(gated, index * chunk, (index + 1) * chunk, axis=0)
        return jnp.dot(rows, weight, preferred_element_type=jnp.float32).astype(jnp.bfloat16)

    if count & (count - 1):
        chunks = jnp.stack([term(index) for index in range(count)])
        total = lax.dynamic_index_in_dim(chunks, place, 0, False).astype(jnp.float32)
        for step, pairs in enumerate(rotations(axis), start=1):
            outgoing = lax.dynamic_index_in_dim(chunks, (place + step) % count, 0, False)
            total = total + lax.ppermute(outgoing, axis, pairs).astype(jnp.float32)
        return total.astype(jnp.bfloat16)
    held = [lax.slice_in_dim(gated, index * chunk, (index + 1) * chunk, axis=0) for index in range(count)]
    odd = place % 2 == 1
    pairs = list(zip(held[0::2], held[1::2]))
    outgoing = jnp.concatenate([jnp.where(odd, low, high) for low, high in pairs])
    outgoing = jnp.dot(outgoing, weight, preferred_element_type=jnp.float32).astype(jnp.bfloat16)
    incoming = lax.ppermute(outgoing, axis, [(source, source ^ 1) for source in range(count)])
    kept = jnp.concatenate([jnp.where(odd, high, low) for low, high in pairs])
    kept = jnp.dot(kept, weight, preferred_element_type=jnp.float32).astype(jnp.bfloat16)
    summed = kept.astype(jnp.float32) + incoming.astype(jnp.float32)
    held = list(jnp.split(summed, len(pairs)))
    mask = 2
    while mask < count:
        odd = (place // mask) % 2 == 1
        pairs = list(zip(held[0::2], held[1::2]))
        keep = [jnp.where(odd, high, low) for low, high in pairs]
        outgoing = jnp.stack([jnp.where(odd, low, high).astype(jnp.bfloat16) for low, high in pairs])
        incoming = lax.ppermute(outgoing, axis, [(source, source ^ mask) for source in range(count)])
        held = [
            kept.astype(jnp.float32) + incoming[index].astype(jnp.float32)
            for index, kept in enumerate(keep)
        ]
        mask *= 2
    return held[0].astype(jnp.bfloat16)


def shards(
    tokens,
    prompt_lengths,
    query_weight,
    key_weight,
    value_weight,
    query_conv,
    key_conv,
    value_conv,
    decay_down,
    decay_up,
    decay_bias,
    gate_weight,
    norm_gain,
    out_weight,
):
    gathered = gather_rows(tokens, "hv")

    def project(weight):
        return jnp.dot(gathered, weight, preferred_element_type=jnp.float32).astype(jnp.bfloat16)

    raw_query = project(query_weight)
    raw_key = project(key_weight)
    raw_value = project(value_weight)
    gate_values = project(gate_weight)
    low_rank = project(decay_down)
    row_count = raw_query.shape[0]
    key_width = raw_query.shape[1]
    value_width = raw_value.shape[1]
    positions = lax.axis_index("tok") * row_count + jnp.arange(row_count, dtype=jnp.int32)
    prompt_index = jnp.arange(prompt_lengths.shape[0])
    offsets = jnp.sum(
        jnp.where(prompt_index[None, :] < prompt_index[:, None], prompt_lengths[None, :], 0), axis=1
    )
    prompt_first, starts = prompt_marks(positions, offsets)
    rim_rows = query_conv.shape[0] - 1
    joined = jnp.concatenate([raw_query, raw_key, raw_value], axis=1)
    before_rows = shifted(joined[row_count - rim_rows :], "tok", 1)
    conv_all = short_conv(
        joined,
        before_rows,
        jnp.concatenate([query_conv, key_conv, value_conv], axis=1),
        positions,
        prompt_first,
    )
    conv_query = conv_all[:, :key_width]
    conv_key = conv_all[:, key_width : 2 * key_width]
    conv_value = conv_all[:, 2 * key_width :]
    decays = (
        jax.nn.log_sigmoid(
            jnp.dot(low_rank, decay_up, preferred_element_type=jnp.float32) + decay_bias
        )
        / 16.0
    )
    local_out, carry_lift, local_memory, local_decay = segment_parts(
        blocked(conv_query), blocked(conv_key), blocked(conv_value), blocked(decays), blocked(starts)
    )
    closing, entering = prefix_states(local_decay, local_memory, "tok")
    heads_out = local_out.reshape((row_count, value_width)) + jnp.dot(
        carry_lift.reshape((row_count, key_width)), entering, precision=HIGH_PRECISION
    )
    gate_float = gate_values.astype(jnp.float32)
    rescale = lax.rsqrt(jnp.mean(heads_out * heads_out, axis=1, keepdims=True) + 1e-05)
    gated_out = (
        heads_out * rescale * norm_gain[None, :] * gate_float * jax.nn.sigmoid(gate_float)
    ).astype(jnp.bfloat16)
    mixed = scatter_sum(gated_out, out_weight, "hv")
    segment_states = closing[None, None]
    in_prompt = positions[row_count - rim_rows :] >= prompt_first[row_count - 1]
    tail_rows = joined[row_count - rim_rows :]
    conv_edges = jnp.where(in_prompt[:, None], tail_rows, jnp.zeros_like(tail_rows))
    conv_edges = conv_edges.reshape((1, rim_rows, 1, joined.shape[1]))
    return (mixed, segment_states, conv_edges)


def solution(mesh):
    in_specs = (
        P(("tok", "hv"), None),
        P(),
        P(None, "hv"),
        P(None, "hv"),
        P(None, "hv"),
        P(None, "hv"),
        P(None, "hv"),
        P(None, "hv"),
        P(),
        P(None, "hv"),
        P("hv"),
        P(None, "hv"),
        P(),
        P("hv", None),
    )
    out_specs = (P(("tok", "hv"), None), P("tok", "hv", None, None), P("tok", None, "hv", None))
    return jax.shard_map(shards, mesh=mesh, in_specs=in_specs, out_specs=out_specs, check_vma=False)
```

```python
import functools

import jax
import jax.numpy as jnp
from jax import lax
from jax.sharding import PartitionSpec as P

SPAN = 64


HIGH_PRECISION = lax.Precision.HIGH


def shifted(value, axis, steps):
    count = lax.axis_size(axis)
    initial, last = (max(0, -steps), min(count, count - steps))
    return lax.ppermute(value, axis, [(source, source + steps) for source in range(initial, last)])


def prompt_marks(positions, offsets):
    before = offsets[None, :] <= positions[:, None]
    prompt_first = jnp.max(jnp.where(before, offsets[None, :], 0), axis=1)
    return (prompt_first, (prompt_first == positions).astype(jnp.float32))


def short_conv(raw_rows, before_rows, weight, positions, prompt_first):
    tap_count = weight.shape[0]
    row_count = raw_rows.shape[0]
    extended = jnp.concatenate([before_rows, raw_rows], axis=0)
    lags = tap_count - 1 - jnp.arange(tap_count)
    inside_prompt = (positions[None, :] - lags[:, None] >= prompt_first[None, :]).astype(jnp.float32)
    windows = jnp.stack(
        [lax.slice_in_dim(extended, tap, tap + row_count, axis=0) for tap in range(tap_count)]
    )
    summed = jnp.sum(
        weight.astype(jnp.float32)[:, None, :]
        * windows.astype(jnp.float32)
        * inside_prompt[:, :, None],
        axis=0,
    )
    return jax.nn.silu(summed).astype(jnp.bfloat16)


def blocked(array_in):
    return array_in.reshape((array_in.shape[0] // SPAN, SPAN) + array_in.shape[1:])


def segment_parts(queries, head_keys, head_values, decays, starts):
    cumulative = jnp.cumsum(decays, axis=1)
    groups = jnp.cumsum(starts, axis=1)
    intact = (groups == 0.0).astype(jnp.float32)
    final_log = cumulative[:, -1]
    in_tail = (groups == groups[:, -1:]).astype(jnp.float32)
    weighted = (
        head_keys.astype(jnp.float32)
        * jnp.exp(final_log[:, None, :] - cumulative)
        * in_tail[:, :, None]
    ).astype(jnp.bfloat16)
    update = jnp.einsum("bsk,bsv->bkv", weighted, head_values, preferred_element_type=jnp.float32)
    step_decay = jnp.exp(final_log) * intact[:, -1:]
    index_rows = jnp.arange(queries.shape[1])
    allowed = (groups[:, :, None] == groups[:, None, :]) & (
        index_rows[None, :, None] >= index_rows[None, None, :]
    )
    lifted = queries.astype(jnp.float32) * jnp.exp(cumulative)
    lowered = (head_keys.astype(jnp.float32) * jnp.exp(-cumulative)).astype(jnp.bfloat16)
    raw_scores = jnp.einsum(
        "bak,bck->bac", lifted.astype(jnp.bfloat16), lowered, preferred_element_type=jnp.float32
    )
    scores = jnp.where(allowed, raw_scores, 0.0).astype(jnp.bfloat16)
    inside = jnp.einsum("bac,bcv->bav", scores, head_values, preferred_element_type=jnp.float32)
    lifted_intact = lifted * intact[:, :, None]
    block_count = queries.shape[0]
    memory = jnp.zeros(update.shape[1:], jnp.float32)
    product = jnp.ones(step_decay.shape[1:], jnp.float32)
    local_outs = [jnp.zeros(inside.shape[1:], jnp.float32)]
    products = [product]
    for block in range(block_count):
        if block > 0:
            local_outs.append(jnp.dot(lifted_intact[block], memory, precision=HIGH_PRECISION))
            products.append(product)
        memory = step_decay[block][:, None] * memory + update[block]
        product = product * step_decay[block]
    local_out = inside + jnp.stack(local_outs)
    carry_lift = lifted_intact * jnp.stack(products)[:, None, :]
    return (local_out, carry_lift, memory, product)


def packed_state(decay, memory):
    high = decay.astype(jnp.bfloat16)
    low = (decay - high.astype(jnp.float32)).astype(jnp.bfloat16)
    width = memory.shape[1]
    flat = jnp.concatenate([high, low])
    flat = jnp.pad(flat, (0, -flat.shape[0] % width))
    return jnp.concatenate([memory.astype(jnp.bfloat16), flat.reshape((-1, width))], axis=0)


def unpacked_state(packed, key_width):
    memory = packed[:key_width].astype(jnp.float32)
    flat = packed[key_width:].reshape((-1,)).astype(jnp.float32)
    return (flat[:key_width] + flat[key_width : 2 * key_width], memory)


def prefix_states(decay, memory, axis):
    count = lax.axis_size(axis)
    place = lax.axis_index(axis)
    key_width = memory.shape[0]
    entering_decay = jnp.ones_like(decay)
    entering = jnp.zeros_like(memory)
    steps = 1
    while steps < count:
        valid = place >= steps
        if steps * 2 < count:
            earlier_decay, earlier_memory = unpacked_state(
                shifted(packed_state(decay, memory), axis, steps), key_width
            )
        else:
            earlier_decay = None
            earlier_memory = shifted(memory.astype(jnp.bfloat16), axis, steps).astype(jnp.float32)
        memory = jnp.where(valid, decay[:, None] * earlier_memory + memory, memory)
        if steps == 1:
            entering = earlier_memory
            entering_decay = earlier_decay
        else:
            entering = jnp.where(valid, entering_decay[:, None] * earlier_memory + entering, entering)
        if earlier_decay is not None:
            decay = jnp.where(valid, earlier_decay * decay, decay)
            if steps > 1:
                entering_decay = jnp.where(valid, earlier_decay * entering_decay, entering_decay)
        steps *= 2
    return (memory, entering)


def rotations(axis):
    count = lax.axis_size(axis)
    return [[(source, (source + step) % count) for source in range(count)] for step in range(1, count)]


def gather_rows(rows, axis):
    count = lax.axis_size(axis)
    place = lax.axis_index(axis)
    if count & (count - 1):
        received = [rows] + [lax.ppermute(rows, axis, pairs) for pairs in rotations(axis)]
        order = [(-step) % count for step in range(count)]
    else:
        received = [rows]
        order = [0]
        mask = count // 2
        while mask >= 1:
            incoming = lax.ppermute(
                jnp.concatenate(received), axis, [(source, source ^ mask) for source in range(count)]
            )
            received = received + list(jnp.split(incoming, len(received)))
            order = order + [flip ^ mask for flip in order]
            mask //= 2

    def ordered(shift):
        if count & (count - 1):
            picks = [order.index((index - shift) % count) for index in range(count)]
        else:
            picks = [order.index(shift ^ index) for index in range(count)]
        return jnp.concatenate([received[pick] for pick in picks])

    return lax.switch(place, [functools.partial(ordered, shift) for shift in range(count)])


def scatter_sum(gated, weight, axis):
    count = lax.axis_size(axis)
    place = lax.axis_index(axis)
    chunk = gated.shape[0] // count

    def term(index):
        rows = lax.slice_in_dim(gated, index * chunk, (index + 1) * chunk, axis=0)
        return jnp.dot(rows, weight, preferred_element_type=jnp.float32).astype(jnp.bfloat16)

    if count & (count - 1):
        chunks = jnp.stack([term(index) for index in range(count)])
        total = lax.dynamic_index_in_dim(chunks, place, 0, False).astype(jnp.float32)
        for step, pairs in enumerate(rotations(axis), start=1):
            outgoing = lax.dynamic_index_in_dim(chunks, (place + step) % count, 0, False)
            total = total + lax.ppermute(outgoing, axis, pairs).astype(jnp.float32)
        return total.astype(jnp.bfloat16)
    held = [lax.slice_in_dim(gated, index * chunk, (index + 1) * chunk, axis=0) for index in range(count)]
    odd = place % 2 == 1
    pairs = list(zip(held[0::2], held[1::2]))
    outgoing = jnp.concatenate([jnp.where(odd, low, high) for low, high in pairs])
    outgoing = jnp.dot(outgoing, weight, preferred_element_type=jnp.float32).astype(jnp.bfloat16)
    incoming = lax.ppermute(outgoing, axis, [(source, source ^ 1) for source in range(count)])
    kept = jnp.concatenate([jnp.where(odd, high, low) for low, high in pairs])
    kept = jnp.dot(kept, weight, preferred_element_type=jnp.float32).astype(jnp.bfloat16)
    summed = kept.astype(jnp.float32) + incoming.astype(jnp.float32)
    held = list(jnp.split(summed, len(pairs)))
    mask = 2
    while mask < count:
        odd = (place // mask) % 2 == 1
        pairs = list(zip(held[0::2], held[1::2]))
        keep = [jnp.where(odd, high, low) for low, high in pairs]
        outgoing = jnp.stack([jnp.where(odd, low, high).astype(jnp.bfloat16) for low, high in pairs])
        incoming = lax.ppermute(outgoing, axis, [(source, source ^ mask) for source in range(count)])
        held = [
            kept.astype(jnp.float32) + incoming[index].astype(jnp.float32)
            for index, kept in enumerate(keep)
        ]
        mask *= 2
    return held[0].astype(jnp.bfloat16)


def shards(
    tokens,
    prompt_lengths,
    query_weight,
    key_weight,
    value_weight,
    query_conv,
    key_conv,
    value_conv,
    decay_down,
    decay_up,
    decay_bias,
    gate_weight,
    norm_gain,
    out_weight,
):
    gathered = gather_rows(tokens, "hv")

    def project(weight):
        return jnp.dot(gathered, weight, preferred_element_type=jnp.float32).astype(jnp.bfloat16)

    raw_query = project(query_weight)
    raw_key = project(key_weight)
    raw_value = project(value_weight)
    gate_values = project(gate_weight)
    low_rank = project(decay_down)
    row_count = raw_query.shape[0]
    key_width = raw_query.shape[1]
    value_width = raw_value.shape[1]
    positions = lax.axis_index("tok") * row_count + jnp.arange(row_count, dtype=jnp.int32)
    prompt_index = jnp.arange(prompt_lengths.shape[0])
    offsets = jnp.sum(
        jnp.where(prompt_index[None, :] < prompt_index[:, None], prompt_lengths[None, :], 0), axis=1
    )
    prompt_first, starts = prompt_marks(positions, offsets)
    rim_rows = query_conv.shape[0] - 1
    joined = jnp.concatenate([raw_query, raw_key, raw_value], axis=1)
    before_rows = shifted(joined[row_count - rim_rows :], "tok", 1)
    conv_query = short_conv(
        raw_query, before_rows[:, :key_width], query_conv, positions, prompt_first
    )
    conv_key = short_conv(
        raw_key, before_rows[:, key_width : 2 * key_width], key_conv, positions, prompt_first
    )
    conv_value = short_conv(
        raw_value, before_rows[:, 2 * key_width :], value_conv, positions, prompt_first
    )
    decays = (
        jax.nn.log_sigmoid(
            jnp.dot(low_rank, decay_up, preferred_element_type=jnp.float32) + decay_bias
        )
        / 16.0
    )
    local_out, carry_lift, local_memory, local_decay = segment_parts(
        blocked(conv_query), blocked(conv_key), blocked(conv_value), blocked(decays), blocked(starts)
    )
    closing, entering = prefix_states(local_decay, local_memory, "tok")
    heads_out = local_out.reshape((row_count, value_width)) + jnp.dot(
        carry_lift.reshape((row_count, key_width)), entering, precision=HIGH_PRECISION
    )
    gate_float = gate_values.astype(jnp.float32)
    rescale = lax.rsqrt(jnp.mean(heads_out * heads_out, axis=1, keepdims=True) + 1e-05)
    gated_out = (
        heads_out * rescale * norm_gain[None, :] * gate_float * jax.nn.sigmoid(gate_float)
    ).astype(jnp.bfloat16)
    mixed = scatter_sum(gated_out, out_weight, "hv")
    segment_states = closing[None, None]
    in_prompt = positions[row_count - rim_rows :] >= prompt_first[row_count - 1]
    tail_rows = joined[row_count - rim_rows :]
    conv_edges = jnp.where(in_prompt[:, None], tail_rows, jnp.zeros_like(tail_rows))
    conv_edges = conv_edges.reshape((1, rim_rows, 1, joined.shape[1]))
    return (mixed, segment_states, conv_edges)


def solution(mesh):
    in_specs = (
        P(("tok", "hv"), None),
        P(),
        P(None, "hv"),
        P(None, "hv"),
        P(None, "hv"),
        P(None, "hv"),
        P(None, "hv"),
        P(None, "hv"),
        P(),
        P(None, "hv"),
        P("hv"),
        P(None, "hv"),
        P(),
        P("hv", None),
    )
    out_specs = (P(("tok", "hv"), None), P("tok", "hv", None, None), P("tok", None, "hv", None))
    return jax.shard_map(shards, mesh=mesh, in_specs=in_specs, out_specs=out_specs, check_vma=False)
```

```python
import functools

import jax
import jax.numpy as jnp
from jax import lax
from jax.sharding import PartitionSpec as P

SPAN = 64


HIGH_PRECISION = lax.Precision.HIGH


def shifted(value, axis, steps):
    count = lax.axis_size(axis)
    initial, last = (max(0, -steps), min(count, count - steps))
    return lax.ppermute(value, axis, [(source, source + steps) for source in range(initial, last)])


def prompt_marks(positions, offsets):
    before = offsets[None, :] <= positions[:, None]
    prompt_first = jnp.max(jnp.where(before, offsets[None, :], 0), axis=1)
    return (prompt_first, (prompt_first == positions).astype(jnp.float32))


def short_conv(raw_rows, before_rows, weight, positions, prompt_first):
    tap_count = weight.shape[0]
    row_count = raw_rows.shape[0]
    extended = jnp.concatenate([before_rows, raw_rows], axis=0)
    lags = tap_count - 1 - jnp.arange(tap_count)
    inside_prompt = (positions[None, :] - lags[:, None] >= prompt_first[None, :]).astype(jnp.float32)
    windows = jnp.stack(
        [lax.slice_in_dim(extended, tap, tap + row_count, axis=0) for tap in range(tap_count)]
    )
    summed = jnp.sum(
        weight.astype(jnp.float32)[:, None, :]
        * windows.astype(jnp.float32)
        * inside_prompt[:, :, None],
        axis=0,
    )
    return jax.nn.silu(summed).astype(jnp.bfloat16)


def blocked(array_in):
    return array_in.reshape((array_in.shape[0] // SPAN, SPAN) + array_in.shape[1:])


def segment_parts(queries, head_keys, head_values, decays, starts):
    cumulative = jnp.cumsum(decays, axis=1)
    groups = jnp.cumsum(starts, axis=1)
    intact = (groups == 0.0).astype(jnp.float32)
    final_log = cumulative[:, -1]
    in_tail = (groups == groups[:, -1:]).astype(jnp.float32)
    weighted = (
        head_keys.astype(jnp.float32)
        * jnp.exp(final_log[:, None, :] - cumulative)
        * in_tail[:, :, None]
    ).astype(jnp.bfloat16)
    update = jnp.einsum("bsk,bsv->bkv", weighted, head_values, preferred_element_type=jnp.float32)
    step_decay = jnp.exp(final_log) * intact[:, -1:]
    index_rows = jnp.arange(queries.shape[1])
    allowed = (groups[:, :, None] == groups[:, None, :]) & (
        index_rows[None, :, None] >= index_rows[None, None, :]
    )
    lifted = queries.astype(jnp.float32) * jnp.exp(cumulative)
    lowered = (head_keys.astype(jnp.float32) * jnp.exp(-cumulative)).astype(jnp.bfloat16)
    raw_scores = jnp.einsum(
        "bak,bck->bac", lifted.astype(jnp.bfloat16), lowered, preferred_element_type=jnp.float32
    )
    scores = jnp.where(allowed, raw_scores, 0.0).astype(jnp.bfloat16)
    inside = jnp.einsum("bac,bcv->bav", scores, head_values, preferred_element_type=jnp.float32)
    lifted_intact = lifted * intact[:, :, None]
    block_count = queries.shape[0]
    memory = jnp.zeros(update.shape[1:], jnp.float32)
    product = jnp.ones(step_decay.shape[1:], jnp.float32)
    local_outs = [jnp.zeros(inside.shape[1:], jnp.float32)]
    products = [product]
    for block in range(block_count):
        if block > 0:
            local_outs.append(jnp.dot(lifted_intact[block], memory, precision=HIGH_PRECISION))
            products.append(product)
        memory = step_decay[block][:, None] * memory + update[block]
        product = product * step_decay[block]
    local_out = inside + jnp.stack(local_outs)
    carry_lift = lifted_intact * jnp.stack(products)[:, None, :]
    return (local_out, carry_lift, memory, product)


def packed_state(decay, memory):
    high = decay.astype(jnp.bfloat16)
    low = (decay - high.astype(jnp.float32)).astype(jnp.bfloat16)
    width = memory.shape[1]
    flat = jnp.concatenate([high, low])
    flat = jnp.pad(flat, (0, -flat.shape[0] % width))
    return jnp.concatenate([memory.astype(jnp.bfloat16), flat.reshape((-1, width))], axis=0)


def unpacked_state(packed, key_width):
    memory = packed[:key_width].astype(jnp.float32)
    flat = packed[key_width:].reshape((-1,)).astype(jnp.float32)
    return (flat[:key_width] + flat[key_width : 2 * key_width], memory)


def prefix_states(decay, memory, axis):
    count = lax.axis_size(axis)
    place = lax.axis_index(axis)
    key_width = memory.shape[0]
    entering_decay = jnp.ones_like(decay)
    entering = jnp.zeros_like(memory)
    steps = 1
    while steps < count:
        valid = place >= steps
        if steps * 2 < count:
            earlier_decay, earlier_memory = unpacked_state(
                shifted(packed_state(decay, memory), axis, steps), key_width
            )
        else:
            earlier_decay = None
            earlier_memory = shifted(memory.astype(jnp.bfloat16), axis, steps).astype(jnp.float32)
        memory = jnp.where(valid, decay[:, None] * earlier_memory + memory, memory)
        if steps == 1:
            entering = earlier_memory
            entering_decay = earlier_decay
        else:
            entering = jnp.where(valid, entering_decay[:, None] * earlier_memory + entering, entering)
        if earlier_decay is not None:
            decay = jnp.where(valid, earlier_decay * decay, decay)
            if steps > 1:
                entering_decay = jnp.where(valid, earlier_decay * entering_decay, entering_decay)
        steps *= 2
    return (memory, entering)


def rotations(axis):
    count = lax.axis_size(axis)
    return [[(source, (source + step) % count) for source in range(count)] for step in range(1, count)]


def gather_rows(rows, axis):
    count = lax.axis_size(axis)
    place = lax.axis_index(axis)
    if count & (count - 1):
        received = [rows] + [lax.ppermute(rows, axis, pairs) for pairs in rotations(axis)]
        order = [(-step) % count for step in range(count)]
    else:
        received = [rows]
        order = [0]
        mask = count // 2
        while mask >= 1:
            pairs = [(source, source ^ mask) for source in range(count)]
            received = received + [lax.ppermute(block, axis, pairs) for block in received]
            order = order + [flip ^ mask for flip in order]
            mask //= 2

    def ordered(shift):
        if count & (count - 1):
            picks = [order.index((index - shift) % count) for index in range(count)]
        else:
            picks = [order.index(shift ^ index) for index in range(count)]
        return jnp.concatenate([received[pick] for pick in picks])

    return lax.switch(place, [functools.partial(ordered, shift) for shift in range(count)])


def scatter_sum(gated, weight, axis):
    count = lax.axis_size(axis)
    place = lax.axis_index(axis)
    chunk = gated.shape[0] // count

    def term(index):
        rows = lax.slice_in_dim(gated, index * chunk, (index + 1) * chunk, axis=0)
        return jnp.dot(rows, weight, preferred_element_type=jnp.float32).astype(jnp.bfloat16)

    if count & (count - 1):
        chunks = jnp.stack([term(index) for index in range(count)])
        total = lax.dynamic_index_in_dim(chunks, place, 0, False).astype(jnp.float32)
        for step, pairs in enumerate(rotations(axis), start=1):
            outgoing = lax.dynamic_index_in_dim(chunks, (place + step) % count, 0, False)
            total = total + lax.ppermute(outgoing, axis, pairs).astype(jnp.float32)
        return total.astype(jnp.bfloat16)
    held = [lax.slice_in_dim(gated, index * chunk, (index + 1) * chunk, axis=0) for index in range(count)]
    odd = place % 2 == 1
    pairs = list(zip(held[0::2], held[1::2]))
    outgoing = jnp.concatenate([jnp.where(odd, low, high) for low, high in pairs])
    outgoing = jnp.dot(outgoing, weight, preferred_element_type=jnp.float32).astype(jnp.bfloat16)
    incoming = lax.ppermute(outgoing, axis, [(source, source ^ 1) for source in range(count)])
    kept = jnp.concatenate([jnp.where(odd, high, low) for low, high in pairs])
    kept = jnp.dot(kept, weight, preferred_element_type=jnp.float32).astype(jnp.bfloat16)
    summed = kept.astype(jnp.float32) + incoming.astype(jnp.float32)
    held = list(jnp.split(summed, len(pairs)))
    mask = 2
    while mask < count:
        odd = (place // mask) % 2 == 1
        pairs = list(zip(held[0::2], held[1::2]))
        keep = [jnp.where(odd, high, low) for low, high in pairs]
        outgoing = jnp.stack([jnp.where(odd, low, high).astype(jnp.bfloat16) for low, high in pairs])
        incoming = lax.ppermute(outgoing, axis, [(source, source ^ mask) for source in range(count)])
        held = [
            kept.astype(jnp.float32) + incoming[index].astype(jnp.float32)
            for index, kept in enumerate(keep)
        ]
        mask *= 2
    return held[0].astype(jnp.bfloat16)


def shards(
    tokens,
    prompt_lengths,
    query_weight,
    key_weight,
    value_weight,
    query_conv,
    key_conv,
    value_conv,
    decay_down,
    decay_up,
    decay_bias,
    gate_weight,
    norm_gain,
    out_weight,
):
    gathered = gather_rows(tokens, "hv")

    def project(weight):
        return jnp.dot(gathered, weight, preferred_element_type=jnp.float32).astype(jnp.bfloat16)

    raw_query = project(query_weight)
    raw_key = project(key_weight)
    raw_value = project(value_weight)
    gate_values = project(gate_weight)
    low_rank = project(decay_down)
    row_count = raw_query.shape[0]
    key_width = raw_query.shape[1]
    value_width = raw_value.shape[1]
    positions = lax.axis_index("tok") * row_count + jnp.arange(row_count, dtype=jnp.int32)
    prompt_index = jnp.arange(prompt_lengths.shape[0])
    offsets = jnp.sum(
        jnp.where(prompt_index[None, :] < prompt_index[:, None], prompt_lengths[None, :], 0), axis=1
    )
    prompt_first, starts = prompt_marks(positions, offsets)
    rim_rows = query_conv.shape[0] - 1
    joined = jnp.concatenate([raw_query, raw_key, raw_value], axis=1)
    before_rows = shifted(joined[row_count - rim_rows :], "tok", 1)
    conv_query = short_conv(
        raw_query, before_rows[:, :key_width], query_conv, positions, prompt_first
    )
    conv_key = short_conv(
        raw_key, before_rows[:, key_width : 2 * key_width], key_conv, positions, prompt_first
    )
    conv_value = short_conv(
        raw_value, before_rows[:, 2 * key_width :], value_conv, positions, prompt_first
    )
    decays = (
        jax.nn.log_sigmoid(
            jnp.dot(low_rank, decay_up, preferred_element_type=jnp.float32) + decay_bias
        )
        / 16.0
    )
    local_out, carry_lift, local_memory, local_decay = segment_parts(
        blocked(conv_query), blocked(conv_key), blocked(conv_value), blocked(decays), blocked(starts)
    )
    closing, entering = prefix_states(local_decay, local_memory, "tok")
    heads_out = local_out.reshape((row_count, value_width)) + jnp.dot(
        carry_lift.reshape((row_count, key_width)), entering, precision=HIGH_PRECISION
    )
    gate_float = gate_values.astype(jnp.float32)
    rescale = lax.rsqrt(jnp.mean(heads_out * heads_out, axis=1, keepdims=True) + 1e-05)
    gated_out = (
        heads_out * rescale * norm_gain[None, :] * gate_float * jax.nn.sigmoid(gate_float)
    ).astype(jnp.bfloat16)
    mixed = scatter_sum(gated_out, out_weight, "hv")
    segment_states = closing[None, None]
    in_prompt = positions[row_count - rim_rows :] >= prompt_first[row_count - 1]
    tail_rows = joined[row_count - rim_rows :]
    conv_edges = jnp.where(in_prompt[:, None], tail_rows, jnp.zeros_like(tail_rows))
    conv_edges = conv_edges.reshape((1, rim_rows, 1, joined.shape[1]))
    return (mixed, segment_states, conv_edges)


def solution(mesh):
    in_specs = (
        P(("tok", "hv"), None),
        P(),
        P(None, "hv"),
        P(None, "hv"),
        P(None, "hv"),
        P(None, "hv"),
        P(None, "hv"),
        P(None, "hv"),
        P(),
        P(None, "hv"),
        P("hv"),
        P(None, "hv"),
        P(),
        P("hv", None),
    )
    out_specs = (P(("tok", "hv"), None), P("tok", "hv", None, None), P("tok", None, "hv", None))
    return jax.shard_map(shards, mesh=mesh, in_specs=in_specs, out_specs=out_specs, check_vma=False)
```

```python
import functools

import jax
import jax.numpy as jnp
from jax import lax
from jax.sharding import PartitionSpec as P

SPAN = 64


HIGH_PRECISION = lax.Precision.HIGH


def shifted(value, axis, steps):
    count = lax.axis_size(axis)
    initial, last = (max(0, -steps), min(count, count - steps))
    return lax.ppermute(value, axis, [(source, source + steps) for source in range(initial, last)])


def prompt_marks(positions, offsets):
    before = offsets[None, :] <= positions[:, None]
    prompt_first = jnp.max(jnp.where(before, offsets[None, :], 0), axis=1)
    return (prompt_first, (prompt_first == positions).astype(jnp.float32))


def short_conv(raw_rows, before_rows, weight, positions, prompt_first):
    tap_count = weight.shape[0]
    row_count = raw_rows.shape[0]
    extended = jnp.concatenate([before_rows, raw_rows], axis=0)
    lags = tap_count - 1 - jnp.arange(tap_count)
    inside_prompt = (positions[None, :] - lags[:, None] >= prompt_first[None, :]).astype(jnp.float32)
    windows = jnp.stack(
        [lax.slice_in_dim(extended, tap, tap + row_count, axis=0) for tap in range(tap_count)]
    )
    summed = jnp.sum(
        weight.astype(jnp.float32)[:, None, :]
        * windows.astype(jnp.float32)
        * inside_prompt[:, :, None],
        axis=0,
    )
    return jax.nn.silu(summed).astype(jnp.bfloat16)


def blocked(array_in):
    return array_in.reshape((array_in.shape[0] // SPAN, SPAN) + array_in.shape[1:])


def segment_parts(queries, head_keys, head_values, decays, starts):
    cumulative = jnp.cumsum(decays, axis=1)
    groups = jnp.cumsum(starts, axis=1)
    intact = (groups == 0.0).astype(jnp.float32)
    final_log = cumulative[:, -1]
    in_tail = (groups == groups[:, -1:]).astype(jnp.float32)
    weighted = (
        head_keys.astype(jnp.float32)
        * jnp.exp(final_log[:, None, :] - cumulative)
        * in_tail[:, :, None]
    ).astype(jnp.bfloat16)
    update = jnp.einsum("bsk,bsv->bkv", weighted, head_values, preferred_element_type=jnp.float32)
    step_decay = jnp.exp(final_log) * intact[:, -1:]
    index_rows = jnp.arange(queries.shape[1])
    allowed = (groups[:, :, None] == groups[:, None, :]) & (
        index_rows[None, :, None] >= index_rows[None, None, :]
    )
    lifted = queries.astype(jnp.float32) * jnp.exp(cumulative)
    lowered = (head_keys.astype(jnp.float32) * jnp.exp(-cumulative)).astype(jnp.bfloat16)
    raw_scores = jnp.einsum(
        "bak,bck->bac", lifted.astype(jnp.bfloat16), lowered, preferred_element_type=jnp.float32
    )
    scores = jnp.where(allowed, raw_scores, 0.0).astype(jnp.bfloat16)
    inside = jnp.einsum("bac,bcv->bav", scores, head_values, preferred_element_type=jnp.float32)
    lifted_intact = lifted * intact[:, :, None]
    block_count = queries.shape[0]
    memory = jnp.zeros(update.shape[1:], jnp.float32)
    product = jnp.ones(step_decay.shape[1:], jnp.float32)
    local_outs = [jnp.zeros(inside.shape[1:], jnp.float32)]
    products = [product]
    for block in range(block_count):
        if block > 0:
            local_outs.append(jnp.dot(lifted_intact[block], memory, precision=HIGH_PRECISION))
            products.append(product)
        memory = step_decay[block][:, None] * memory + update[block]
        product = product * step_decay[block]
    local_out = inside + jnp.stack(local_outs)
    carry_lift = lifted_intact * jnp.stack(products)[:, None, :]
    return (local_out, carry_lift, memory, product)


def packed_state(decay, memory):
    high = decay.astype(jnp.bfloat16)
    low = (decay - high.astype(jnp.float32)).astype(jnp.bfloat16)
    width = memory.shape[1]
    flat = jnp.concatenate([high, low])
    flat = jnp.pad(flat, (0, -flat.shape[0] % width))
    return jnp.concatenate([memory.astype(jnp.bfloat16), flat.reshape((-1, width))], axis=0)


def unpacked_state(packed, key_width):
    memory = packed[:key_width].astype(jnp.float32)
    flat = packed[key_width:].reshape((-1,)).astype(jnp.float32)
    return (flat[:key_width] + flat[key_width : 2 * key_width], memory)


def prefix_states(decay, memory, axis):
    count = lax.axis_size(axis)
    place = lax.axis_index(axis)
    key_width = memory.shape[0]
    entering_decay = jnp.ones_like(decay)
    entering = jnp.zeros_like(memory)
    steps = 1
    while steps < count:
        valid = place >= steps
        if steps * 2 < count:
            earlier_decay, earlier_memory = unpacked_state(
                shifted(packed_state(decay, memory), axis, steps), key_width
            )
        else:
            earlier_decay = None
            earlier_memory = shifted(memory.astype(jnp.bfloat16), axis, steps).astype(jnp.float32)
        memory = jnp.where(valid, decay[:, None] * earlier_memory + memory, memory)
        if steps == 1:
            entering = earlier_memory
            entering_decay = earlier_decay
        else:
            entering = jnp.where(valid, entering_decay[:, None] * earlier_memory + entering, entering)
        if earlier_decay is not None:
            decay = jnp.where(valid, earlier_decay * decay, decay)
            if steps > 1:
                entering_decay = jnp.where(valid, earlier_decay * entering_decay, entering_decay)
        steps *= 2
    return (memory, entering)


def rotations(axis):
    count = lax.axis_size(axis)
    return [[(source, (source + step) % count) for source in range(count)] for step in range(1, count)]


def gather_rows(rows, axis):
    count = lax.axis_size(axis)
    place = lax.axis_index(axis)
    if count & (count - 1):
        received = [rows] + [lax.ppermute(rows, axis, pairs) for pairs in rotations(axis)]
        order = [(-step) % count for step in range(count)]
    else:
        received = [rows]
        order = [0]
        mask = count // 2
        while mask >= 1:
            pairs = [(source, source ^ mask) for source in range(count)]
            received = received + [lax.ppermute(block, axis, pairs) for block in received]
            order = order + [flip ^ mask for flip in order]
            mask //= 2

    block = rows.shape[0]
    lookup = jnp.asarray([order.index(index) for index in range(count)], jnp.int32)
    target = jnp.arange(count * block, dtype=jnp.int32)
    if count & (count - 1):
        source_block = lookup[(target // block - place) % count]
    else:
        source_block = lookup[jnp.bitwise_xor(target // block, place)]
    source = source_block * block + target % block
    choose = (source[:, None] == target[None, :]).astype(rows.dtype)
    unordered = jnp.concatenate(received)
    return jnp.dot(choose, unordered, preferred_element_type=jnp.float32).astype(rows.dtype)


def scatter_sum(gated, weight, axis):
    count = lax.axis_size(axis)
    place = lax.axis_index(axis)
    chunk = gated.shape[0] // count

    def term(index):
        rows = lax.slice_in_dim(gated, index * chunk, (index + 1) * chunk, axis=0)
        return jnp.dot(rows, weight, preferred_element_type=jnp.float32).astype(jnp.bfloat16)

    if count & (count - 1):
        chunks = jnp.stack([term(index) for index in range(count)])
        total = lax.dynamic_index_in_dim(chunks, place, 0, False).astype(jnp.float32)
        for step, pairs in enumerate(rotations(axis), start=1):
            outgoing = lax.dynamic_index_in_dim(chunks, (place + step) % count, 0, False)
            total = total + lax.ppermute(outgoing, axis, pairs).astype(jnp.float32)
        return total.astype(jnp.bfloat16)
    held = [lax.slice_in_dim(gated, index * chunk, (index + 1) * chunk, axis=0) for index in range(count)]
    odd = place % 2 == 1
    pairs = list(zip(held[0::2], held[1::2]))
    outgoing = jnp.concatenate([jnp.where(odd, low, high) for low, high in pairs])
    outgoing = jnp.dot(outgoing, weight, preferred_element_type=jnp.float32).astype(jnp.bfloat16)
    incoming = lax.ppermute(outgoing, axis, [(source, source ^ 1) for source in range(count)])
    kept = jnp.concatenate([jnp.where(odd, high, low) for low, high in pairs])
    kept = jnp.dot(kept, weight, preferred_element_type=jnp.float32).astype(jnp.bfloat16)
    summed = kept.astype(jnp.float32) + incoming.astype(jnp.float32)
    held = list(jnp.split(summed, len(pairs)))
    mask = 2
    while mask < count:
        odd = (place // mask) % 2 == 1
        pairs = list(zip(held[0::2], held[1::2]))
        keep = [jnp.where(odd, high, low) for low, high in pairs]
        outgoing = jnp.stack([jnp.where(odd, low, high).astype(jnp.bfloat16) for low, high in pairs])
        incoming = lax.ppermute(outgoing, axis, [(source, source ^ mask) for source in range(count)])
        held = [
            kept.astype(jnp.float32) + incoming[index].astype(jnp.float32)
            for index, kept in enumerate(keep)
        ]
        mask *= 2
    return held[0].astype(jnp.bfloat16)


def shards(
    tokens,
    prompt_lengths,
    query_weight,
    key_weight,
    value_weight,
    query_conv,
    key_conv,
    value_conv,
    decay_down,
    decay_up,
    decay_bias,
    gate_weight,
    norm_gain,
    out_weight,
):
    gathered = gather_rows(tokens, "hv")

    def project(weight):
        return jnp.dot(gathered, weight, preferred_element_type=jnp.float32).astype(jnp.bfloat16)

    raw_query = project(query_weight)
    raw_key = project(key_weight)
    raw_value = project(value_weight)
    gate_values = project(gate_weight)
    low_rank = project(decay_down)
    row_count = raw_query.shape[0]
    key_width = raw_query.shape[1]
    value_width = raw_value.shape[1]
    positions = lax.axis_index("tok") * row_count + jnp.arange(row_count, dtype=jnp.int32)
    prompt_index = jnp.arange(prompt_lengths.shape[0])
    offsets = jnp.sum(
        jnp.where(prompt_index[None, :] < prompt_index[:, None], prompt_lengths[None, :], 0), axis=1
    )
    prompt_first, starts = prompt_marks(positions, offsets)
    rim_rows = query_conv.shape[0] - 1
    joined = jnp.concatenate([raw_query, raw_key, raw_value], axis=1)
    before_rows = shifted(joined[row_count - rim_rows :], "tok", 1)
    conv_query = short_conv(
        raw_query, before_rows[:, :key_width], query_conv, positions, prompt_first
    )
    conv_key = short_conv(
        raw_key, before_rows[:, key_width : 2 * key_width], key_conv, positions, prompt_first
    )
    conv_value = short_conv(
        raw_value, before_rows[:, 2 * key_width :], value_conv, positions, prompt_first
    )
    decays = (
        jax.nn.log_sigmoid(
            jnp.dot(low_rank, decay_up, preferred_element_type=jnp.float32) + decay_bias
        )
        / 16.0
    )
    local_out, carry_lift, local_memory, local_decay = segment_parts(
        blocked(conv_query), blocked(conv_key), blocked(conv_value), blocked(decays), blocked(starts)
    )
    closing, entering = prefix_states(local_decay, local_memory, "tok")
    heads_out = local_out.reshape((row_count, value_width)) + jnp.dot(
        carry_lift.reshape((row_count, key_width)), entering, precision=HIGH_PRECISION
    )
    gate_float = gate_values.astype(jnp.float32)
    rescale = lax.rsqrt(jnp.mean(heads_out * heads_out, axis=1, keepdims=True) + 1e-05)
    gated_out = (
        heads_out * rescale * norm_gain[None, :] * gate_float * jax.nn.sigmoid(gate_float)
    ).astype(jnp.bfloat16)
    mixed = scatter_sum(gated_out, out_weight, "hv")
    segment_states = closing[None, None]
    in_prompt = positions[row_count - rim_rows :] >= prompt_first[row_count - 1]
    tail_rows = joined[row_count - rim_rows :]
    conv_edges = jnp.where(in_prompt[:, None], tail_rows, jnp.zeros_like(tail_rows))
    conv_edges = conv_edges.reshape((1, rim_rows, 1, joined.shape[1]))
    return (mixed, segment_states, conv_edges)


def solution(mesh):
    in_specs = (
        P(("tok", "hv"), None),
        P(),
        P(None, "hv"),
        P(None, "hv"),
        P(None, "hv"),
        P(None, "hv"),
        P(None, "hv"),
        P(None, "hv"),
        P(),
        P(None, "hv"),
        P("hv"),
        P(None, "hv"),
        P(),
        P("hv", None),
    )
    out_specs = (P(("tok", "hv"), None), P("tok", "hv", None, None), P("tok", None, "hv", None))
    return jax.shard_map(shards, mesh=mesh, in_specs=in_specs, out_specs=out_specs, check_vma=False)
```

```python
import functools

import jax
import jax.numpy as jnp
from jax import lax
from jax.sharding import PartitionSpec as P

SPAN = 64


HIGH_PRECISION = lax.Precision.HIGH


def shifted(value, axis, steps):
    count = lax.axis_size(axis)
    initial, last = (max(0, -steps), min(count, count - steps))
    return lax.ppermute(value, axis, [(source, source + steps) for source in range(initial, last)])


def prompt_marks(positions, offsets):
    before = offsets[None, :] <= positions[:, None]
    prompt_first = jnp.max(jnp.where(before, offsets[None, :], 0), axis=1)
    return (prompt_first, (prompt_first == positions).astype(jnp.float32))


def short_conv(raw_rows, before_rows, weight, positions, prompt_first):
    tap_count = weight.shape[0]
    row_count = raw_rows.shape[0]
    extended = jnp.concatenate([before_rows, raw_rows], axis=0)
    lags = tap_count - 1 - jnp.arange(tap_count)
    inside_prompt = (positions[None, :] - lags[:, None] >= prompt_first[None, :]).astype(jnp.float32)
    windows = jnp.stack(
        [lax.slice_in_dim(extended, tap, tap + row_count, axis=0) for tap in range(tap_count)]
    )
    summed = jnp.sum(
        weight.astype(jnp.float32)[:, None, :]
        * windows.astype(jnp.float32)
        * inside_prompt[:, :, None],
        axis=0,
    )
    return jax.nn.silu(summed).astype(jnp.bfloat16)


def blocked(array_in):
    return array_in.reshape((array_in.shape[0] // SPAN, SPAN) + array_in.shape[1:])


def segment_parts(queries, head_keys, head_values, decays, starts):
    cumulative = jnp.cumsum(decays, axis=1)
    groups = jnp.cumsum(starts, axis=1)
    intact = (groups == 0.0).astype(jnp.float32)
    final_log = cumulative[:, -1]
    in_tail = (groups == groups[:, -1:]).astype(jnp.float32)
    weighted = (
        head_keys.astype(jnp.float32)
        * jnp.exp(final_log[:, None, :] - cumulative)
        * in_tail[:, :, None]
    ).astype(jnp.bfloat16)
    update = jnp.einsum("bsk,bsv->bkv", weighted, head_values, preferred_element_type=jnp.float32)
    step_decay = jnp.exp(final_log) * intact[:, -1:]
    index_rows = jnp.arange(queries.shape[1])
    allowed = (groups[:, :, None] == groups[:, None, :]) & (
        index_rows[None, :, None] >= index_rows[None, None, :]
    )
    lifted = queries.astype(jnp.float32) * jnp.exp(cumulative)
    lowered = (head_keys.astype(jnp.float32) * jnp.exp(-cumulative)).astype(jnp.bfloat16)
    raw_scores = jnp.einsum(
        "bak,bck->bac", lifted.astype(jnp.bfloat16), lowered, preferred_element_type=jnp.float32
    )
    scores = jnp.where(allowed, raw_scores, 0.0).astype(jnp.bfloat16)
    inside = jnp.einsum("bac,bcv->bav", scores, head_values, preferred_element_type=jnp.float32)
    lifted_intact = lifted * intact[:, :, None]
    block_count = queries.shape[0]
    memory = jnp.zeros(update.shape[1:], jnp.float32)
    product = jnp.ones(step_decay.shape[1:], jnp.float32)
    local_outs = [jnp.zeros(inside.shape[1:], jnp.float32)]
    products = [product]
    for block in range(block_count):
        if block > 0:
            local_outs.append(jnp.dot(lifted_intact[block], memory, precision=HIGH_PRECISION))
            products.append(product)
        memory = step_decay[block][:, None] * memory + update[block]
        product = product * step_decay[block]
    local_out = inside + jnp.stack(local_outs)
    carry_lift = lifted_intact * jnp.stack(products)[:, None, :]
    return (local_out, carry_lift, memory, product)


def packed_state(decay, memory):
    high = decay.astype(jnp.bfloat16)
    low = (decay - high.astype(jnp.float32)).astype(jnp.bfloat16)
    width = memory.shape[1]
    flat = jnp.concatenate([high, low])
    flat = jnp.pad(flat, (0, -flat.shape[0] % width))
    return jnp.concatenate([memory.astype(jnp.bfloat16), flat.reshape((-1, width))], axis=0)


def unpacked_state(packed, key_width):
    memory = packed[:key_width].astype(jnp.float32)
    flat = packed[key_width:].reshape((-1,)).astype(jnp.float32)
    return (flat[:key_width] + flat[key_width : 2 * key_width], memory)


def prefix_states(decay, memory, axis):
    count = lax.axis_size(axis)
    place = lax.axis_index(axis)
    key_width = memory.shape[0]
    entering_decay = jnp.ones_like(decay)
    entering = jnp.zeros_like(memory)
    steps = 1
    while steps < count:
        valid = place >= steps
        if steps * 2 < count:
            earlier_decay, earlier_memory = unpacked_state(
                shifted(packed_state(decay, memory), axis, steps), key_width
            )
        else:
            earlier_decay = None
            earlier_memory = shifted(memory.astype(jnp.bfloat16), axis, steps).astype(jnp.float32)
        memory = jnp.where(valid, decay[:, None] * earlier_memory + memory, memory)
        if steps == 1:
            entering = earlier_memory
            entering_decay = earlier_decay
        else:
            entering = jnp.where(valid, entering_decay[:, None] * earlier_memory + entering, entering)
        if earlier_decay is not None:
            decay = jnp.where(valid, earlier_decay * decay, decay)
            if steps > 1:
                entering_decay = jnp.where(valid, earlier_decay * entering_decay, entering_decay)
        steps *= 2
    return (memory, entering)


def rotations(axis):
    count = lax.axis_size(axis)
    return [[(source, (source + step) % count) for source in range(count)] for step in range(1, count)]


def gather_rows(rows, axis):
    count = lax.axis_size(axis)
    place = lax.axis_index(axis)
    if count & (count - 1):
        received = [rows] + [lax.ppermute(rows, axis, pairs) for pairs in rotations(axis)]
        order = [(-step) % count for step in range(count)]
    else:
        received = [rows]
        order = [0]
        mask = count // 2
        while mask >= 1:
            incoming = lax.ppermute(
                jnp.concatenate(received), axis, [(source, source ^ mask) for source in range(count)]
            )
            received = received + list(jnp.split(incoming, len(received)))
            order = order + [flip ^ mask for flip in order]
            mask //= 2

    def ordered(shift):
        if count & (count - 1):
            picks = [order.index((index - shift) % count) for index in range(count)]
        else:
            picks = [order.index(shift ^ index) for index in range(count)]
        return jnp.concatenate([received[pick] for pick in picks])

    return lax.switch(place, [functools.partial(ordered, shift) for shift in range(count)])


def scatter_sum(gated, weight, axis):
    count = lax.axis_size(axis)
    place = lax.axis_index(axis)
    chunk = gated.shape[0] // count

    def term(index):
        rows = lax.slice_in_dim(gated, index * chunk, (index + 1) * chunk, axis=0)
        return jnp.dot(rows, weight, preferred_element_type=jnp.float32).astype(jnp.bfloat16)

    if count & (count - 1):
        chunks = jnp.stack([term(index) for index in range(count)])
        total = lax.dynamic_index_in_dim(chunks, place, 0, False).astype(jnp.float32)
        for step, pairs in enumerate(rotations(axis), start=1):
            outgoing = lax.dynamic_index_in_dim(chunks, (place + step) % count, 0, False)
            total = total + lax.ppermute(outgoing, axis, pairs).astype(jnp.float32)
        return total.astype(jnp.bfloat16)
    held = [lax.slice_in_dim(gated, index * chunk, (index + 1) * chunk, axis=0) for index in range(count)]
    odd = place % 2 == 1
    pairs = list(zip(held[0::2], held[1::2]))
    outgoing = jnp.concatenate([jnp.where(odd, low, high) for low, high in pairs])
    outgoing = jnp.dot(outgoing, weight, preferred_element_type=jnp.float32).astype(jnp.bfloat16)
    incoming = lax.ppermute(outgoing, axis, [(source, source ^ 1) for source in range(count)])
    kept = jnp.concatenate([jnp.where(odd, high, low) for low, high in pairs])
    kept = lax.optimization_barrier(
        jnp.dot(kept, weight, preferred_element_type=jnp.float32).astype(jnp.bfloat16)
    )
    summed = kept.astype(jnp.float32) + incoming.astype(jnp.float32)
    held = list(jnp.split(summed, len(pairs)))
    mask = 2
    while mask < count:
        odd = (place // mask) % 2 == 1
        pairs = list(zip(held[0::2], held[1::2]))
        keep = [jnp.where(odd, high, low) for low, high in pairs]
        outgoing = jnp.stack([jnp.where(odd, low, high).astype(jnp.bfloat16) for low, high in pairs])
        incoming = lax.ppermute(outgoing, axis, [(source, source ^ mask) for source in range(count)])
        held = [
            kept.astype(jnp.float32) + incoming[index].astype(jnp.float32)
            for index, kept in enumerate(keep)
        ]
        mask *= 2
    return held[0].astype(jnp.bfloat16)


def shards(
    tokens,
    prompt_lengths,
    query_weight,
    key_weight,
    value_weight,
    query_conv,
    key_conv,
    value_conv,
    decay_down,
    decay_up,
    decay_bias,
    gate_weight,
    norm_gain,
    out_weight,
):
    gathered = gather_rows(tokens, "hv")

    def project(weight):
        return jnp.dot(gathered, weight, preferred_element_type=jnp.float32).astype(jnp.bfloat16)

    raw_query = project(query_weight)
    raw_key = project(key_weight)
    raw_value = project(value_weight)
    gate_values = lax.optimization_barrier(project(gate_weight))
    low_rank = project(decay_down)
    row_count = raw_query.shape[0]
    key_width = raw_query.shape[1]
    value_width = raw_value.shape[1]
    positions = lax.axis_index("tok") * row_count + jnp.arange(row_count, dtype=jnp.int32)
    prompt_index = jnp.arange(prompt_lengths.shape[0])
    offsets = jnp.sum(
        jnp.where(prompt_index[None, :] < prompt_index[:, None], prompt_lengths[None, :], 0), axis=1
    )
    prompt_first, starts = prompt_marks(positions, offsets)
    rim_rows = query_conv.shape[0] - 1
    joined = jnp.concatenate([raw_query, raw_key, raw_value], axis=1)
    before_rows = shifted(joined[row_count - rim_rows :], "tok", 1)
    conv_query = short_conv(
        raw_query, before_rows[:, :key_width], query_conv, positions, prompt_first
    )
    conv_key = short_conv(
        raw_key, before_rows[:, key_width : 2 * key_width], key_conv, positions, prompt_first
    )
    conv_value = short_conv(
        raw_value, before_rows[:, 2 * key_width :], value_conv, positions, prompt_first
    )
    decays = (
        jax.nn.log_sigmoid(
            jnp.dot(low_rank, decay_up, preferred_element_type=jnp.float32) + decay_bias
        )
        / 16.0
    )
    local_out, carry_lift, local_memory, local_decay = segment_parts(
        blocked(conv_query), blocked(conv_key), blocked(conv_value), blocked(decays), blocked(starts)
    )
    closing, entering = prefix_states(local_decay, local_memory, "tok")
    heads_out = local_out.reshape((row_count, value_width)) + jnp.dot(
        carry_lift.reshape((row_count, key_width)), entering, precision=HIGH_PRECISION
    )
    gate_float = gate_values.astype(jnp.float32)
    rescale = lax.rsqrt(jnp.mean(heads_out * heads_out, axis=1, keepdims=True) + 1e-05)
    gated_out = (
        heads_out * rescale * norm_gain[None, :] * gate_float * jax.nn.sigmoid(gate_float)
    ).astype(jnp.bfloat16)
    mixed = scatter_sum(gated_out, out_weight, "hv")
    segment_states = closing[None, None]
    in_prompt = positions[row_count - rim_rows :] >= prompt_first[row_count - 1]
    tail_rows = joined[row_count - rim_rows :]
    conv_edges = jnp.where(in_prompt[:, None], tail_rows, jnp.zeros_like(tail_rows))
    conv_edges = conv_edges.reshape((1, rim_rows, 1, joined.shape[1]))
    return (mixed, segment_states, conv_edges)


def solution(mesh):
    in_specs = (
        P(("tok", "hv"), None),
        P(),
        P(None, "hv"),
        P(None, "hv"),
        P(None, "hv"),
        P(None, "hv"),
        P(None, "hv"),
        P(None, "hv"),
        P(),
        P(None, "hv"),
        P("hv"),
        P(None, "hv"),
        P(),
        P("hv", None),
    )
    out_specs = (P(("tok", "hv"), None), P("tok", "hv", None, None), P("tok", None, "hv", None))
    return jax.shard_map(shards, mesh=mesh, in_specs=in_specs, out_specs=out_specs, check_vma=False)
```

```python
import functools

import jax
import jax.numpy as jnp
from jax import lax
from jax.sharding import PartitionSpec as P

SPAN = 64


HIGH_PRECISION = lax.Precision.HIGH


def shifted(value, axis, steps):
    count = lax.axis_size(axis)
    initial, last = (max(0, -steps), min(count, count - steps))
    return lax.ppermute(value, axis, [(source, source + steps) for source in range(initial, last)])


def prompt_marks(positions, offsets):
    before = offsets[None, :] <= positions[:, None]
    prompt_first = jnp.max(jnp.where(before, offsets[None, :], 0), axis=1)
    return (prompt_first, (prompt_first == positions).astype(jnp.float32))


def short_conv(raw_rows, before_rows, weight, positions, prompt_first):
    tap_count = weight.shape[0]
    row_count = raw_rows.shape[0]
    extended = jnp.concatenate([before_rows, raw_rows], axis=0)
    lags = tap_count - 1 - jnp.arange(tap_count)
    inside_prompt = (positions[None, :] - lags[:, None] >= prompt_first[None, :]).astype(jnp.float32)
    windows = jnp.stack(
        [lax.slice_in_dim(extended, tap, tap + row_count, axis=0) for tap in range(tap_count)]
    )
    summed = jnp.sum(
        weight.astype(jnp.float32)[:, None, :]
        * windows.astype(jnp.float32)
        * inside_prompt[:, :, None],
        axis=0,
    )
    return jax.nn.silu(summed).astype(jnp.bfloat16)


def blocked(array_in):
    return array_in.reshape((array_in.shape[0] // SPAN, SPAN) + array_in.shape[1:])


def segment_parts(queries, head_keys, head_values, decays, starts):
    cumulative = jnp.cumsum(decays, axis=1)
    groups = jnp.cumsum(starts, axis=1)
    intact = (groups == 0.0).astype(jnp.float32)
    final_log = cumulative[:, -1]
    in_tail = (groups == groups[:, -1:]).astype(jnp.float32)
    weighted = (
        head_keys.astype(jnp.float32)
        * jnp.exp(final_log[:, None, :] - cumulative)
        * in_tail[:, :, None]
    ).astype(jnp.bfloat16)
    update = jnp.einsum("bsk,bsv->bkv", weighted, head_values, preferred_element_type=jnp.float32)
    step_decay = jnp.exp(final_log) * intact[:, -1:]
    index_rows = jnp.arange(queries.shape[1])
    allowed = (groups[:, :, None] == groups[:, None, :]) & (
        index_rows[None, :, None] >= index_rows[None, None, :]
    )
    lifted = queries.astype(jnp.float32) * jnp.exp(cumulative)
    lowered = (head_keys.astype(jnp.float32) * jnp.exp(-cumulative)).astype(jnp.bfloat16)
    raw_scores = jnp.einsum(
        "bak,bck->bac", lifted.astype(jnp.bfloat16), lowered, preferred_element_type=jnp.float32
    )
    scores = jnp.where(allowed, raw_scores, 0.0).astype(jnp.bfloat16)
    inside = jnp.einsum("bac,bcv->bav", scores, head_values, preferred_element_type=jnp.float32)
    lifted_intact = lifted * intact[:, :, None]
    block_count = queries.shape[0]
    memory = jnp.zeros(update.shape[1:], jnp.float32)
    product = jnp.ones(step_decay.shape[1:], jnp.float32)
    local_outs = [jnp.zeros(inside.shape[1:], jnp.float32)]
    products = [product]
    for block in range(block_count):
        if block > 0:
            local_outs.append(jnp.dot(lifted_intact[block], memory, precision=HIGH_PRECISION))
            products.append(product)
        memory = step_decay[block][:, None] * memory + update[block]
        product = product * step_decay[block]
    local_out = inside + jnp.stack(local_outs)
    carry_lift = lifted_intact * jnp.stack(products)[:, None, :]
    return (local_out, carry_lift, memory, product)


def packed_state(decay, memory):
    high = decay.astype(jnp.bfloat16)
    low = (decay - high.astype(jnp.float32)).astype(jnp.bfloat16)
    width = memory.shape[1]
    flat = jnp.concatenate([high, low])
    flat = jnp.pad(flat, (0, -flat.shape[0] % width))
    return jnp.concatenate([memory.astype(jnp.bfloat16), flat.reshape((-1, width))], axis=0)


def unpacked_state(packed, key_width):
    memory = packed[:key_width].astype(jnp.float32)
    flat = packed[key_width:].reshape((-1,)).astype(jnp.float32)
    return (flat[:key_width] + flat[key_width : 2 * key_width], memory)


def prefix_states(decay, memory, axis):
    count = lax.axis_size(axis)
    place = lax.axis_index(axis)
    key_width = memory.shape[0]
    entering_decay = jnp.ones_like(decay)
    entering = jnp.zeros_like(memory)
    steps = 1
    while steps < count:
        valid = place >= steps
        if steps * 2 < count:
            earlier_decay, earlier_memory = unpacked_state(
                shifted(packed_state(decay, memory), axis, steps), key_width
            )
        else:
            earlier_decay = None
            earlier_memory = shifted(memory.astype(jnp.bfloat16), axis, steps).astype(jnp.float32)
        memory = jnp.where(valid, decay[:, None] * earlier_memory + memory, memory)
        if steps == 1:
            entering = earlier_memory
            entering_decay = earlier_decay
        else:
            entering = jnp.where(valid, entering_decay[:, None] * earlier_memory + entering, entering)
        if earlier_decay is not None:
            decay = jnp.where(valid, earlier_decay * decay, decay)
            if steps > 1:
                entering_decay = jnp.where(valid, earlier_decay * entering_decay, entering_decay)
        steps *= 2
    return (memory, entering)


def rotations(axis):
    count = lax.axis_size(axis)
    return [[(source, (source + step) % count) for source in range(count)] for step in range(1, count)]


def gather_rows(rows, axis):
    count = lax.axis_size(axis)
    place = lax.axis_index(axis)
    if count & (count - 1):
        received = [rows] + [lax.ppermute(rows, axis, pairs) for pairs in rotations(axis)]
        order = [(-step) % count for step in range(count)]
    else:
        received = [rows]
        order = [0]
        mask = count // 2
        while mask >= 1:
            incoming = lax.ppermute(
                jnp.concatenate(received), axis, [(source, source ^ mask) for source in range(count)]
            )
            received = received + list(jnp.split(incoming, len(received)))
            order = order + [flip ^ mask for flip in order]
            mask //= 2

    def ordered(shift):
        if count & (count - 1):
            picks = [order.index((index - shift) % count) for index in range(count)]
        else:
            picks = [order.index(shift ^ index) for index in range(count)]
        return jnp.concatenate([received[pick] for pick in picks])

    return lax.switch(place, [functools.partial(ordered, shift) for shift in range(count)])


def scatter_sum(gated, weight, axis):
    count = lax.axis_size(axis)
    place = lax.axis_index(axis)
    chunk = gated.shape[0] // count

    def term(index):
        rows = lax.slice_in_dim(gated, index * chunk, (index + 1) * chunk, axis=0)
        return jnp.dot(rows, weight, preferred_element_type=jnp.float32).astype(jnp.bfloat16)

    if count & (count - 1):
        chunks = jnp.stack([term(index) for index in range(count)])
        total = lax.dynamic_index_in_dim(chunks, place, 0, False).astype(jnp.float32)
        for step, pairs in enumerate(rotations(axis), start=1):
            outgoing = lax.dynamic_index_in_dim(chunks, (place + step) % count, 0, False)
            total = total + lax.ppermute(outgoing, axis, pairs).astype(jnp.float32)
        return total.astype(jnp.bfloat16)
    held = [lax.slice_in_dim(gated, index * chunk, (index + 1) * chunk, axis=0) for index in range(count)]
    odd = place % 2 == 1
    pairs = list(zip(held[0::2], held[1::2]))
    outgoing = jnp.concatenate([jnp.where(odd, low, high) for low, high in pairs])
    outgoing = jnp.dot(outgoing, weight, preferred_element_type=jnp.float32).astype(jnp.bfloat16)
    incoming = lax.ppermute(outgoing, axis, [(source, source ^ 1) for source in range(count)])
    kept = jnp.concatenate([jnp.where(odd, high, low) for low, high in pairs])
    kept = jnp.dot(kept, weight, preferred_element_type=jnp.float32).astype(jnp.bfloat16)
    summed = kept.astype(jnp.float32) + incoming.astype(jnp.float32)
    held = list(jnp.split(summed, len(pairs)))
    mask = 2
    while mask < count:
        odd = (place // mask) % 2 == 1
        pairs = list(zip(held[0::2], held[1::2]))
        keep = [jnp.where(odd, high, low) for low, high in pairs]
        outgoing = jnp.stack([jnp.where(odd, low, high).astype(jnp.bfloat16) for low, high in pairs])
        incoming = lax.ppermute(outgoing, axis, [(source, source ^ mask) for source in range(count)])
        held = [
            kept.astype(jnp.float32) + incoming[index].astype(jnp.float32)
            for index, kept in enumerate(keep)
        ]
        mask *= 2
    return held[0].astype(jnp.bfloat16)


def shards(
    tokens,
    prompt_lengths,
    query_weight,
    key_weight,
    value_weight,
    query_conv,
    key_conv,
    value_conv,
    decay_down,
    decay_up,
    decay_bias,
    gate_weight,
    norm_gain,
    out_weight,
):
    gathered = gather_rows(tokens, "hv")

    def project(weight):
        return jnp.dot(gathered, weight, preferred_element_type=jnp.float32).astype(jnp.bfloat16)

    raw_query = project(query_weight)
    raw_key = project(key_weight)
    raw_value = project(value_weight)
    gate_values = project(gate_weight)
    low_rank = project(decay_down)
    row_count = raw_query.shape[0]
    key_width = raw_query.shape[1]
    value_width = raw_value.shape[1]
    positions = lax.axis_index("tok") * row_count + jnp.arange(row_count, dtype=jnp.int32)
    prompt_index = jnp.arange(prompt_lengths.shape[0])
    offsets = jnp.sum(
        jnp.where(prompt_index[None, :] < prompt_index[:, None], prompt_lengths[None, :], 0), axis=1
    )
    prompt_first, starts = prompt_marks(positions, offsets)
    rim_rows = query_conv.shape[0] - 1
    joined = jnp.concatenate([raw_query, raw_key, raw_value], axis=1)
    before_rows = shifted(joined[row_count - rim_rows :], "tok", 1)
    conv_query = short_conv(
        raw_query, before_rows[:, :key_width], query_conv, positions, prompt_first
    )
    conv_key = short_conv(
        raw_key, before_rows[:, key_width : 2 * key_width], key_conv, positions, prompt_first
    )
    conv_value = short_conv(
        raw_value, before_rows[:, 2 * key_width :], value_conv, positions, prompt_first
    )
    decays = (
        jax.nn.log_sigmoid(
            jnp.dot(low_rank, decay_up, preferred_element_type=jnp.float32) + decay_bias
        )
        / 16.0
    )
    local_out, carry_lift, local_memory, local_decay = segment_parts(
        blocked(conv_query), blocked(conv_key), blocked(conv_value), blocked(decays), blocked(starts)
    )
    closing, entering = prefix_states(local_decay, local_memory, "tok")
    heads_out = local_out.reshape((row_count, value_width)) + jnp.dot(
        carry_lift.reshape((row_count, key_width)), entering
    )
    gate_float = gate_values.astype(jnp.float32)
    rescale = lax.rsqrt(jnp.mean(heads_out * heads_out, axis=1, keepdims=True) + 1e-05)
    gated_out = (
        heads_out * rescale * norm_gain[None, :] * gate_float * jax.nn.sigmoid(gate_float)
    ).astype(jnp.bfloat16)
    mixed = scatter_sum(gated_out, out_weight, "hv")
    segment_states = closing[None, None]
    in_prompt = positions[row_count - rim_rows :] >= prompt_first[row_count - 1]
    tail_rows = joined[row_count - rim_rows :]
    conv_edges = jnp.where(in_prompt[:, None], tail_rows, jnp.zeros_like(tail_rows))
    conv_edges = conv_edges.reshape((1, rim_rows, 1, joined.shape[1]))
    return (mixed, segment_states, conv_edges)


def solution(mesh):
    in_specs = (
        P(("tok", "hv"), None),
        P(),
        P(None, "hv"),
        P(None, "hv"),
        P(None, "hv"),
        P(None, "hv"),
        P(None, "hv"),
        P(None, "hv"),
        P(),
        P(None, "hv"),
        P("hv"),
        P(None, "hv"),
        P(),
        P("hv", None),
    )
    out_specs = (P(("tok", "hv"), None), P("tok", "hv", None, None), P("tok", None, "hv", None))
    return jax.shard_map(shards, mesh=mesh, in_specs=in_specs, out_specs=out_specs, check_vma=False)
```

```python
import functools

import jax
import jax.numpy as jnp
from jax import lax
from jax.sharding import PartitionSpec as P

SPAN = 64


HIGH_PRECISION = lax.Precision.HIGH


def shifted(value, axis, steps):
    count = lax.axis_size(axis)
    initial, last = (max(0, -steps), min(count, count - steps))
    return lax.ppermute(value, axis, [(source, source + steps) for source in range(initial, last)])


def prompt_marks(positions, offsets):
    before = offsets[None, :] <= positions[:, None]
    prompt_first = jnp.max(jnp.where(before, offsets[None, :], 0), axis=1)
    return (prompt_first, (prompt_first == positions).astype(jnp.float32))


def short_conv(raw_rows, before_rows, weight, positions, prompt_first):
    tap_count = weight.shape[0]
    row_count = raw_rows.shape[0]
    extended = jnp.concatenate([before_rows, raw_rows], axis=0)
    lags = tap_count - 1 - jnp.arange(tap_count)
    inside_prompt = (positions[None, :] - lags[:, None] >= prompt_first[None, :]).astype(jnp.float32)
    windows = jnp.stack(
        [lax.slice_in_dim(extended, tap, tap + row_count, axis=0) for tap in range(tap_count)]
    )
    summed = jnp.sum(
        weight.astype(jnp.float32)[:, None, :]
        * windows.astype(jnp.float32)
        * inside_prompt[:, :, None],
        axis=0,
    )
    return jax.nn.silu(summed).astype(jnp.bfloat16)


def blocked(array_in):
    return array_in.reshape((array_in.shape[0] // SPAN, SPAN) + array_in.shape[1:])


def segment_parts(queries, head_keys, head_values, decays, starts):
    index_rows = jnp.arange(queries.shape[1])
    lower = (index_rows[:, None] >= index_rows[None, :]).astype(jnp.float32)
    cumulative = jnp.einsum("ac,bck->bak", lower, decays, precision=lax.Precision.HIGHEST)
    groups = jnp.cumsum(starts, axis=1)
    intact = (groups == 0.0).astype(jnp.float32)
    final_log = cumulative[:, -1]
    in_tail = (groups == groups[:, -1:]).astype(jnp.float32)
    weighted = (
        head_keys.astype(jnp.float32)
        * jnp.exp(final_log[:, None, :] - cumulative)
        * in_tail[:, :, None]
    ).astype(jnp.bfloat16)
    update = jnp.einsum("bsk,bsv->bkv", weighted, head_values, preferred_element_type=jnp.float32)
    step_decay = jnp.exp(final_log) * intact[:, -1:]
    allowed = (groups[:, :, None] == groups[:, None, :]) & (
        index_rows[None, :, None] >= index_rows[None, None, :]
    )
    lifted = queries.astype(jnp.float32) * jnp.exp(cumulative)
    lowered = (head_keys.astype(jnp.float32) * jnp.exp(-cumulative)).astype(jnp.bfloat16)
    raw_scores = jnp.einsum(
        "bak,bck->bac", lifted.astype(jnp.bfloat16), lowered, preferred_element_type=jnp.float32
    )
    scores = jnp.where(allowed, raw_scores, 0.0).astype(jnp.bfloat16)
    inside = jnp.einsum("bac,bcv->bav", scores, head_values, preferred_element_type=jnp.float32)
    lifted_intact = lifted * intact[:, :, None]
    block_count = queries.shape[0]
    memory = jnp.zeros(update.shape[1:], jnp.float32)
    product = jnp.ones(step_decay.shape[1:], jnp.float32)
    local_outs = [jnp.zeros(inside.shape[1:], jnp.float32)]
    products = [product]
    for block in range(block_count):
        if block > 0:
            local_outs.append(jnp.dot(lifted_intact[block], memory, precision=HIGH_PRECISION))
            products.append(product)
        memory = step_decay[block][:, None] * memory + update[block]
        product = product * step_decay[block]
    local_out = inside + jnp.stack(local_outs)
    carry_lift = lifted_intact * jnp.stack(products)[:, None, :]
    return (local_out, carry_lift, memory, product)


def packed_state(decay, memory):
    high = decay.astype(jnp.bfloat16)
    low = (decay - high.astype(jnp.float32)).astype(jnp.bfloat16)
    width = memory.shape[1]
    flat = jnp.concatenate([high, low])
    flat = jnp.pad(flat, (0, -flat.shape[0] % width))
    return jnp.concatenate([memory.astype(jnp.bfloat16), flat.reshape((-1, width))], axis=0)


def unpacked_state(packed, key_width):
    memory = packed[:key_width].astype(jnp.float32)
    flat = packed[key_width:].reshape((-1,)).astype(jnp.float32)
    return (flat[:key_width] + flat[key_width : 2 * key_width], memory)


def prefix_states(decay, memory, axis):
    count = lax.axis_size(axis)
    place = lax.axis_index(axis)
    key_width = memory.shape[0]
    entering_decay = jnp.ones_like(decay)
    entering = jnp.zeros_like(memory)
    steps = 1
    while steps < count:
        valid = place >= steps
        if steps * 2 < count:
            earlier_decay, earlier_memory = unpacked_state(
                shifted(packed_state(decay, memory), axis, steps), key_width
            )
        else:
            earlier_decay = None
            earlier_memory = shifted(memory.astype(jnp.bfloat16), axis, steps).astype(jnp.float32)
        memory = jnp.where(valid, decay[:, None] * earlier_memory + memory, memory)
        if steps == 1:
            entering = earlier_memory
            entering_decay = earlier_decay
        else:
            entering = jnp.where(valid, entering_decay[:, None] * earlier_memory + entering, entering)
        if earlier_decay is not None:
            decay = jnp.where(valid, earlier_decay * decay, decay)
            if steps > 1:
                entering_decay = jnp.where(valid, earlier_decay * entering_decay, entering_decay)
        steps *= 2
    return (memory, entering)


def rotations(axis):
    count = lax.axis_size(axis)
    return [[(source, (source + step) % count) for source in range(count)] for step in range(1, count)]


def gather_rows(rows, axis):
    count = lax.axis_size(axis)
    place = lax.axis_index(axis)
    if count & (count - 1):
        received = [rows] + [lax.ppermute(rows, axis, pairs) for pairs in rotations(axis)]
        order = [(-step) % count for step in range(count)]
    else:
        received = [rows]
        order = [0]
        mask = count // 2
        while mask >= 1:
            incoming = lax.ppermute(
                jnp.concatenate(received), axis, [(source, source ^ mask) for source in range(count)]
            )
            received = received + list(jnp.split(incoming, len(received)))
            order = order + [flip ^ mask for flip in order]
            mask //= 2

    def ordered(shift):
        if count & (count - 1):
            picks = [order.index((index - shift) % count) for index in range(count)]
        else:
            picks = [order.index(shift ^ index) for index in range(count)]
        return jnp.concatenate([received[pick] for pick in picks])

    return lax.switch(place, [functools.partial(ordered, shift) for shift in range(count)])


def scatter_sum(gated, weight, axis):
    count = lax.axis_size(axis)
    place = lax.axis_index(axis)
    chunk = gated.shape[0] // count

    def term(index):
        rows = lax.slice_in_dim(gated, index * chunk, (index + 1) * chunk, axis=0)
        return jnp.dot(rows, weight, preferred_element_type=jnp.float32).astype(jnp.bfloat16)

    if count & (count - 1):
        chunks = jnp.stack([term(index) for index in range(count)])
        total = lax.dynamic_index_in_dim(chunks, place, 0, False).astype(jnp.float32)
        for step, pairs in enumerate(rotations(axis), start=1):
            outgoing = lax.dynamic_index_in_dim(chunks, (place + step) % count, 0, False)
            total = total + lax.ppermute(outgoing, axis, pairs).astype(jnp.float32)
        return total.astype(jnp.bfloat16)
    held = [lax.slice_in_dim(gated, index * chunk, (index + 1) * chunk, axis=0) for index in range(count)]
    odd = place % 2 == 1
    pairs = list(zip(held[0::2], held[1::2]))
    outgoing = jnp.concatenate([jnp.where(odd, low, high) for low, high in pairs])
    outgoing = jnp.dot(outgoing, weight, preferred_element_type=jnp.float32).astype(jnp.bfloat16)
    incoming = lax.ppermute(outgoing, axis, [(source, source ^ 1) for source in range(count)])
    kept = jnp.concatenate([jnp.where(odd, high, low) for low, high in pairs])
    kept = jnp.dot(kept, weight, preferred_element_type=jnp.float32).astype(jnp.bfloat16)
    summed = kept.astype(jnp.float32) + incoming.astype(jnp.float32)
    held = list(jnp.split(summed, len(pairs)))
    mask = 2
    while mask < count:
        odd = (place // mask) % 2 == 1
        pairs = list(zip(held[0::2], held[1::2]))
        keep = [jnp.where(odd, high, low) for low, high in pairs]
        outgoing = jnp.stack([jnp.where(odd, low, high).astype(jnp.bfloat16) for low, high in pairs])
        incoming = lax.ppermute(outgoing, axis, [(source, source ^ mask) for source in range(count)])
        held = [
            kept.astype(jnp.float32) + incoming[index].astype(jnp.float32)
            for index, kept in enumerate(keep)
        ]
        mask *= 2
    return held[0].astype(jnp.bfloat16)


def shards(
    tokens,
    prompt_lengths,
    query_weight,
    key_weight,
    value_weight,
    query_conv,
    key_conv,
    value_conv,
    decay_down,
    decay_up,
    decay_bias,
    gate_weight,
    norm_gain,
    out_weight,
):
    gathered = gather_rows(tokens, "hv")

    def project(weight):
        return jnp.dot(gathered, weight, preferred_element_type=jnp.float32).astype(jnp.bfloat16)

    raw_query = project(query_weight)
    raw_key = project(key_weight)
    raw_value = project(value_weight)
    gate_values = project(gate_weight)
    low_rank = project(decay_down)
    row_count = raw_query.shape[0]
    key_width = raw_query.shape[1]
    value_width = raw_value.shape[1]
    positions = lax.axis_index("tok") * row_count + jnp.arange(row_count, dtype=jnp.int32)
    prompt_index = jnp.arange(prompt_lengths.shape[0])
    offsets = jnp.sum(
        jnp.where(prompt_index[None, :] < prompt_index[:, None], prompt_lengths[None, :], 0), axis=1
    )
    prompt_first, starts = prompt_marks(positions, offsets)
    rim_rows = query_conv.shape[0] - 1
    joined = jnp.concatenate([raw_query, raw_key, raw_value], axis=1)
    before_rows = shifted(joined[row_count - rim_rows :], "tok", 1)
    conv_query = short_conv(
        raw_query, before_rows[:, :key_width], query_conv, positions, prompt_first
    )
    conv_key = short_conv(
        raw_key, before_rows[:, key_width : 2 * key_width], key_conv, positions, prompt_first
    )
    conv_value = short_conv(
        raw_value, before_rows[:, 2 * key_width :], value_conv, positions, prompt_first
    )
    decays = (
        jax.nn.log_sigmoid(
            jnp.dot(low_rank, decay_up, preferred_element_type=jnp.float32) + decay_bias
        )
        / 16.0
    )
    local_out, carry_lift, local_memory, local_decay = segment_parts(
        blocked(conv_query), blocked(conv_key), blocked(conv_value), blocked(decays), blocked(starts)
    )
    closing, entering = prefix_states(local_decay, local_memory, "tok")
    heads_out = local_out.reshape((row_count, value_width)) + jnp.dot(
        carry_lift.reshape((row_count, key_width)), entering, precision=HIGH_PRECISION
    )
    gate_float = gate_values.astype(jnp.float32)
    rescale = lax.rsqrt(jnp.mean(heads_out * heads_out, axis=1, keepdims=True) + 1e-05)
    gated_out = (
        heads_out * rescale * norm_gain[None, :] * gate_float * jax.nn.sigmoid(gate_float)
    ).astype(jnp.bfloat16)
    mixed = scatter_sum(gated_out, out_weight, "hv")
    segment_states = closing[None, None]
    in_prompt = positions[row_count - rim_rows :] >= prompt_first[row_count - 1]
    tail_rows = joined[row_count - rim_rows :]
    conv_edges = jnp.where(in_prompt[:, None], tail_rows, jnp.zeros_like(tail_rows))
    conv_edges = conv_edges.reshape((1, rim_rows, 1, joined.shape[1]))
    return (mixed, segment_states, conv_edges)


def solution(mesh):
    in_specs = (
        P(("tok", "hv"), None),
        P(),
        P(None, "hv"),
        P(None, "hv"),
        P(None, "hv"),
        P(None, "hv"),
        P(None, "hv"),
        P(None, "hv"),
        P(),
        P(None, "hv"),
        P("hv"),
        P(None, "hv"),
        P(),
        P("hv", None),
    )
    out_specs = (P(("tok", "hv"), None), P("tok", "hv", None, None), P("tok", None, "hv", None))
    return jax.shard_map(shards, mesh=mesh, in_specs=in_specs, out_specs=out_specs, check_vma=False)
```

```python
import functools

import jax
import jax.numpy as jnp
from jax import lax
from jax.sharding import PartitionSpec as P

SPAN = 64


HIGH_PRECISION = lax.Precision.HIGH


def shifted(value, axis, steps):
    count = lax.axis_size(axis)
    initial, last = (max(0, -steps), min(count, count - steps))
    return lax.ppermute(value, axis, [(source, source + steps) for source in range(initial, last)])


def prompt_marks(positions, offsets):
    before = offsets[None, :] <= positions[:, None]
    prompt_first = jnp.max(jnp.where(before, offsets[None, :], 0), axis=1)
    return (prompt_first, (prompt_first == positions).astype(jnp.float32))


def short_conv(raw_rows, before_rows, weight, positions, prompt_first):
    tap_count = weight.shape[0]
    row_count = raw_rows.shape[0]
    extended = jnp.concatenate([before_rows, raw_rows], axis=0)
    lags = tap_count - 1 - jnp.arange(tap_count)
    inside_prompt = (positions[None, :] - lags[:, None] >= prompt_first[None, :]).astype(jnp.float32)
    windows = jnp.stack(
        [lax.slice_in_dim(extended, tap, tap + row_count, axis=0) for tap in range(tap_count)]
    )
    summed = jnp.sum(
        weight.astype(jnp.float32)[:, None, :]
        * windows.astype(jnp.float32)
        * inside_prompt[:, :, None],
        axis=0,
    )
    return jax.nn.silu(summed).astype(jnp.bfloat16)


def blocked(array_in):
    return array_in.reshape((array_in.shape[0] // SPAN, SPAN) + array_in.shape[1:])


def segment_parts(queries, head_keys, head_values, decays, starts):
    index_rows = jnp.arange(queries.shape[1])
    lower = (index_rows[:, None] >= index_rows[None, :]).astype(jnp.float32)
    cumulative = jnp.einsum("ac,bck->bak", lower, decays, precision=lax.Precision.HIGHEST)
    groups = jnp.cumsum(starts, axis=1)
    intact = (groups == 0.0).astype(jnp.float32)
    final_log = cumulative[:, -1]
    in_tail = (groups == groups[:, -1:]).astype(jnp.float32)
    weighted = (
        head_keys.astype(jnp.float32)
        * jnp.exp(final_log[:, None, :] - cumulative)
        * in_tail[:, :, None]
    ).astype(jnp.bfloat16)
    update = jnp.einsum("bsk,bsv->bkv", weighted, head_values, preferred_element_type=jnp.float32)
    step_decay = jnp.exp(final_log) * intact[:, -1:]
    allowed = (groups[:, :, None] == groups[:, None, :]) & (
        index_rows[None, :, None] >= index_rows[None, None, :]
    )
    lifted = queries.astype(jnp.float32) * jnp.exp(cumulative)
    lowered = (head_keys.astype(jnp.float32) * jnp.exp(-cumulative)).astype(jnp.bfloat16)
    raw_scores = jnp.einsum(
        "bak,bck->bac", lifted.astype(jnp.bfloat16), lowered, preferred_element_type=jnp.float32
    )
    scores = jnp.where(allowed, raw_scores, 0.0).astype(jnp.bfloat16)
    inside = jnp.einsum("bac,bcv->bav", scores, head_values, preferred_element_type=jnp.float32)
    lifted_intact = lifted * intact[:, :, None]
    block_count = queries.shape[0]
    memory = jnp.zeros(update.shape[1:], jnp.float32)
    product = jnp.ones(step_decay.shape[1:], jnp.float32)
    local_outs = [jnp.zeros(inside.shape[1:], jnp.float32)]
    products = [product]
    for block in range(block_count):
        if block > 0:
            local_outs.append(jnp.dot(lifted_intact[block], memory, precision=HIGH_PRECISION))
            products.append(product)
        memory = step_decay[block][:, None] * memory + update[block]
        product = product * step_decay[block]
    local_out = inside + jnp.stack(local_outs)
    carry_lift = lifted_intact * jnp.stack(products)[:, None, :]
    return (local_out, carry_lift, memory, product)


def packed_state(decay, memory):
    high = decay.astype(jnp.bfloat16)
    low = (decay - high.astype(jnp.float32)).astype(jnp.bfloat16)
    width = memory.shape[1]
    flat = jnp.concatenate([high, low])
    flat = jnp.pad(flat, (0, -flat.shape[0] % width))
    return jnp.concatenate([memory.astype(jnp.bfloat16), flat.reshape((-1, width))], axis=0)


def unpacked_state(packed, key_width):
    memory = packed[:key_width].astype(jnp.float32)
    flat = packed[key_width:].reshape((-1,)).astype(jnp.float32)
    return (flat[:key_width] + flat[key_width : 2 * key_width], memory)


def prefix_states(decay, memory, axis):
    count = lax.axis_size(axis)
    place = lax.axis_index(axis)
    key_width = memory.shape[0]
    entering_decay = jnp.ones_like(decay)
    entering = jnp.zeros_like(memory)
    steps = 1
    while steps < count:
        valid = place >= steps
        if steps * 2 < count:
            earlier_decay, earlier_memory = unpacked_state(
                shifted(packed_state(decay, memory), axis, steps), key_width
            )
        else:
            earlier_decay = None
            earlier_memory = shifted(memory.astype(jnp.bfloat16), axis, steps).astype(jnp.float32)
        memory = jnp.where(valid, decay[:, None] * earlier_memory + memory, memory)
        if steps == 1:
            entering = earlier_memory
            entering_decay = earlier_decay
        else:
            entering = jnp.where(valid, entering_decay[:, None] * earlier_memory + entering, entering)
        if earlier_decay is not None:
            decay = jnp.where(valid, earlier_decay * decay, decay)
            if steps > 1:
                entering_decay = jnp.where(valid, earlier_decay * entering_decay, entering_decay)
        steps *= 2
    return (memory, entering)


def rotations(axis):
    count = lax.axis_size(axis)
    return [[(source, (source + step) % count) for source in range(count)] for step in range(1, count)]


def gather_rows(rows, axis):
    count = lax.axis_size(axis)
    place = lax.axis_index(axis)
    if count & (count - 1):
        received = [rows] + [lax.ppermute(rows, axis, pairs) for pairs in rotations(axis)]
        order = [(-step) % count for step in range(count)]
    else:
        received = [rows]
        order = [0]
        mask = count // 2
        while mask >= 1:
            incoming = lax.ppermute(
                jnp.concatenate(received), axis, [(source, source ^ mask) for source in range(count)]
            )
            received = received + list(jnp.split(incoming, len(received)))
            order = order + [flip ^ mask for flip in order]
            mask //= 2

    def ordered(shift):
        if count & (count - 1):
            picks = [order.index((index - shift) % count) for index in range(count)]
        else:
            picks = [order.index(shift ^ index) for index in range(count)]
        return jnp.concatenate([received[pick] for pick in picks])

    return lax.switch(place, [functools.partial(ordered, shift) for shift in range(count)])


def scatter_sum(gated, weight, axis):
    count = lax.axis_size(axis)
    place = lax.axis_index(axis)
    chunk = gated.shape[0] // count

    def term(index):
        rows = lax.slice_in_dim(gated, index * chunk, (index + 1) * chunk, axis=0)
        return jnp.dot(rows, weight, preferred_element_type=jnp.float32).astype(jnp.bfloat16)

    if count & (count - 1):
        chunks = jnp.stack([term(index) for index in range(count)])
        total = lax.dynamic_index_in_dim(chunks, place, 0, False).astype(jnp.float32)
        for step, pairs in enumerate(rotations(axis), start=1):
            outgoing = lax.dynamic_index_in_dim(chunks, (place + step) % count, 0, False)
            total = total + lax.ppermute(outgoing, axis, pairs).astype(jnp.float32)
        return total.astype(jnp.bfloat16)
    def term(rows):
        return jnp.dot(rows, weight, preferred_element_type=jnp.float32).astype(jnp.bfloat16)

    held = [lax.slice_in_dim(gated, index * chunk, (index + 1) * chunk, axis=0) for index in range(count)]
    sums = None
    mask = 1
    while mask < count:
        odd = (place // mask) % 2 == 1
        rows = list(zip(held[0::2], held[1::2]))
        outgoing = term(jnp.concatenate([jnp.where(odd, low, high) for low, high in rows]))
        if sums is not None:
            parts = list(zip(sums[0::2], sums[1::2]))
            carried = jnp.concatenate([jnp.where(odd, low, high) for low, high in parts])
            outgoing = (outgoing.astype(jnp.float32) + carried).astype(jnp.bfloat16)
            kept_sums = [jnp.where(odd, high, low) for low, high in parts]
        else:
            kept_sums = [0.0] * len(rows)
        incoming = lax.ppermute(outgoing, axis, [(source, source ^ mask) for source in range(count)])
        incoming = jnp.split(incoming.astype(jnp.float32), len(rows))
        sums = [kept + arrived for kept, arrived in zip(kept_sums, incoming)]
        held = [jnp.where(odd, high, low) for low, high in rows]
        mask *= 2
    return (term(held[0]).astype(jnp.float32) + sums[0]).astype(jnp.bfloat16)


def shards(
    tokens,
    prompt_lengths,
    query_weight,
    key_weight,
    value_weight,
    query_conv,
    key_conv,
    value_conv,
    decay_down,
    decay_up,
    decay_bias,
    gate_weight,
    norm_gain,
    out_weight,
):
    gathered = gather_rows(tokens, "hv")

    def project(weight):
        return jnp.dot(gathered, weight, preferred_element_type=jnp.float32).astype(jnp.bfloat16)

    raw_query = project(query_weight)
    raw_key = project(key_weight)
    raw_value = project(value_weight)
    gate_values = project(gate_weight)
    low_rank = project(decay_down)
    row_count = raw_query.shape[0]
    key_width = raw_query.shape[1]
    value_width = raw_value.shape[1]
    positions = lax.axis_index("tok") * row_count + jnp.arange(row_count, dtype=jnp.int32)
    prompt_index = jnp.arange(prompt_lengths.shape[0])
    offsets = jnp.sum(
        jnp.where(prompt_index[None, :] < prompt_index[:, None], prompt_lengths[None, :], 0), axis=1
    )
    prompt_first, starts = prompt_marks(positions, offsets)
    rim_rows = query_conv.shape[0] - 1
    joined = jnp.concatenate([raw_query, raw_key, raw_value], axis=1)
    before_rows = shifted(joined[row_count - rim_rows :], "tok", 1)
    conv_query = short_conv(
        raw_query, before_rows[:, :key_width], query_conv, positions, prompt_first
    )
    conv_key = short_conv(
        raw_key, before_rows[:, key_width : 2 * key_width], key_conv, positions, prompt_first
    )
    conv_value = short_conv(
        raw_value, before_rows[:, 2 * key_width :], value_conv, positions, prompt_first
    )
    decays = (
        jax.nn.log_sigmoid(
            jnp.dot(low_rank, decay_up, preferred_element_type=jnp.float32) + decay_bias
        )
        / 16.0
    )
    local_out, carry_lift, local_memory, local_decay = segment_parts(
        blocked(conv_query), blocked(conv_key), blocked(conv_value), blocked(decays), blocked(starts)
    )
    closing, entering = prefix_states(local_decay, local_memory, "tok")
    heads_out = local_out.reshape((row_count, value_width)) + jnp.dot(
        carry_lift.reshape((row_count, key_width)), entering, precision=HIGH_PRECISION
    )
    gate_float = gate_values.astype(jnp.float32)
    rescale = lax.rsqrt(jnp.mean(heads_out * heads_out, axis=1, keepdims=True) + 1e-05)
    gated_out = (
        heads_out * rescale * norm_gain[None, :] * gate_float * jax.nn.sigmoid(gate_float)
    ).astype(jnp.bfloat16)
    mixed = scatter_sum(gated_out, out_weight, "hv")
    segment_states = closing[None, None]
    in_prompt = positions[row_count - rim_rows :] >= prompt_first[row_count - 1]
    tail_rows = joined[row_count - rim_rows :]
    conv_edges = jnp.where(in_prompt[:, None], tail_rows, jnp.zeros_like(tail_rows))
    conv_edges = conv_edges.reshape((1, rim_rows, 1, joined.shape[1]))
    return (mixed, segment_states, conv_edges)


def solution(mesh):
    in_specs = (
        P(("tok", "hv"), None),
        P(),
        P(None, "hv"),
        P(None, "hv"),
        P(None, "hv"),
        P(None, "hv"),
        P(None, "hv"),
        P(None, "hv"),
        P(),
        P(None, "hv"),
        P("hv"),
        P(None, "hv"),
        P(),
        P("hv", None),
    )
    out_specs = (P(("tok", "hv"), None), P("tok", "hv", None, None), P("tok", None, "hv", None))
    return jax.shard_map(shards, mesh=mesh, in_specs=in_specs, out_specs=out_specs, check_vma=False)
```

```python
import functools

import jax
import jax.numpy as jnp
from jax import lax
from jax.sharding import PartitionSpec as P

SPAN = 64


HIGH_PRECISION = lax.Precision.HIGH


def shifted(value, axis, steps):
    count = lax.axis_size(axis)
    initial, last = (max(0, -steps), min(count, count - steps))
    return lax.ppermute(value, axis, [(source, source + steps) for source in range(initial, last)])


def prompt_marks(positions, offsets):
    before = offsets[None, :] <= positions[:, None]
    prompt_first = jnp.max(jnp.where(before, offsets[None, :], 0), axis=1)
    return (prompt_first, (prompt_first == positions).astype(jnp.float32))


def short_conv(raw_rows, before_rows, weight, positions, prompt_first):
    tap_count = weight.shape[0]
    row_count = raw_rows.shape[0]
    extended = jnp.concatenate([before_rows, raw_rows], axis=0)
    lags = tap_count - 1 - jnp.arange(tap_count)
    inside_prompt = (positions[None, :] - lags[:, None] >= prompt_first[None, :]).astype(jnp.float32)
    windows = jnp.stack(
        [lax.slice_in_dim(extended, tap, tap + row_count, axis=0) for tap in range(tap_count)]
    )
    summed = jnp.sum(
        weight.astype(jnp.float32)[:, None, :]
        * windows.astype(jnp.float32)
        * inside_prompt[:, :, None],
        axis=0,
    )
    return jax.nn.silu(summed).astype(jnp.bfloat16)


def blocked(array_in):
    return array_in.reshape((array_in.shape[0] // SPAN, SPAN) + array_in.shape[1:])


def segment_parts(queries, head_keys, head_values, decays, starts):
    index_rows = jnp.arange(queries.shape[1])
    lower = (index_rows[:, None] >= index_rows[None, :]).astype(jnp.float32)
    cumulative = jnp.einsum("ac,bck->bak", lower, decays, precision=lax.Precision.HIGHEST)
    groups = jnp.cumsum(starts, axis=1)
    intact = (groups == 0.0).astype(jnp.float32)
    final_log = cumulative[:, -1]
    in_tail = (groups == groups[:, -1:]).astype(jnp.float32)
    weighted = (
        head_keys.astype(jnp.float32)
        * jnp.exp(final_log[:, None, :] - cumulative)
        * in_tail[:, :, None]
    ).astype(jnp.bfloat16)
    update = jnp.einsum("bsk,bsv->bkv", weighted, head_values, preferred_element_type=jnp.float32)
    step_decay = jnp.exp(final_log) * intact[:, -1:]
    allowed = (groups[:, :, None] == groups[:, None, :]) & (
        index_rows[None, :, None] >= index_rows[None, None, :]
    )
    lifted = queries.astype(jnp.float32) * jnp.exp(cumulative)
    lowered = (head_keys.astype(jnp.float32) * jnp.exp(-cumulative)).astype(jnp.bfloat16)
    raw_scores = jnp.einsum(
        "bak,bck->bac", lifted.astype(jnp.bfloat16), lowered, preferred_element_type=jnp.float32
    )
    scores = jnp.where(allowed, raw_scores, 0.0).astype(jnp.bfloat16)
    inside = jnp.einsum("bac,bcv->bav", scores, head_values, preferred_element_type=jnp.float32)
    lifted_intact = lifted * intact[:, :, None]
    block_count = queries.shape[0]
    memory = jnp.zeros(update.shape[1:], jnp.float32)
    product = jnp.ones(step_decay.shape[1:], jnp.float32)
    local_outs = [jnp.zeros(inside.shape[1:], jnp.float32)]
    products = [product]
    for block in range(block_count):
        if block > 0:
            local_outs.append(jnp.dot(lifted_intact[block], memory, precision=HIGH_PRECISION))
            products.append(product)
        memory = step_decay[block][:, None] * memory + update[block]
        product = product * step_decay[block]
    local_out = inside + jnp.stack(local_outs)
    carry_lift = lifted_intact * jnp.stack(products)[:, None, :]
    return (local_out, carry_lift, memory, product)


def packed_state(decay, memory):
    high = decay.astype(jnp.bfloat16)
    low = (decay - high.astype(jnp.float32)).astype(jnp.bfloat16)
    width = memory.shape[1]
    flat = jnp.concatenate([high, low])
    flat = jnp.pad(flat, (0, -flat.shape[0] % width))
    return jnp.concatenate([memory.astype(jnp.bfloat16), flat.reshape((-1, width))], axis=0)


def unpacked_state(packed, key_width):
    memory = packed[:key_width].astype(jnp.float32)
    flat = packed[key_width:].reshape((-1,)).astype(jnp.float32)
    return (flat[:key_width] + flat[key_width : 2 * key_width], memory)


def prefix_states(decay, memory, axis):
    count = lax.axis_size(axis)
    place = lax.axis_index(axis)
    key_width = memory.shape[0]
    entering_decay = jnp.ones_like(decay)
    entering = jnp.zeros_like(memory)
    steps = 1
    while steps < count:
        valid = place >= steps
        if steps * 2 < count:
            earlier_decay, earlier_memory = unpacked_state(
                shifted(packed_state(decay, memory), axis, steps), key_width
            )
        else:
            earlier_decay = None
            earlier_memory = shifted(memory.astype(jnp.bfloat16), axis, steps).astype(jnp.float32)
        memory = jnp.where(valid, decay[:, None] * earlier_memory + memory, memory)
        if steps == 1:
            entering = earlier_memory
            entering_decay = earlier_decay
        else:
            entering = jnp.where(valid, entering_decay[:, None] * earlier_memory + entering, entering)
        if earlier_decay is not None:
            decay = jnp.where(valid, earlier_decay * decay, decay)
            if steps > 1:
                entering_decay = jnp.where(valid, earlier_decay * entering_decay, entering_decay)
        steps *= 2
    return (memory, entering)


def rotations(axis):
    count = lax.axis_size(axis)
    return [[(source, (source + step) % count) for source in range(count)] for step in range(1, count)]


def gather_rows(rows, axis):
    count = lax.axis_size(axis)
    place = lax.axis_index(axis)
    if count & (count - 1):
        received = [rows] + [lax.ppermute(rows, axis, pairs) for pairs in rotations(axis)]
        order = [(-step) % count for step in range(count)]
    else:
        received = [rows]
        order = [0]
        mask = count // 2
        while mask >= 1:
            incoming = lax.ppermute(
                jnp.concatenate(received), axis, [(source, source ^ mask) for source in range(count)]
            )
            received = received + list(jnp.split(incoming, len(received)))
            order = order + [flip ^ mask for flip in order]
            mask //= 2

    def ordered(shift):
        if count & (count - 1):
            picks = [order.index((index - shift) % count) for index in range(count)]
        else:
            picks = [order.index(shift ^ index) for index in range(count)]
        return jnp.concatenate([received[pick] for pick in picks])

    return lax.switch(place, [functools.partial(ordered, shift) for shift in range(count)])


def scatter_sum(gated, weight, axis):
    count = lax.axis_size(axis)
    place = lax.axis_index(axis)
    chunk = gated.shape[0] // count

    def term(index):
        rows = lax.slice_in_dim(gated, index * chunk, (index + 1) * chunk, axis=0)
        return jnp.dot(rows, weight, preferred_element_type=jnp.float32).astype(jnp.bfloat16)

    if count & (count - 1):
        chunks = jnp.stack([term(index) for index in range(count)])
        total = lax.dynamic_index_in_dim(chunks, place, 0, False).astype(jnp.float32)
        for step, pairs in enumerate(rotations(axis), start=1):
            outgoing = lax.dynamic_index_in_dim(chunks, (place + step) % count, 0, False)
            total = total + lax.ppermute(outgoing, axis, pairs).astype(jnp.float32)
        return total.astype(jnp.bfloat16)
    held = [lax.slice_in_dim(gated, index * chunk, (index + 1) * chunk, axis=0) for index in range(count)]
    odd = place % 2 == 1
    pairs = list(zip(held[0::2], held[1::2]))
    outgoing = jnp.concatenate([jnp.where(odd, low, high) for low, high in pairs])
    outgoing = jnp.dot(outgoing, weight, preferred_element_type=jnp.float32).astype(jnp.bfloat16)
    incoming = lax.ppermute(outgoing, axis, [(source, source ^ 1) for source in range(count)])
    kept = jnp.concatenate([jnp.where(odd, high, low) for low, high in pairs])
    kept = jnp.dot(kept, weight, preferred_element_type=jnp.float32).astype(jnp.bfloat16)
    summed = kept.astype(jnp.float32) + incoming.astype(jnp.float32)
    held = list(jnp.split(summed, len(pairs)))
    mask = 2
    while mask < count:
        odd = (place // mask) % 2 == 1
        pairs = list(zip(held[0::2], held[1::2]))
        keep = [jnp.where(odd, high, low) for low, high in pairs]
        outgoing = jnp.stack([jnp.where(odd, low, high).astype(jnp.bfloat16) for low, high in pairs])
        incoming = lax.ppermute(outgoing, axis, [(source, source ^ mask) for source in range(count)])
        held = [
            kept.astype(jnp.float32) + incoming[index].astype(jnp.float32)
            for index, kept in enumerate(keep)
        ]
        mask *= 2
    return held[0].astype(jnp.bfloat16)


def shards(
    tokens,
    prompt_lengths,
    query_weight,
    key_weight,
    value_weight,
    query_conv,
    key_conv,
    value_conv,
    decay_down,
    decay_up,
    decay_bias,
    gate_weight,
    norm_gain,
    out_weight,
):
    width = tokens.shape[1]
    own_low_rank = jnp.dot(tokens, decay_down, preferred_element_type=jnp.float32).astype(jnp.bfloat16)
    gathered_all = gather_rows(jnp.concatenate([tokens, own_low_rank], axis=1), "hv")
    gathered = gathered_all[:, :width]

    def project(weight):
        return jnp.dot(gathered, weight, preferred_element_type=jnp.float32).astype(jnp.bfloat16)

    raw_query = project(query_weight)
    raw_key = project(key_weight)
    raw_value = project(value_weight)
    gate_values = project(gate_weight)
    low_rank = gathered_all[:, width:]
    row_count = raw_query.shape[0]
    key_width = raw_query.shape[1]
    value_width = raw_value.shape[1]
    positions = lax.axis_index("tok") * row_count + jnp.arange(row_count, dtype=jnp.int32)
    prompt_index = jnp.arange(prompt_lengths.shape[0])
    offsets = jnp.sum(
        jnp.where(prompt_index[None, :] < prompt_index[:, None], prompt_lengths[None, :], 0), axis=1
    )
    prompt_first, starts = prompt_marks(positions, offsets)
    rim_rows = query_conv.shape[0] - 1
    joined = jnp.concatenate([raw_query, raw_key, raw_value], axis=1)
    before_rows = shifted(joined[row_count - rim_rows :], "tok", 1)
    conv_query = short_conv(
        raw_query, before_rows[:, :key_width], query_conv, positions, prompt_first
    )
    conv_key = short_conv(
        raw_key, before_rows[:, key_width : 2 * key_width], key_conv, positions, prompt_first
    )
    conv_value = short_conv(
        raw_value, before_rows[:, 2 * key_width :], value_conv, positions, prompt_first
    )
    decays = (
        jax.nn.log_sigmoid(
            jnp.dot(low_rank, decay_up, preferred_element_type=jnp.float32) + decay_bias
        )
        / 16.0
    )
    local_out, carry_lift, local_memory, local_decay = segment_parts(
        blocked(conv_query), blocked(conv_key), blocked(conv_value), blocked(decays), blocked(starts)
    )
    closing, entering = prefix_states(local_decay, local_memory, "tok")
    heads_out = local_out.reshape((row_count, value_width)) + jnp.dot(
        carry_lift.reshape((row_count, key_width)), entering, precision=HIGH_PRECISION
    )
    gate_float = gate_values.astype(jnp.float32)
    rescale = lax.rsqrt(jnp.mean(heads_out * heads_out, axis=1, keepdims=True) + 1e-05)
    gated_out = (
        heads_out * rescale * norm_gain[None, :] * gate_float * jax.nn.sigmoid(gate_float)
    ).astype(jnp.bfloat16)
    mixed = scatter_sum(gated_out, out_weight, "hv")
    segment_states = closing[None, None]
    in_prompt = positions[row_count - rim_rows :] >= prompt_first[row_count - 1]
    tail_rows = joined[row_count - rim_rows :]
    conv_edges = jnp.where(in_prompt[:, None], tail_rows, jnp.zeros_like(tail_rows))
    conv_edges = conv_edges.reshape((1, rim_rows, 1, joined.shape[1]))
    return (mixed, segment_states, conv_edges)


def solution(mesh):
    in_specs = (
        P(("tok", "hv"), None),
        P(),
        P(None, "hv"),
        P(None, "hv"),
        P(None, "hv"),
        P(None, "hv"),
        P(None, "hv"),
        P(None, "hv"),
        P(),
        P(None, "hv"),
        P("hv"),
        P(None, "hv"),
        P(),
        P("hv", None),
    )
    out_specs = (P(("tok", "hv"), None), P("tok", "hv", None, None), P("tok", None, "hv", None))
    return jax.shard_map(shards, mesh=mesh, in_specs=in_specs, out_specs=out_specs, check_vma=False)
```

```python
import functools

import jax
import jax.numpy as jnp
from jax import lax
from jax.sharding import PartitionSpec as P

SPAN = 64


HIGH_PRECISION = lax.Precision.HIGH


def shifted(value, axis, steps):
    count = lax.axis_size(axis)
    initial, last = (max(0, -steps), min(count, count - steps))
    return lax.ppermute(value, axis, [(source, source + steps) for source in range(initial, last)])


def prompt_marks(positions, offsets):
    before = offsets[None, :] <= positions[:, None]
    prompt_first = jnp.max(jnp.where(before, offsets[None, :], 0), axis=1)
    return (prompt_first, (prompt_first == positions).astype(jnp.float32))


def short_conv(raw_rows, before_rows, weight, positions, prompt_first):
    tap_count = weight.shape[0]
    row_count = raw_rows.shape[0]
    extended = jnp.concatenate([before_rows, raw_rows], axis=0)
    lags = tap_count - 1 - jnp.arange(tap_count)
    inside_prompt = (positions[None, :] - lags[:, None] >= prompt_first[None, :]).astype(jnp.float32)
    windows = jnp.stack(
        [lax.slice_in_dim(extended, tap, tap + row_count, axis=0) for tap in range(tap_count)]
    )
    summed = jnp.sum(
        weight.astype(jnp.float32)[:, None, :]
        * windows.astype(jnp.float32)
        * inside_prompt[:, :, None],
        axis=0,
    )
    return jax.nn.silu(summed).astype(jnp.bfloat16)


def blocked(array_in):
    return array_in.reshape((array_in.shape[0] // SPAN, SPAN) + array_in.shape[1:])


def segment_parts(queries, head_keys, head_values, decays, firsts, block_starts):
    index_rows = jnp.arange(queries.shape[1])
    lower = (index_rows[:, None] >= index_rows[None, :]).astype(jnp.float32)
    cumulative = jnp.einsum("ac,bck->bak", lower, decays, precision=lax.Precision.HIGHEST)
    intact = (firsts < block_starts[:, None]).astype(jnp.float32)
    final_log = cumulative[:, -1]
    in_tail = (firsts == firsts[:, -1:]).astype(jnp.float32)
    weighted = (
        head_keys.astype(jnp.float32)
        * jnp.exp(final_log[:, None, :] - cumulative)
        * in_tail[:, :, None]
    ).astype(jnp.bfloat16)
    update = jnp.einsum("bsk,bsv->bkv", weighted, head_values, preferred_element_type=jnp.float32)
    step_decay = jnp.exp(final_log) * intact[:, -1:]
    allowed = (firsts[:, :, None] == firsts[:, None, :]) & (
        index_rows[None, :, None] >= index_rows[None, None, :]
    )
    lifted = queries.astype(jnp.float32) * jnp.exp(cumulative)
    lowered = (head_keys.astype(jnp.float32) * jnp.exp(-cumulative)).astype(jnp.bfloat16)
    raw_scores = jnp.einsum(
        "bak,bck->bac", lifted.astype(jnp.bfloat16), lowered, preferred_element_type=jnp.float32
    )
    scores = jnp.where(allowed, raw_scores, 0.0).astype(jnp.bfloat16)
    inside = jnp.einsum("bac,bcv->bav", scores, head_values, preferred_element_type=jnp.float32)
    lifted_intact = lifted * intact[:, :, None]
    block_count = queries.shape[0]
    memory = jnp.zeros(update.shape[1:], jnp.float32)
    product = jnp.ones(step_decay.shape[1:], jnp.float32)
    local_outs = [jnp.zeros(inside.shape[1:], jnp.float32)]
    products = [product]
    for block in range(block_count):
        if block > 0:
            local_outs.append(jnp.dot(lifted_intact[block], memory, precision=HIGH_PRECISION))
            products.append(product)
        memory = step_decay[block][:, None] * memory + update[block]
        product = product * step_decay[block]
    local_out = inside + jnp.stack(local_outs)
    carry_lift = lifted_intact * jnp.stack(products)[:, None, :]
    return (local_out, carry_lift, memory, product)


def packed_state(decay, memory):
    high = decay.astype(jnp.bfloat16)
    low = (decay - high.astype(jnp.float32)).astype(jnp.bfloat16)
    width = memory.shape[1]
    flat = jnp.concatenate([high, low])
    flat = jnp.pad(flat, (0, -flat.shape[0] % width))
    return jnp.concatenate([memory.astype(jnp.bfloat16), flat.reshape((-1, width))], axis=0)


def unpacked_state(packed, key_width):
    memory = packed[:key_width].astype(jnp.float32)
    flat = packed[key_width:].reshape((-1,)).astype(jnp.float32)
    return (flat[:key_width] + flat[key_width : 2 * key_width], memory)


def prefix_states(decay, memory, axis):
    count = lax.axis_size(axis)
    place = lax.axis_index(axis)
    key_width = memory.shape[0]
    entering_decay = jnp.ones_like(decay)
    entering = jnp.zeros_like(memory)
    steps = 1
    while steps < count:
        valid = place >= steps
        if steps * 2 < count:
            earlier_decay, earlier_memory = unpacked_state(
                shifted(packed_state(decay, memory), axis, steps), key_width
            )
        else:
            earlier_decay = None
            earlier_memory = shifted(memory.astype(jnp.bfloat16), axis, steps).astype(jnp.float32)
        memory = jnp.where(valid, decay[:, None] * earlier_memory + memory, memory)
        if steps == 1:
            entering = earlier_memory
            entering_decay = earlier_decay
        else:
            entering = jnp.where(valid, entering_decay[:, None] * earlier_memory + entering, entering)
        if earlier_decay is not None:
            decay = jnp.where(valid, earlier_decay * decay, decay)
            if steps > 1:
                entering_decay = jnp.where(valid, earlier_decay * entering_decay, entering_decay)
        steps *= 2
    return (memory, entering)


def rotations(axis):
    count = lax.axis_size(axis)
    return [[(source, (source + step) % count) for source in range(count)] for step in range(1, count)]


def gather_rows(rows, axis):
    count = lax.axis_size(axis)
    place = lax.axis_index(axis)
    if count & (count - 1):
        received = [rows] + [lax.ppermute(rows, axis, pairs) for pairs in rotations(axis)]
        order = [(-step) % count for step in range(count)]
    else:
        received = [rows]
        order = [0]
        mask = count // 2
        while mask >= 1:
            incoming = lax.ppermute(
                jnp.concatenate(received), axis, [(source, source ^ mask) for source in range(count)]
            )
            received = received + list(jnp.split(incoming, len(received)))
            order = order + [flip ^ mask for flip in order]
            mask //= 2

    def ordered(shift):
        if count & (count - 1):
            picks = [order.index((index - shift) % count) for index in range(count)]
        else:
            picks = [order.index(shift ^ index) for index in range(count)]
        return jnp.concatenate([received[pick] for pick in picks])

    return lax.switch(place, [functools.partial(ordered, shift) for shift in range(count)])


def scatter_sum(gated, weight, axis):
    count = lax.axis_size(axis)
    place = lax.axis_index(axis)
    chunk = gated.shape[0] // count

    def term(index):
        rows = lax.slice_in_dim(gated, index * chunk, (index + 1) * chunk, axis=0)
        return jnp.dot(rows, weight, preferred_element_type=jnp.float32).astype(jnp.bfloat16)

    if count & (count - 1):
        chunks = jnp.stack([term(index) for index in range(count)])
        total = lax.dynamic_index_in_dim(chunks, place, 0, False).astype(jnp.float32)
        for step, pairs in enumerate(rotations(axis), start=1):
            outgoing = lax.dynamic_index_in_dim(chunks, (place + step) % count, 0, False)
            total = total + lax.ppermute(outgoing, axis, pairs).astype(jnp.float32)
        return total.astype(jnp.bfloat16)
    held = [lax.slice_in_dim(gated, index * chunk, (index + 1) * chunk, axis=0) for index in range(count)]
    odd = place % 2 == 1
    pairs = list(zip(held[0::2], held[1::2]))
    outgoing = jnp.concatenate([jnp.where(odd, low, high) for low, high in pairs])
    outgoing = jnp.dot(outgoing, weight, preferred_element_type=jnp.float32).astype(jnp.bfloat16)
    incoming = lax.ppermute(outgoing, axis, [(source, source ^ 1) for source in range(count)])
    kept = jnp.concatenate([jnp.where(odd, high, low) for low, high in pairs])
    kept = jnp.dot(kept, weight, preferred_element_type=jnp.float32).astype(jnp.bfloat16)
    summed = kept.astype(jnp.float32) + incoming.astype(jnp.float32)
    held = list(jnp.split(summed, len(pairs)))
    mask = 2
    while mask < count:
        odd = (place // mask) % 2 == 1
        pairs = list(zip(held[0::2], held[1::2]))
        keep = [jnp.where(odd, high, low) for low, high in pairs]
        outgoing = jnp.stack([jnp.where(odd, low, high).astype(jnp.bfloat16) for low, high in pairs])
        incoming = lax.ppermute(outgoing, axis, [(source, source ^ mask) for source in range(count)])
        held = [
            kept.astype(jnp.float32) + incoming[index].astype(jnp.float32)
            for index, kept in enumerate(keep)
        ]
        mask *= 2
    return held[0].astype(jnp.bfloat16)


def shards(
    tokens,
    prompt_lengths,
    query_weight,
    key_weight,
    value_weight,
    query_conv,
    key_conv,
    value_conv,
    decay_down,
    decay_up,
    decay_bias,
    gate_weight,
    norm_gain,
    out_weight,
):
    gathered = gather_rows(tokens, "hv")

    def project(weight):
        return jnp.dot(gathered, weight, preferred_element_type=jnp.float32).astype(jnp.bfloat16)

    raw_query = project(query_weight)
    raw_key = project(key_weight)
    raw_value = project(value_weight)
    gate_values = project(gate_weight)
    low_rank = project(decay_down)
    row_count = raw_query.shape[0]
    key_width = raw_query.shape[1]
    value_width = raw_value.shape[1]
    positions = lax.axis_index("tok") * row_count + jnp.arange(row_count, dtype=jnp.int32)
    prompt_index = jnp.arange(prompt_lengths.shape[0])
    offsets = jnp.sum(
        jnp.where(prompt_index[None, :] < prompt_index[:, None], prompt_lengths[None, :], 0), axis=1
    )
    prompt_first, starts = prompt_marks(positions, offsets)
    rim_rows = query_conv.shape[0] - 1
    joined = jnp.concatenate([raw_query, raw_key, raw_value], axis=1)
    before_rows = shifted(joined[row_count - rim_rows :], "tok", 1)
    conv_query = short_conv(
        raw_query, before_rows[:, :key_width], query_conv, positions, prompt_first
    )
    conv_key = short_conv(
        raw_key, before_rows[:, key_width : 2 * key_width], key_conv, positions, prompt_first
    )
    conv_value = short_conv(
        raw_value, before_rows[:, 2 * key_width :], value_conv, positions, prompt_first
    )
    decays = (
        jax.nn.log_sigmoid(
            jnp.dot(low_rank, decay_up, preferred_element_type=jnp.float32) + decay_bias
        )
        / 16.0
    )
    local_out, carry_lift, local_memory, local_decay = segment_parts(
        blocked(conv_query),
        blocked(conv_key),
        blocked(conv_value),
        blocked(decays),
        blocked(prompt_first),
        blocked(positions)[:, 0],
    )
    closing, entering = prefix_states(local_decay, local_memory, "tok")
    heads_out = local_out.reshape((row_count, value_width)) + jnp.dot(
        carry_lift.reshape((row_count, key_width)), entering, precision=HIGH_PRECISION
    )
    gate_float = gate_values.astype(jnp.float32)
    rescale = lax.rsqrt(jnp.mean(heads_out * heads_out, axis=1, keepdims=True) + 1e-05)
    gated_out = (
        heads_out * rescale * norm_gain[None, :] * gate_float * jax.nn.sigmoid(gate_float)
    ).astype(jnp.bfloat16)
    mixed = scatter_sum(gated_out, out_weight, "hv")
    segment_states = closing[None, None]
    in_prompt = positions[row_count - rim_rows :] >= prompt_first[row_count - 1]
    tail_rows = joined[row_count - rim_rows :]
    conv_edges = jnp.where(in_prompt[:, None], tail_rows, jnp.zeros_like(tail_rows))
    conv_edges = conv_edges.reshape((1, rim_rows, 1, joined.shape[1]))
    return (mixed, segment_states, conv_edges)


def solution(mesh):
    in_specs = (
        P(("tok", "hv"), None),
        P(),
        P(None, "hv"),
        P(None, "hv"),
        P(None, "hv"),
        P(None, "hv"),
        P(None, "hv"),
        P(None, "hv"),
        P(),
        P(None, "hv"),
        P("hv"),
        P(None, "hv"),
        P(),
        P("hv", None),
    )
    out_specs = (P(("tok", "hv"), None), P("tok", "hv", None, None), P("tok", None, "hv", None))
    return jax.shard_map(shards, mesh=mesh, in_specs=in_specs, out_specs=out_specs, check_vma=False)
```

```python
import functools

import jax
import jax.numpy as jnp
from jax import lax
from jax.sharding import PartitionSpec as P

SPAN = 64


HIGH_PRECISION = lax.Precision.HIGH


def shifted(value, axis, steps):
    count = lax.axis_size(axis)
    initial, last = (max(0, -steps), min(count, count - steps))
    return lax.ppermute(value, axis, [(source, source + steps) for source in range(initial, last)])


def prompt_marks(positions, offsets):
    before = offsets[None, :] <= positions[:, None]
    prompt_first = jnp.max(jnp.where(before, offsets[None, :], 0), axis=1)
    return (prompt_first, (prompt_first == positions).astype(jnp.float32))


def short_conv(raw_rows, before_rows, weight, positions, prompt_first):
    tap_count = weight.shape[0]
    row_count = raw_rows.shape[0]
    extended = jnp.concatenate([before_rows, raw_rows], axis=0)
    lags = tap_count - 1 - jnp.arange(tap_count)
    inside_prompt = (positions[None, :] - lags[:, None] >= prompt_first[None, :]).astype(jnp.float32)
    windows = jnp.stack(
        [lax.slice_in_dim(extended, tap, tap + row_count, axis=0) for tap in range(tap_count)]
    )
    summed = jnp.sum(
        weight.astype(jnp.float32)[:, None, :]
        * windows.astype(jnp.float32)
        * inside_prompt[:, :, None],
        axis=0,
    )
    return jax.nn.silu(summed).astype(jnp.bfloat16)


def blocked(array_in):
    return array_in.reshape((array_in.shape[0] // SPAN, SPAN) + array_in.shape[1:])


def segment_parts(queries, head_keys, head_values, decays, firsts, block_starts):
    index_rows = jnp.arange(queries.shape[1])
    lower = (index_rows[:, None] >= index_rows[None, :]).astype(jnp.float32)
    cumulative = jnp.einsum("ac,bck->bak", lower, decays, precision=lax.Precision.HIGHEST)
    intact = (firsts < block_starts[:, None]).astype(jnp.float32)
    final_log = cumulative[:, -1]
    in_tail = (firsts == firsts[:, -1:]).astype(jnp.float32)
    weighted = (
        head_keys.astype(jnp.float32)
        * jnp.exp(final_log[:, None, :] - cumulative)
        * in_tail[:, :, None]
    ).astype(jnp.bfloat16)
    update = jnp.einsum("bsk,bsv->bkv", weighted, head_values, preferred_element_type=jnp.float32)
    step_decay = jnp.exp(final_log) * intact[:, -1:]
    allowed = (firsts[:, :, None] == firsts[:, None, :]) & (
        index_rows[None, :, None] >= index_rows[None, None, :]
    )
    lifted = queries.astype(jnp.float32) * jnp.exp(cumulative)
    lowered = (head_keys.astype(jnp.float32) * jnp.exp(-cumulative)).astype(jnp.bfloat16)
    raw_scores = jnp.einsum(
        "bak,bck->bac", lifted.astype(jnp.bfloat16), lowered, preferred_element_type=jnp.float32
    )
    scores = jnp.where(allowed, raw_scores, 0.0).astype(jnp.bfloat16)
    inside = jnp.einsum("bac,bcv->bav", scores, head_values, preferred_element_type=jnp.float32)
    lifted_intact = lifted * intact[:, :, None]
    block_count = queries.shape[0]
    memory = jnp.zeros(update.shape[1:], jnp.float32)
    product = jnp.ones(step_decay.shape[1:], jnp.float32)
    local_outs = [jnp.zeros(inside.shape[1:], jnp.float32)]
    products = [product]
    for block in range(block_count):
        if block > 0:
            local_outs.append(jnp.dot(lifted_intact[block], memory, precision=HIGH_PRECISION))
            products.append(product)
        memory = step_decay[block][:, None] * memory + update[block]
        product = product * step_decay[block]
    local_out = inside + jnp.stack(local_outs)
    carry_lift = lifted_intact * jnp.stack(products)[:, None, :]
    return (local_out, carry_lift, memory, product)


def packed_state(decay, memory):
    high = decay.astype(jnp.bfloat16)
    low = (decay - high.astype(jnp.float32)).astype(jnp.bfloat16)
    width = memory.shape[1]
    flat = jnp.concatenate([high, low])
    flat = jnp.pad(flat, (0, -flat.shape[0] % width))
    return jnp.concatenate([memory.astype(jnp.bfloat16), flat.reshape((-1, width))], axis=0)


def unpacked_state(packed, key_width):
    memory = packed[:key_width].astype(jnp.float32)
    flat = packed[key_width:].reshape((-1,)).astype(jnp.float32)
    return (flat[:key_width] + flat[key_width : 2 * key_width], memory)


def prefix_states(decay, memory, axis):
    count = lax.axis_size(axis)
    place = lax.axis_index(axis)
    key_width = memory.shape[0]
    entering_decay = jnp.ones_like(decay)
    entering = jnp.zeros_like(memory)
    steps = 1
    while steps < count:
        valid = place >= steps
        if steps * 2 < count:
            earlier_decay, earlier_memory = unpacked_state(
                shifted(packed_state(decay, memory), axis, steps), key_width
            )
        else:
            earlier_decay = None
            earlier_memory = shifted(memory.astype(jnp.bfloat16), axis, steps).astype(jnp.float32)
        memory = jnp.where(valid, decay[:, None] * earlier_memory + memory, memory)
        if steps == 1:
            entering = earlier_memory
            entering_decay = earlier_decay
        else:
            entering = jnp.where(valid, entering_decay[:, None] * earlier_memory + entering, entering)
        if earlier_decay is not None:
            decay = jnp.where(valid, earlier_decay * decay, decay)
            if steps > 1:
                entering_decay = jnp.where(valid, earlier_decay * entering_decay, entering_decay)
        steps *= 2
    return (memory, entering)


def rotations(axis):
    count = lax.axis_size(axis)
    return [[(source, (source + step) % count) for source in range(count)] for step in range(1, count)]


def gather_rows(rows, axis):
    count = lax.axis_size(axis)
    place = lax.axis_index(axis)
    if count & (count - 1):
        received = [rows] + [lax.ppermute(rows, axis, pairs) for pairs in rotations(axis)]
        order = [(-step) % count for step in range(count)]
    else:
        received = [rows]
        order = [0]
        mask = count // 2
        while mask >= 1:
            incoming = lax.ppermute(
                jnp.concatenate(received), axis, [(source, source ^ mask) for source in range(count)]
            )
            received = received + list(jnp.split(incoming, len(received)))
            order = order + [flip ^ mask for flip in order]
            mask //= 2

    def pick(index):
        if count & (count - 1):
            wanted = (place - index) % count
            table = [order.index((-step) % count) for step in range(count)]
        else:
            wanted = jnp.bitwise_xor(place, index)
            table = [order.index(flip) for flip in range(count)]
        chosen = received[table[count - 1]]
        for flip in range(count - 2, -1, -1):
            chosen = jnp.where(wanted == flip, received[table[flip]], chosen)
        return chosen

    return jnp.concatenate([pick(index) for index in range(count)])


def scatter_sum(gated, weight, axis):
    count = lax.axis_size(axis)
    place = lax.axis_index(axis)
    chunk = gated.shape[0] // count

    def term(index):
        rows = lax.slice_in_dim(gated, index * chunk, (index + 1) * chunk, axis=0)
        return jnp.dot(rows, weight, preferred_element_type=jnp.float32).astype(jnp.bfloat16)

    if count & (count - 1):
        chunks = jnp.stack([term(index) for index in range(count)])
        total = lax.dynamic_index_in_dim(chunks, place, 0, False).astype(jnp.float32)
        for step, pairs in enumerate(rotations(axis), start=1):
            outgoing = lax.dynamic_index_in_dim(chunks, (place + step) % count, 0, False)
            total = total + lax.ppermute(outgoing, axis, pairs).astype(jnp.float32)
        return total.astype(jnp.bfloat16)
    held = [lax.slice_in_dim(gated, index * chunk, (index + 1) * chunk, axis=0) for index in range(count)]
    odd = place % 2 == 1
    pairs = list(zip(held[0::2], held[1::2]))
    outgoing = jnp.concatenate([jnp.where(odd, low, high) for low, high in pairs])
    outgoing = jnp.dot(outgoing, weight, preferred_element_type=jnp.float32).astype(jnp.bfloat16)
    incoming = lax.ppermute(outgoing, axis, [(source, source ^ 1) for source in range(count)])
    kept = jnp.concatenate([jnp.where(odd, high, low) for low, high in pairs])
    kept = jnp.dot(kept, weight, preferred_element_type=jnp.float32).astype(jnp.bfloat16)
    summed = kept.astype(jnp.float32) + incoming.astype(jnp.float32)
    held = list(jnp.split(summed, len(pairs)))
    mask = 2
    while mask < count:
        odd = (place // mask) % 2 == 1
        pairs = list(zip(held[0::2], held[1::2]))
        keep = [jnp.where(odd, high, low) for low, high in pairs]
        outgoing = jnp.stack([jnp.where(odd, low, high).astype(jnp.bfloat16) for low, high in pairs])
        incoming = lax.ppermute(outgoing, axis, [(source, source ^ mask) for source in range(count)])
        held = [
            kept.astype(jnp.float32) + incoming[index].astype(jnp.float32)
            for index, kept in enumerate(keep)
        ]
        mask *= 2
    return held[0].astype(jnp.bfloat16)


def shards(
    tokens,
    prompt_lengths,
    query_weight,
    key_weight,
    value_weight,
    query_conv,
    key_conv,
    value_conv,
    decay_down,
    decay_up,
    decay_bias,
    gate_weight,
    norm_gain,
    out_weight,
):
    gathered = gather_rows(tokens, "hv")

    def project(weight):
        return jnp.dot(gathered, weight, preferred_element_type=jnp.float32).astype(jnp.bfloat16)

    raw_query = project(query_weight)
    raw_key = project(key_weight)
    raw_value = project(value_weight)
    gate_values = project(gate_weight)
    low_rank = project(decay_down)
    row_count = raw_query.shape[0]
    key_width = raw_query.shape[1]
    value_width = raw_value.shape[1]
    positions = lax.axis_index("tok") * row_count + jnp.arange(row_count, dtype=jnp.int32)
    prompt_index = jnp.arange(prompt_lengths.shape[0])
    offsets = jnp.sum(
        jnp.where(prompt_index[None, :] < prompt_index[:, None], prompt_lengths[None, :], 0), axis=1
    )
    prompt_first, starts = prompt_marks(positions, offsets)
    rim_rows = query_conv.shape[0] - 1
    joined = jnp.concatenate([raw_query, raw_key, raw_value], axis=1)
    before_rows = shifted(joined[row_count - rim_rows :], "tok", 1)
    conv_query = short_conv(
        raw_query, before_rows[:, :key_width], query_conv, positions, prompt_first
    )
    conv_key = short_conv(
        raw_key, before_rows[:, key_width : 2 * key_width], key_conv, positions, prompt_first
    )
    conv_value = short_conv(
        raw_value, before_rows[:, 2 * key_width :], value_conv, positions, prompt_first
    )
    decays = (
        jax.nn.log_sigmoid(
            jnp.dot(low_rank, decay_up, preferred_element_type=jnp.float32) + decay_bias
        )
        / 16.0
    )
    local_out, carry_lift, local_memory, local_decay = segment_parts(
        blocked(conv_query),
        blocked(conv_key),
        blocked(conv_value),
        blocked(decays),
        blocked(prompt_first),
        blocked(positions)[:, 0],
    )
    closing, entering = prefix_states(local_decay, local_memory, "tok")
    heads_out = local_out.reshape((row_count, value_width)) + jnp.dot(
        carry_lift.reshape((row_count, key_width)), entering, precision=HIGH_PRECISION
    )
    gate_float = gate_values.astype(jnp.float32)
    rescale = lax.rsqrt(jnp.mean(heads_out * heads_out, axis=1, keepdims=True) + 1e-05)
    gated_out = (
        heads_out * rescale * norm_gain[None, :] * gate_float * jax.nn.sigmoid(gate_float)
    ).astype(jnp.bfloat16)
    mixed = scatter_sum(gated_out, out_weight, "hv")
    segment_states = closing[None, None]
    in_prompt = positions[row_count - rim_rows :] >= prompt_first[row_count - 1]
    tail_rows = joined[row_count - rim_rows :]
    conv_edges = jnp.where(in_prompt[:, None], tail_rows, jnp.zeros_like(tail_rows))
    conv_edges = conv_edges.reshape((1, rim_rows, 1, joined.shape[1]))
    return (mixed, segment_states, conv_edges)


def solution(mesh):
    in_specs = (
        P(("tok", "hv"), None),
        P(),
        P(None, "hv"),
        P(None, "hv"),
        P(None, "hv"),
        P(None, "hv"),
        P(None, "hv"),
        P(None, "hv"),
        P(),
        P(None, "hv"),
        P("hv"),
        P(None, "hv"),
        P(),
        P("hv", None),
    )
    out_specs = (P(("tok", "hv"), None), P("tok", "hv", None, None), P("tok", None, "hv", None))
    return jax.shard_map(shards, mesh=mesh, in_specs=in_specs, out_specs=out_specs, check_vma=False)
```

```python
import functools

import jax
import jax.numpy as jnp
from jax import lax
from jax.sharding import PartitionSpec as P

SPAN = 64


HIGH_PRECISION = lax.Precision.HIGH


def shifted(value, axis, steps):
    count = lax.axis_size(axis)
    initial, last = (max(0, -steps), min(count, count - steps))
    return lax.ppermute(value, axis, [(source, source + steps) for source in range(initial, last)])


def prompt_marks(positions, offsets):
    before = offsets[None, :] <= positions[:, None]
    prompt_first = jnp.max(jnp.where(before, offsets[None, :], 0), axis=1)
    return (prompt_first, (prompt_first == positions).astype(jnp.float32))


def short_conv(raw_rows, before_rows, weight, positions, prompt_first):
    tap_count = weight.shape[0]
    row_count = raw_rows.shape[0]
    extended = jnp.concatenate([before_rows, raw_rows], axis=0)
    lags = tap_count - 1 - jnp.arange(tap_count)
    inside_prompt = (positions[None, :] - lags[:, None] >= prompt_first[None, :]).astype(jnp.float32)
    windows = jnp.stack(
        [lax.slice_in_dim(extended, tap, tap + row_count, axis=0) for tap in range(tap_count)]
    )
    summed = jnp.sum(
        weight.astype(jnp.float32)[:, None, :]
        * windows.astype(jnp.float32)
        * inside_prompt[:, :, None],
        axis=0,
    )
    return jax.nn.silu(summed).astype(jnp.bfloat16)


def blocked(array_in):
    return array_in.reshape((array_in.shape[0] // SPAN, SPAN) + array_in.shape[1:])


def segment_parts(queries, head_keys, head_values, decays, firsts, block_starts):
    index_rows = jnp.arange(queries.shape[1])
    lower = (index_rows[:, None] >= index_rows[None, :]).astype(jnp.float32)
    cumulative = jnp.einsum("ac,bck->bak", lower, decays, precision=lax.Precision.HIGHEST)
    intact = (firsts < block_starts[:, None]).astype(jnp.float32)
    final_log = cumulative[:, -1]
    in_tail = (firsts == firsts[:, -1:]).astype(jnp.float32)
    weighted = (
        head_keys.astype(jnp.float32)
        * jnp.exp(final_log[:, None, :] - cumulative)
        * in_tail[:, :, None]
    ).astype(jnp.bfloat16)
    update = jnp.einsum("bsk,bsv->bkv", weighted, head_values, preferred_element_type=jnp.float32)
    step_decay = jnp.exp(final_log) * intact[:, -1:]
    allowed = (firsts[:, :, None] == firsts[:, None, :]) & (
        index_rows[None, :, None] >= index_rows[None, None, :]
    )
    lifted = queries.astype(jnp.float32) * jnp.exp(cumulative)
    lowered = (head_keys.astype(jnp.float32) * jnp.exp(-cumulative)).astype(jnp.bfloat16)
    raw_scores = jnp.einsum(
        "bak,bck->bac", lifted.astype(jnp.bfloat16), lowered, preferred_element_type=jnp.float32
    )
    scores = jnp.where(allowed, raw_scores, 0.0).astype(jnp.bfloat16)
    inside = jnp.einsum("bac,bcv->bav", scores, head_values, preferred_element_type=jnp.float32)
    lifted_intact = lifted * intact[:, :, None]
    block_count = queries.shape[0]
    memory = jnp.zeros(update.shape[1:], jnp.float32)
    product = jnp.ones(step_decay.shape[1:], jnp.float32)
    local_outs = [jnp.zeros(inside.shape[1:], jnp.float32)]
    products = [product]
    for block in range(block_count):
        if block > 0:
            local_outs.append(jnp.dot(lifted_intact[block], memory, precision=HIGH_PRECISION))
            products.append(product)
        memory = step_decay[block][:, None] * memory + update[block]
        product = product * step_decay[block]
    local_out = inside + jnp.stack(local_outs)
    carry_lift = lifted_intact * jnp.stack(products)[:, None, :]
    return (local_out, carry_lift, memory, product)


def packed_state(decay, memory):
    high = decay.astype(jnp.bfloat16)
    low = (decay - high.astype(jnp.float32)).astype(jnp.bfloat16)
    width = memory.shape[1]
    flat = jnp.concatenate([high, low])
    flat = jnp.pad(flat, (0, -flat.shape[0] % width))
    return jnp.concatenate([memory.astype(jnp.bfloat16), flat.reshape((-1, width))], axis=0)


def unpacked_state(packed, key_width):
    memory = packed[:key_width].astype(jnp.float32)
    flat = packed[key_width:].reshape((-1,)).astype(jnp.float32)
    return (flat[:key_width] + flat[key_width : 2 * key_width], memory)


def prefix_states(decay, memory, axis):
    count = lax.axis_size(axis)
    place = lax.axis_index(axis)
    key_width = memory.shape[0]
    entering_decay = jnp.ones_like(decay)
    entering = jnp.zeros_like(memory)
    steps = 1
    while steps < count:
        valid = place >= steps
        if steps * 2 < count:
            earlier_decay, earlier_memory = unpacked_state(
                shifted(packed_state(decay, memory), axis, steps), key_width
            )
        else:
            earlier_decay = None
            earlier_memory = shifted(memory.astype(jnp.bfloat16), axis, steps).astype(jnp.float32)
        memory = decay[:, None] * earlier_memory + memory
        if steps == 1:
            entering = earlier_memory
            entering_decay = earlier_decay
        else:
            entering = entering_decay[:, None] * earlier_memory + entering
        if earlier_decay is not None:
            decay = jnp.where(valid, earlier_decay * decay, decay)
            if steps > 1:
                entering_decay = jnp.where(valid, earlier_decay * entering_decay, entering_decay)
        steps *= 2
    return (memory, entering)


def rotations(axis):
    count = lax.axis_size(axis)
    return [[(source, (source + step) % count) for source in range(count)] for step in range(1, count)]


def gather_rows(rows, axis):
    count = lax.axis_size(axis)
    place = lax.axis_index(axis)
    if count & (count - 1):
        received = [rows] + [lax.ppermute(rows, axis, pairs) for pairs in rotations(axis)]
        order = [(-step) % count for step in range(count)]
    else:
        received = [rows]
        order = [0]
        mask = count // 2
        while mask >= 1:
            incoming = lax.ppermute(
                jnp.concatenate(received), axis, [(source, source ^ mask) for source in range(count)]
            )
            received = received + list(jnp.split(incoming, len(received)))
            order = order + [flip ^ mask for flip in order]
            mask //= 2

    def ordered(shift):
        if count & (count - 1):
            picks = [order.index((index - shift) % count) for index in range(count)]
        else:
            picks = [order.index(shift ^ index) for index in range(count)]
        return jnp.concatenate([received[pick] for pick in picks])

    return lax.switch(place, [functools.partial(ordered, shift) for shift in range(count)])


def scatter_sum(gated, weight, axis):
    count = lax.axis_size(axis)
    place = lax.axis_index(axis)
    chunk = gated.shape[0] // count

    def term(index):
        rows = lax.slice_in_dim(gated, index * chunk, (index + 1) * chunk, axis=0)
        return jnp.dot(rows, weight, preferred_element_type=jnp.float32).astype(jnp.bfloat16)

    if count & (count - 1):
        chunks = jnp.stack([term(index) for index in range(count)])
        total = lax.dynamic_index_in_dim(chunks, place, 0, False).astype(jnp.float32)
        for step, pairs in enumerate(rotations(axis), start=1):
            outgoing = lax.dynamic_index_in_dim(chunks, (place + step) % count, 0, False)
            total = total + lax.ppermute(outgoing, axis, pairs).astype(jnp.float32)
        return total.astype(jnp.bfloat16)
    held = [lax.slice_in_dim(gated, index * chunk, (index + 1) * chunk, axis=0) for index in range(count)]
    odd = place % 2 == 1
    pairs = list(zip(held[0::2], held[1::2]))
    outgoing = jnp.concatenate([jnp.where(odd, low, high) for low, high in pairs])
    outgoing = jnp.dot(outgoing, weight, preferred_element_type=jnp.float32).astype(jnp.bfloat16)
    incoming = lax.ppermute(outgoing, axis, [(source, source ^ 1) for source in range(count)])
    kept = jnp.concatenate([jnp.where(odd, high, low) for low, high in pairs])
    kept = jnp.dot(kept, weight, preferred_element_type=jnp.float32).astype(jnp.bfloat16)
    summed = kept.astype(jnp.float32) + incoming.astype(jnp.float32)
    held = list(jnp.split(summed, len(pairs)))
    mask = 2
    while mask < count:
        odd = (place // mask) % 2 == 1
        pairs = list(zip(held[0::2], held[1::2]))
        keep = [jnp.where(odd, high, low) for low, high in pairs]
        outgoing = jnp.stack([jnp.where(odd, low, high).astype(jnp.bfloat16) for low, high in pairs])
        incoming = lax.ppermute(outgoing, axis, [(source, source ^ mask) for source in range(count)])
        held = [
            kept.astype(jnp.float32) + incoming[index].astype(jnp.float32)
            for index, kept in enumerate(keep)
        ]
        mask *= 2
    return held[0].astype(jnp.bfloat16)


def shards(
    tokens,
    prompt_lengths,
    query_weight,
    key_weight,
    value_weight,
    query_conv,
    key_conv,
    value_conv,
    decay_down,
    decay_up,
    decay_bias,
    gate_weight,
    norm_gain,
    out_weight,
):
    gathered = gather_rows(tokens, "hv")

    def project(weight):
        return jnp.dot(gathered, weight, preferred_element_type=jnp.float32).astype(jnp.bfloat16)

    raw_query = project(query_weight)
    raw_key = project(key_weight)
    raw_value = project(value_weight)
    gate_values = project(gate_weight)
    low_rank = project(decay_down)
    row_count = raw_query.shape[0]
    key_width = raw_query.shape[1]
    value_width = raw_value.shape[1]
    positions = lax.axis_index("tok") * row_count + jnp.arange(row_count, dtype=jnp.int32)
    prompt_index = jnp.arange(prompt_lengths.shape[0])
    offsets = jnp.sum(
        jnp.where(prompt_index[None, :] < prompt_index[:, None], prompt_lengths[None, :], 0), axis=1
    )
    prompt_first, starts = prompt_marks(positions, offsets)
    rim_rows = query_conv.shape[0] - 1
    joined = jnp.concatenate([raw_query, raw_key, raw_value], axis=1)
    before_rows = shifted(joined[row_count - rim_rows :], "tok", 1)
    conv_query = short_conv(
        raw_query, before_rows[:, :key_width], query_conv, positions, prompt_first
    )
    conv_key = short_conv(
        raw_key, before_rows[:, key_width : 2 * key_width], key_conv, positions, prompt_first
    )
    conv_value = short_conv(
        raw_value, before_rows[:, 2 * key_width :], value_conv, positions, prompt_first
    )
    decays = (
        jax.nn.log_sigmoid(
            jnp.dot(low_rank, decay_up, preferred_element_type=jnp.float32) + decay_bias
        )
        / 16.0
    )
    local_out, carry_lift, local_memory, local_decay = segment_parts(
        blocked(conv_query),
        blocked(conv_key),
        blocked(conv_value),
        blocked(decays),
        blocked(prompt_first),
        blocked(positions)[:, 0],
    )
    closing, entering = prefix_states(local_decay, local_memory, "tok")
    heads_out = local_out.reshape((row_count, value_width)) + jnp.dot(
        carry_lift.reshape((row_count, key_width)), entering, precision=HIGH_PRECISION
    )
    gate_float = gate_values.astype(jnp.float32)
    rescale = lax.rsqrt(jnp.mean(heads_out * heads_out, axis=1, keepdims=True) + 1e-05)
    gated_out = (
        heads_out * rescale * norm_gain[None, :] * gate_float * jax.nn.sigmoid(gate_float)
    ).astype(jnp.bfloat16)
    mixed = scatter_sum(gated_out, out_weight, "hv")
    segment_states = closing[None, None]
    in_prompt = positions[row_count - rim_rows :] >= prompt_first[row_count - 1]
    tail_rows = joined[row_count - rim_rows :]
    conv_edges = jnp.where(in_prompt[:, None], tail_rows, jnp.zeros_like(tail_rows))
    conv_edges = conv_edges.reshape((1, rim_rows, 1, joined.shape[1]))
    return (mixed, segment_states, conv_edges)


def solution(mesh):
    in_specs = (
        P(("tok", "hv"), None),
        P(),
        P(None, "hv"),
        P(None, "hv"),
        P(None, "hv"),
        P(None, "hv"),
        P(None, "hv"),
        P(None, "hv"),
        P(),
        P(None, "hv"),
        P("hv"),
        P(None, "hv"),
        P(),
        P("hv", None),
    )
    out_specs = (P(("tok", "hv"), None), P("tok", "hv", None, None), P("tok", None, "hv", None))
    return jax.shard_map(shards, mesh=mesh, in_specs=in_specs, out_specs=out_specs, check_vma=False)
```

```python
import functools

import jax
import jax.numpy as jnp
from jax import lax
from jax.sharding import PartitionSpec as P

SPAN = 64


HIGH_PRECISION = lax.Precision.HIGH


def shifted(value, axis, steps):
    count = lax.axis_size(axis)
    initial, last = (max(0, -steps), min(count, count - steps))
    return lax.ppermute(value, axis, [(source, source + steps) for source in range(initial, last)])


def prompt_marks(positions, offsets):
    before = offsets[None, :] <= positions[:, None]
    prompt_first = jnp.max(jnp.where(before, offsets[None, :], 0), axis=1)
    return (prompt_first, (prompt_first == positions).astype(jnp.float32))


def short_conv(raw_rows, before_rows, weight, positions, prompt_first):
    tap_count = weight.shape[0]
    row_count = raw_rows.shape[0]
    extended = jnp.concatenate([before_rows, raw_rows], axis=0)
    lags = tap_count - 1 - jnp.arange(tap_count)
    inside_prompt = (positions[None, :] - lags[:, None] >= prompt_first[None, :]).astype(jnp.float32)
    windows = jnp.stack(
        [lax.slice_in_dim(extended, tap, tap + row_count, axis=0) for tap in range(tap_count)]
    )
    summed = jnp.sum(
        weight.astype(jnp.float32)[:, None, :]
        * windows.astype(jnp.float32)
        * inside_prompt[:, :, None],
        axis=0,
    )
    return jax.nn.silu(summed).astype(jnp.bfloat16)


def blocked(array_in):
    return array_in.reshape((array_in.shape[0] // SPAN, SPAN) + array_in.shape[1:])


def segment_parts(queries, head_keys, head_values, decays, firsts, block_starts):
    index_rows = jnp.arange(queries.shape[1])
    lower = (index_rows[:, None] >= index_rows[None, :]).astype(jnp.float32)
    cumulative = jnp.einsum("ac,bck->bak", lower, decays, precision=lax.Precision.HIGHEST)
    intact = (firsts < block_starts[:, None]).astype(jnp.float32)
    final_log = cumulative[:, -1]
    in_tail = (firsts == firsts[:, -1:]).astype(jnp.float32)
    weighted = (
        head_keys.astype(jnp.float32)
        * jnp.exp(final_log[:, None, :] - cumulative)
        * in_tail[:, :, None]
    ).astype(jnp.bfloat16)
    update = jnp.einsum("bsk,bsv->bkv", weighted, head_values, preferred_element_type=jnp.float32)
    step_decay = jnp.exp(final_log) * intact[:, -1:]
    allowed = (firsts[:, :, None] == firsts[:, None, :]) & (
        index_rows[None, :, None] >= index_rows[None, None, :]
    )
    lifted = queries.astype(jnp.float32) * jnp.exp(cumulative)
    lowered = (head_keys.astype(jnp.float32) * jnp.exp(-cumulative)).astype(jnp.bfloat16)
    raw_scores = jnp.einsum(
        "bak,bck->bac", lifted.astype(jnp.bfloat16), lowered, preferred_element_type=jnp.float32
    )
    scores = jnp.where(allowed, raw_scores, 0.0).astype(jnp.bfloat16)
    inside = jnp.einsum("bac,bcv->bav", scores, head_values, preferred_element_type=jnp.float32)
    lifted_intact = lifted * intact[:, :, None]
    block_count = queries.shape[0]
    memory = jnp.zeros(update.shape[1:], jnp.float32)
    product = jnp.ones(step_decay.shape[1:], jnp.float32)
    local_outs = [jnp.zeros(inside.shape[1:], jnp.float32)]
    products = [product]
    for block in range(block_count):
        if block > 0:
            local_outs.append(jnp.dot(lifted_intact[block], memory, precision=HIGH_PRECISION))
            products.append(product)
        memory = step_decay[block][:, None] * memory + update[block]
        product = product * step_decay[block]
    local_out = inside + jnp.stack(local_outs)
    carry_lift = lifted_intact * jnp.stack(products)[:, None, :]
    return (local_out, carry_lift, memory, product)


def packed_state(decay, memory):
    high = decay.astype(jnp.bfloat16)
    low = (decay - high.astype(jnp.float32)).astype(jnp.bfloat16)
    width = memory.shape[1]
    flat = jnp.concatenate([high, low])
    flat = jnp.pad(flat, (0, -flat.shape[0] % width))
    return jnp.concatenate([memory.astype(jnp.bfloat16), flat.reshape((-1, width))], axis=0)


def unpacked_state(packed, key_width):
    memory = packed[:key_width].astype(jnp.float32)
    flat = packed[key_width:].reshape((-1,)).astype(jnp.float32)
    return (flat[:key_width] + flat[key_width : 2 * key_width], memory)


def prefix_states(decay, memory, axis):
    count = lax.axis_size(axis)
    place = lax.axis_index(axis)
    key_width = memory.shape[0]
    entering_decay = jnp.ones_like(decay)
    entering = jnp.zeros_like(memory)
    steps = 1
    while steps < count:
        valid = place >= steps
        if steps * 2 < count:
            earlier_decay, earlier_memory = unpacked_state(
                shifted(packed_state(decay, memory), axis, steps), key_width
            )
        else:
            earlier_decay = None
            earlier_memory = shifted(memory.astype(jnp.bfloat16), axis, steps).astype(jnp.float32)
        memory = jnp.where(valid, decay[:, None] * earlier_memory + memory, memory)
        if steps == 1:
            entering = earlier_memory
            entering_decay = earlier_decay
        else:
            entering = jnp.where(valid, entering_decay[:, None] * earlier_memory + entering, entering)
        if earlier_decay is not None:
            decay = jnp.where(valid, earlier_decay * decay, decay)
            if steps > 1:
                entering_decay = jnp.where(valid, earlier_decay * entering_decay, entering_decay)
        steps *= 2
    return (memory, entering)


def rotations(axis):
    count = lax.axis_size(axis)
    return [[(source, (source + step) % count) for source in range(count)] for step in range(1, count)]


def gather_rows(rows, axis):
    count = lax.axis_size(axis)
    place = lax.axis_index(axis)
    if count & (count - 1):
        received = [rows] + [lax.ppermute(rows, axis, pairs) for pairs in rotations(axis)]
        order = [(-step) % count for step in range(count)]
    else:
        received = [rows]
        order = [0]
        mask = count // 2
        while mask >= 1:
            pairs = [(source, source ^ mask) for source in range(count)]
            received = received + [lax.ppermute(block, axis, pairs) for block in received]
            order = order + [flip ^ mask for flip in order]
            mask //= 2

    def ordered(shift):
        if count & (count - 1):
            picks = [order.index((index - shift) % count) for index in range(count)]
        else:
            picks = [order.index(shift ^ index) for index in range(count)]
        return jnp.concatenate([received[pick] for pick in picks])

    return lax.switch(place, [functools.partial(ordered, shift) for shift in range(count)])


def scatter_sum(gated, weight, axis):
    count = lax.axis_size(axis)
    place = lax.axis_index(axis)
    chunk = gated.shape[0] // count

    def term(index):
        rows = lax.slice_in_dim(gated, index * chunk, (index + 1) * chunk, axis=0)
        return jnp.dot(rows, weight, preferred_element_type=jnp.float32).astype(jnp.bfloat16)

    if count & (count - 1):
        chunks = jnp.stack([term(index) for index in range(count)])
        total = lax.dynamic_index_in_dim(chunks, place, 0, False).astype(jnp.float32)
        for step, pairs in enumerate(rotations(axis), start=1):
            outgoing = lax.dynamic_index_in_dim(chunks, (place + step) % count, 0, False)
            total = total + lax.ppermute(outgoing, axis, pairs).astype(jnp.float32)
        return total.astype(jnp.bfloat16)
    held = [lax.slice_in_dim(gated, index * chunk, (index + 1) * chunk, axis=0) for index in range(count)]
    odd = place % 2 == 1
    pairs = list(zip(held[0::2], held[1::2]))
    outgoing = jnp.concatenate([jnp.where(odd, low, high) for low, high in pairs])
    outgoing = jnp.dot(outgoing, weight, preferred_element_type=jnp.float32).astype(jnp.bfloat16)
    incoming = lax.ppermute(outgoing, axis, [(source, source ^ 1) for source in range(count)])
    kept = jnp.concatenate([jnp.where(odd, high, low) for low, high in pairs])
    kept = jnp.dot(kept, weight, preferred_element_type=jnp.float32).astype(jnp.bfloat16)
    summed = kept.astype(jnp.float32) + incoming.astype(jnp.float32)
    held = list(jnp.split(summed, len(pairs)))
    mask = 2
    while mask < count:
        odd = (place // mask) % 2 == 1
        pairs = list(zip(held[0::2], held[1::2]))
        keep = [jnp.where(odd, high, low) for low, high in pairs]
        outgoing = jnp.stack([jnp.where(odd, low, high).astype(jnp.bfloat16) for low, high in pairs])
        incoming = lax.ppermute(outgoing, axis, [(source, source ^ mask) for source in range(count)])
        held = [
            kept.astype(jnp.float32) + incoming[index].astype(jnp.float32)
            for index, kept in enumerate(keep)
        ]
        mask *= 2
    return held[0].astype(jnp.bfloat16)


def shards(
    tokens,
    prompt_lengths,
    query_weight,
    key_weight,
    value_weight,
    query_conv,
    key_conv,
    value_conv,
    decay_down,
    decay_up,
    decay_bias,
    gate_weight,
    norm_gain,
    out_weight,
):
    gathered = gather_rows(tokens, "hv")

    def project(weight):
        return jnp.dot(gathered, weight, preferred_element_type=jnp.float32).astype(jnp.bfloat16)

    raw_query = project(query_weight)
    raw_key = project(key_weight)
    raw_value = project(value_weight)
    gate_values = project(gate_weight)
    low_rank = project(decay_down)
    row_count = raw_query.shape[0]
    key_width = raw_query.shape[1]
    value_width = raw_value.shape[1]
    positions = lax.axis_index("tok") * row_count + jnp.arange(row_count, dtype=jnp.int32)
    prompt_index = jnp.arange(prompt_lengths.shape[0])
    offsets = jnp.sum(
        jnp.where(prompt_index[None, :] < prompt_index[:, None], prompt_lengths[None, :], 0), axis=1
    )
    prompt_first, starts = prompt_marks(positions, offsets)
    rim_rows = query_conv.shape[0] - 1
    joined = jnp.concatenate([raw_query, raw_key, raw_value], axis=1)
    before_rows = shifted(joined[row_count - rim_rows :], "tok", 1)
    conv_query = short_conv(
        raw_query, before_rows[:, :key_width], query_conv, positions, prompt_first
    )
    conv_key = short_conv(
        raw_key, before_rows[:, key_width : 2 * key_width], key_conv, positions, prompt_first
    )
    conv_value = short_conv(
        raw_value, before_rows[:, 2 * key_width :], value_conv, positions, prompt_first
    )
    decays = (
        jax.nn.log_sigmoid(
            jnp.dot(low_rank, decay_up, preferred_element_type=jnp.float32) + decay_bias
        )
        / 16.0
    )
    local_out, carry_lift, local_memory, local_decay = segment_parts(
        blocked(conv_query),
        blocked(conv_key),
        blocked(conv_value),
        blocked(decays),
        blocked(prompt_first),
        blocked(positions)[:, 0],
    )
    closing, entering = prefix_states(local_decay, local_memory, "tok")
    heads_out = local_out.reshape((row_count, value_width)) + jnp.dot(
        carry_lift.reshape((row_count, key_width)), entering, precision=HIGH_PRECISION
    )
    gate_float = gate_values.astype(jnp.float32)
    rescale = lax.rsqrt(jnp.mean(heads_out * heads_out, axis=1, keepdims=True) + 1e-05)
    gated_out = (
        heads_out * rescale * norm_gain[None, :] * gate_float * jax.nn.sigmoid(gate_float)
    ).astype(jnp.bfloat16)
    mixed = scatter_sum(gated_out, out_weight, "hv")
    segment_states = closing[None, None]
    in_prompt = positions[row_count - rim_rows :] >= prompt_first[row_count - 1]
    tail_rows = joined[row_count - rim_rows :]
    conv_edges = jnp.where(in_prompt[:, None], tail_rows, jnp.zeros_like(tail_rows))
    conv_edges = conv_edges.reshape((1, rim_rows, 1, joined.shape[1]))
    return (mixed, segment_states, conv_edges)


def solution(mesh):
    in_specs = (
        P(("tok", "hv"), None),
        P(),
        P(None, "hv"),
        P(None, "hv"),
        P(None, "hv"),
        P(None, "hv"),
        P(None, "hv"),
        P(None, "hv"),
        P(),
        P(None, "hv"),
        P("hv"),
        P(None, "hv"),
        P(),
        P("hv", None),
    )
    out_specs = (P(("tok", "hv"), None), P("tok", "hv", None, None), P("tok", None, "hv", None))
    return jax.shard_map(shards, mesh=mesh, in_specs=in_specs, out_specs=out_specs, check_vma=False)
```
